128 devices in a mesh: tile: 32 (over z, x, core), expo: 4 (over y).
Axes of the slice: x: 4, y: 4, z: 4, core: 2. Of those that a mesh axis runs over, the one named last changes fastest.
Arguments:
- pixel_uv: float32 [2, 32, 32768], P(None, 'expo', 'tile'), may hold values from -1 to 1
- ccd_index: int32 [32, 32768], P('expo', 'tile'), may hold values from 0 to 61
- observed: int32 [32, 32768], P('expo', 'tile'), may hold values 0 or 1
- obs_weight: float32 [32, 32768], P('expo', 'tile'), may hold values from 0.001953125 to 0.015625
- obs_resid: float32 [2, 32, 32768], P(None, 'expo', 'tile'), may hold values from -96 to 96
- star_inverse: float32 [5, 5, 32768], P(None, None, 'tile'), as said below
- star_count: int32 [32], P('tile'), may hold values from 64 to 1024, as said below
- ccd_center: float32 [2, 62], replicated, may hold values from -1 to 1
- exp_geom: float32 [3, 512], replicated, may hold values from -1 to 1
- tile_exposures: int32 [32, 32], P('tile'), may hold values from 0 to 511, as said below
- pair_owner: int32 [32, 32, 32], P('tile'), may hold values from 0 to 24575, as said below
Outputs:
- pair_blocks: float32 [24576, 3600], P(('tile', 'expo'))
- reduced_rhs: float32 [512, 60], P(('tile', 'expo'))
The draws below stay inside these ranges and needn't reach their ends.
Inputs may be any that keep to these rules, and one draw needn't show every extreme that they name: `star_count`: the stars of a tile fill its first slots; some tile holds exactly 1024. `tile_exposures`: each row lists 32 distinct exposures; the last 16 of row t are the first 16 of row t + 1 (row 0 after the last), in the same order; every exposure appears in exactly two rows. `pair_owner`: two entries name the same slot exactly when they name the same ordered pair of exposures; every slot is named. The owner of slot k is k // 192 on tile+expo; the rows 8 * j to 8 * j + 7 of one tile name exactly 2 entries with each owner. `star_inverse`: each star's 5 x 5 block is symmetric positive definite.
All inputs are finite; a program needn't handle non-finite values. No bound on the sum of `observed` on one device may be relied on, other than what follows from the above.
Results may differ from the reference program's by a relative error of at most 0.0023.
Values may be sent and summed in bfloat16 or wider, within the bound.
No kernel may reach another device: no remote copies, remote signals or barrier semaphores. Data moves between devices by JAX's collectives and lax.ppermute only.
A program may use at most 256 MiB of HBM per device.

```python
import math
import jax
import jax.numpy as jnp
from jax import lax

DEG_X = 6
DEG_Y = 5
NCCD = 62
L_DEV = 8
STAR_DEV = 1024
PAR = 60
LOC = 32
EXPOSURES = 512
STARS = 32768
PAIRS = 24576
PAIR_DEV = 192
N_TILE = 32
N_EXPO = 4
DEVICES = 128


def draw_star_inverse(key, part):
    first_key, second_key, third_key = jax.random.split(jax.random.fold_in(key, 17), 3)
    scales = jnp.exp(jax.random.uniform(first_key, (STARS,), jnp.float32, math.log(0.02), math.log(0.2))) * STAR_DEV
    diagonal = jax.random.uniform(second_key, (5, STARS), jnp.float32, 1.0, 2.0)
    spread = jax.random.uniform(third_key, (5, 5, STARS), jnp.float32, -0.24, 0.24)
    spread = 0.5 * (spread + jnp.transpose(spread, (1, 0, 2)))
    identity = jnp.eye(5, dtype=jnp.float32)[:, :, None]
    matrix = spread * (1.0 - identity) + identity * diagonal[:, None, :]
    return matrix * scales[None, None, :]


def draw_star_count(key, part):
    first_key, second_key = jax.random.split(jax.random.fold_in(key, 5))
    counts = jax.random.randint(first_key, (N_TILE,), STAR_DEV // 16, STAR_DEV // 2 + 1)
    fullest = jax.random.randint(second_key, (), 0, N_TILE)
    return jnp.where(jnp.arange(N_TILE) == fullest, STAR_DEV, counts).astype(jnp.int32)


def draw_tile_exposures(key, part):
    half_window = LOC // 2
    shuffled = jax.random.permutation(jax.random.fold_in(key, 3), EXPOSURES)
    places = (jnp.arange(N_TILE)[:, None] * half_window + jnp.arange(LOC)[None, :]) % EXPOSURES
    return shuffled[places].astype(jnp.int32)


def draw_pair_owner(key, part):
    half_window = LOC // 2
    class_size = L_DEV * half_window
    repeats = class_size // DEVICES
    half_expo = N_EXPO // 2
    first_key, second_key = jax.random.split(jax.random.fold_in(key, 11))
    tile_ids = jnp.arange(N_TILE)[:, None, None]
    row_ids = jnp.arange(LOC)[None, :, None]
    col_ids = jnp.arange(LOC)[None, None, :]
    shared = (row_ids >= half_window) & (col_ids >= half_window)
    home_tile = jnp.where(shared, (tile_ids + 1) % N_TILE, tile_ids)
    home_row = jnp.where(shared, row_ids - half_window, row_ids)
    home_col = jnp.where(shared, col_ids - half_window, col_ids)
    home_block = home_row // L_DEV
    kind_ids = jnp.where((home_row < half_window) & (home_col >= half_window), 1, 0)
    within = home_row % L_DEV * half_window + home_col % half_window
    class_keys = jax.random.split(first_key, N_TILE * N_EXPO * 2)
    shuffles = jax.vmap(lambda key_one: jax.random.permutation(key_one, class_size))(class_keys)
    shuffles = shuffles.reshape(N_TILE, N_EXPO, 2, class_size)
    drawn_ids = shuffles[home_tile, home_block, kind_ids, within]
    owner_ids = drawn_ids % DEVICES
    rank_ids = drawn_ids // DEVICES
    lower_slot = (home_tile * half_expo + home_block) * 2 * repeats + kind_ids * repeats
    upper_slot = N_TILE * half_expo * 2 * repeats + (home_tile * half_expo + home_block - half_expo) * repeats
    position = jnp.where(home_block < half_expo, lower_slot, upper_slot) + rank_ids
    owner_keys = jax.random.split(second_key, DEVICES)
    local_orders = jax.vmap(lambda key_one: jax.random.permutation(key_one, PAIR_DEV))(owner_keys)
    return (owner_ids * PAIR_DEV + local_orders[owner_ids, position]).astype(jnp.int32)


def set_ends(values, own_key, least, top_value):
    place = [jax.random.randint(jax.random.fold_in(own_key, axis), (), 0, length) for axis, length in enumerate(values.shape)]
    main_axis = values.shape.index(max(values.shape))
    next_to = place[:main_axis] + [(place[main_axis] + 1) % values.shape[main_axis]] + place[main_axis + 1:]
    return values.at[tuple(place)].set(least).at[tuple(next_to)].set(top_value)


def levels(stream_key, dims, shards, low, largest):
    gain, own = 1.0, jax.random.fold_in(stream_key, 6)
    for dim, parts in shards:
        draws = jnp.exp(jax.random.uniform(jax.random.fold_in(own, dim), (parts,), jnp.float32, low / len(shards), largest / len(shards)))
        gain = gain * jnp.repeat(draws, dims[dim] // parts).reshape([-1 if axis == dim else 1 for axis in range(len(dims))])
    return gain


def noise(stream_key, shape, scale, limit, cuts=(), held_as=jnp.bfloat16):
    loudness = levels(stream_key, shape, cuts, -0.22, 0.18) if cuts else 1.0
    entries = jax.random.normal(stream_key, shape, jnp.float32) * scale * loudness
    return jnp.minimum(jnp.maximum(entries, -limit), limit).astype(held_as)


def setup_inputs(seed: int = 0) -> dict:
    splits = jax.random.split(jax.random.key(seed), 12)
    return {
        "pixel_uv": jnp.clip(jax.random.uniform(splits[0], (2, LOC, STARS), jnp.float32, -1.0, 1.0) * levels(splits[0], (2, LOC, STARS), ((1, 4), (2, 32)), -0.4, 0.0), -1.0, 1.0),
        "ccd_index": set_ends(jax.random.randint(splits[1], (LOC, STARS), 0, NCCD), jax.random.fold_in(splits[1], 1), 0, NCCD - 1).astype(jnp.int32),
        "observed": set_ends((jax.random.randint(splits[2], (LOC, STARS), 0, 5) < 3).astype(jnp.int32), jax.random.fold_in(splits[2], 1), 0, 1),
        "obs_weight": jnp.clip(jnp.exp(math.log(0.015625) - 2.0794415 * jax.random.uniform(splits[3], (LOC, STARS), jnp.float32) ** levels(splits[3], (LOC, STARS), ((0, 4), (1, 32)), -0.2, 0.2)), 0.001953125, 0.015625),
        "obs_resid": noise(splits[4], (2, LOC, STARS), (0.5 * STAR_DEV ** 0.5), 96.0, ((1, 4), (2, 32)), jnp.float32),
        "star_inverse": draw_star_inverse(jax.random.fold_in(splits[11], 71), 0),
        "star_count": draw_star_count(jax.random.fold_in(splits[11], 71), 0),
        "ccd_center": jnp.clip(jax.random.uniform(splits[7], (2, NCCD), jnp.float32, -1.0, 1.0), -1.0, 1.0),
        "exp_geom": jnp.clip(jax.random.uniform(splits[8], (3, EXPOSURES), jnp.float32, -1.0, 1.0), -1.0, 1.0),
        "tile_exposures": draw_tile_exposures(jax.random.fold_in(splits[11], 71), 0),
        "pair_owner": draw_pair_owner(jax.random.fold_in(splits[11], 71), 0),
    }


highest = lax.Precision.HIGHEST


def chebyshev(values, degree):
    series = [jnp.ones_like(values), values]
    for degree_at in range(2, degree):
        series.append(2.0 * values * series[-1] - series[-2])
    return series[:degree]


def observation_terms(pixel_uv, ccd_index, observed, obs_weight, live_rows, ccd_center, geometry):
    ccd_total = ccd_center.shape[1]
    picked = (ccd_index[None, :, :] == jnp.arange(ccd_total, dtype=jnp.int32)[:, None, None]).astype(jnp.float32)
    centre = jnp.sum(ccd_center[:, :, None, None] * picked[None], axis=1)
    focal = 0.75 * centre + 0.25 * pixel_uv
    along_first = chebyshev(focal[0], DEG_X)
    along_second = chebyshev(focal[1], DEG_Y)
    basis = jnp.stack([first_term * second_term for first_term in along_first for second_term in along_second], axis=1)
    star_rows = ccd_index.shape[1]
    alive = (jnp.arange(star_rows, dtype=jnp.int32)[None, :] < live_rows).astype(jnp.float32)
    live_weight = obs_weight * observed.astype(jnp.float32) * alive
    shift_time = geometry[0]
    factor_first = geometry[1]
    factor_second = geometry[2]
    unit_row = jnp.ones_like(shift_time)
    zero_row = jnp.zeros_like(shift_time)
    jacobian = jnp.stack([jnp.stack([unit_row, zero_row, shift_time, zero_row, factor_first], axis=-1),
                          jnp.stack([zero_row, unit_row, zero_row, shift_time, factor_second], axis=-1)], axis=1)
    return live_weight, basis, jacobian


def coupling_matrix(live_weight, basis, jacobian):
    full = live_weight[:, None, None, None, :] * jacobian[:, :, None, :, None] * basis[:, None, :, None, :]
    return full.astype(jnp.bfloat16).reshape(basis.shape[0] * 2 * basis.shape[1], 5, basis.shape[2])


def scaled_coupling(coupling, inverse):
    return jnp.einsum("xis,jis->xjs", coupling.astype(jnp.float32), inverse, precision=highest).astype(jnp.bfloat16)


def diagonal_blocks(live_weight, basis):
    weighted = live_weight[:, None, :] * basis
    gram = jnp.einsum("ams,ans->amn", weighted, basis, precision=highest)
    pair_eye = jnp.eye(2, dtype=jnp.float32)
    full = jnp.einsum("cd,amn->acmdn", pair_eye, gram, precision=highest)
    return full.reshape(gram.shape[0], 2 * gram.shape[1], 2 * gram.shape[1]), weighted


def gradient_terms(jacobian, live_weight, obs_resid):
    return jnp.einsum("aci,as,cas->is", jacobian, live_weight, obs_resid, precision=highest)


def local_rhs(weighted, jacobian, obs_resid, solved):
    correction = jnp.einsum("aci,is->cas", jacobian, solved, precision=highest)
    result = jnp.einsum("ams,cas->acm", weighted, obs_resid - correction, precision=highest)
    return result.reshape(weighted.shape[0], 2 * weighted.shape[1])


def reference(pixel_uv, ccd_index, observed, obs_weight, obs_resid, star_inverse, star_count, ccd_center, exp_geom, tile_exposures, pair_owner):
    def one_tile(running, tile_id):
        pair_sum, rhs_sum = running
        first_star = tile_id * STAR_DEV

        def star_slice(source):
            return lax.dynamic_slice_in_dim(source, first_star, STAR_DEV, source.ndim - 1)

        exposure_ids = tile_exposures[tile_id]
        geometry = exp_geom[:, exposure_ids]
        live_weight, basis, jacobian = observation_terms(star_slice(pixel_uv), star_slice(ccd_index), star_slice(observed), star_slice(obs_weight), star_count[tile_id], ccd_center, geometry)
        inverse = star_slice(star_inverse)
        resid_here = star_slice(obs_resid)
        coupling = coupling_matrix(live_weight, basis, jacobian)
        scaled = scaled_coupling(coupling, inverse)
        product = lax.dot_general(coupling.astype(jnp.float32), scaled.astype(jnp.float32), (((1, 2), (1, 2)), ((), ())), precision=highest)
        diagonal, weighted = diagonal_blocks(live_weight, basis)
        blocks = -product.reshape(LOC, PAR, LOC, PAR).transpose(0, 2, 1, 3)
        diag_rows = jnp.arange(LOC, dtype=jnp.int32)
        blocks = blocks.at[diag_rows, diag_rows].add(diagonal)
        pair_sum = pair_sum.at[pair_owner[tile_id].reshape(-1)].add(blocks.reshape(LOC * LOC, PAR * PAR))
        gradient = gradient_terms(jacobian, live_weight, resid_here)
        solved = jnp.einsum("jis,is->js", inverse, gradient, precision=highest)
        rhs_sum = rhs_sum.at[exposure_ids].add(local_rhs(weighted, jacobian, resid_here, solved))
        return (pair_sum, rhs_sum), None

    start_state = (jnp.zeros((PAIRS, PAR * PAR), jnp.float32), jnp.zeros((EXPOSURES, PAR), jnp.float32))
    final_state, unused = lax.scan(one_tile, start_state, jnp.arange(N_TILE, dtype=jnp.int32))
    return final_state[0], final_state[1]
```

```python
import jax
import jax.numpy as jnp
from jax import lax
from jax.experimental import pallas as pl
from jax.experimental.pallas import tpu as pltpu
from jax.sharding import Mesh
from jax.sharding import PartitionSpec as P

DEG_X = 6
DEG_Y = 5
TILE = ("tile_0", "tile_1", "tile_2")
TILE_EXPO = ("tile_0", "tile_1", "tile_2", "expo")


highest = lax.Precision.HIGHEST
contract = (((1, 2), (1, 2)), ((), ()))


def turned_gather(arrays, axis, dims):
    turned = [jnp.moveaxis(a, dim, 0) for a, dim in zip(arrays, dims)]
    both = jnp.concatenate([t.reshape(len(t), -1) for t in turned], axis=1)
    filled, at, done = (lax.all_gather(both, axis, axis=0, tiled=True), 0, [])
    for t, dim in zip(turned, dims):
        piece = filled[:, at : at + t[0].size].reshape(-1, *t.shape[1:])
        done.append(jnp.moveaxis(piece, 0, dim))
        at += t[0].size
    return tuple(done)


def sum_in_order(tiles, axes, order):
    inside = tiles.shape[1:]
    tiles = tiles.reshape(*(lax.axis_size(a) for a in axes), *inside)
    tiles = jnp.moveaxis(tiles, order, range(len(axes))).reshape(-1, *inside)
    for k in order:
        tiles = lax.psum_scatter(tiles, axes[k], scatter_dimension=0, tiled=True)
    return tiles[0]


def split_up(array, dim, length):
    before, after = (array.shape[:dim], array.shape[dim + 1 :])
    return jnp.moveaxis(array.reshape(*before, length, -1, *after), dim, 0)


def scatter_axes(array, axes, order, dim):
    length = lax.axis_size(axes)
    return sum_in_order(split_up(array, dim, length), axes, order)


def chebyshev(values, degree):
    series = [jnp.ones_like(values), values]
    for degree_at in range(2, degree):
        series.append(2.0 * values * series[-1] - series[-2])
    return series[:degree]


def focal_weight(pixel_uv, ccd_index, observed, obs_weight, live_rows, ccd_center):
    ccd_total = ccd_center.shape[1]
    picked = (
        ccd_index[None, :, :] == jnp.arange(ccd_total, dtype=jnp.int32)[:, None, None]
    ).astype(jnp.float32)
    centre = jnp.sum(ccd_center[:, :, None, None] * picked[None], axis=1)
    focal = 0.75 * centre + 0.25 * pixel_uv
    star_rows = ccd_index.shape[1]
    alive = (jnp.arange(star_rows, dtype=jnp.int32)[None, :] < live_rows).astype(jnp.float32)
    live_weight = obs_weight * observed.astype(jnp.float32) * alive
    return (focal, live_weight)


def basis_of(focal):
    along_first = chebyshev(focal[0], DEG_X)
    along_second = chebyshev(focal[1], DEG_Y)
    return jnp.stack(
        [first_term * second_term for first_term in along_first for second_term in along_second],
        axis=1,
    )


def jacobian_of(geometry):
    shift_time = geometry[0]
    factor_first = geometry[1]
    factor_second = geometry[2]
    unit_row = jnp.ones_like(shift_time)
    zero_row = jnp.zeros_like(shift_time)
    return jnp.stack(
        [
            jnp.stack([unit_row, zero_row, shift_time, zero_row, factor_first], axis=-1),
            jnp.stack([zero_row, unit_row, zero_row, shift_time, factor_second], axis=-1),
        ],
        axis=1,
    )


def geometry_of(exp_geom, exposure_ids):
    picked = (
        jnp.arange(exp_geom.shape[1], dtype=jnp.int32)[:, None] == exposure_ids[None, :]
    ).astype(jnp.float32)
    return (jnp.sum(exp_geom[:, :, None] * picked[None], axis=1), picked)


def coupling_matrix(live_weight, basis, jacobian):
    full = (
        live_weight[:, None, None, None, :]
        * jacobian[:, :, None, :, None]
        * basis[:, None, :, None, :]
    )
    return full.astype(jnp.bfloat16).reshape(basis.shape[0] * 2 * basis.shape[1], 5, basis.shape[2])


def negated_scaled(coupling, inverse):
    return (
        -jnp.einsum("xis,jis->xjs", coupling.astype(jnp.float32), inverse, precision=highest)
    ).astype(jnp.bfloat16)


def diagonal_blocks(live_weight, basis):
    weighted = live_weight[:, None, :] * basis
    gram = jnp.einsum("ams,ans->amn", weighted, basis, precision=highest)
    pair_eye = jnp.eye(2, dtype=jnp.float32)
    full = jnp.einsum("cd,amn->acmdn", pair_eye, gram, precision=highest)
    return (full.reshape(gram.shape[0], 2 * gram.shape[1], 2 * gram.shape[1]), weighted)


def gradient_terms(jacobian, live_weight, obs_resid):
    return jnp.einsum("aci,as,cas->is", jacobian, live_weight, obs_resid, precision=highest)


def local_rhs(weighted, jacobian, obs_resid, solved):
    correction = jnp.einsum("aci,is->cas", jacobian, solved, precision=highest)
    result = jnp.einsum("ams,cas->acm", weighted, obs_resid - correction, precision=highest)
    return result.reshape(weighted.shape[0], 2 * weighted.shape[1])


def star_product(former, latter):
    return lax.dot_general(former, latter, contract, preferred_element_type=jnp.float32)


LANES = 128


def schur_kernel(xa, ya, wa, wda, wfa, wga, xo, yo, wo, wdo, wfo, wgo, si, out, rhs0, rhs1, lhs0, lhs1):
    step = pl.program_id(0)
    bf = jnp.bfloat16
    f32 = jnp.float32
    n_all = xa.shape[0]
    n_own = xo.shape[0]
    terms = DEG_X * DEG_Y

    @pl.when(step == 0)
    def _():
        out[...] = jnp.zeros_like(out)

    tx = chebyshev(xa[...], DEG_X)
    ty = chebyshev(ya[...], DEG_Y)
    txo = chebyshev(xo[...], DEG_X)
    tyo = chebyshev(yo[...], DEG_Y)
    w, wd, wf, wg = wa[...], wda[...], wfa[...], wga[...]
    w_o, wd_o, wf_o, wg_o = wo[...], wdo[...], wfo[...], wgo[...]
    inv = [[si[pl.ds(j * 5 + i, 1), :] for i in range(5)] for j in range(5)]
    for p in range(DEG_X):
        for q in range(DEG_Y):
            m = p * DEG_Y + q
            b = tx[p] * ty[q]
            cp = (w * b).astype(bf).astype(f32)
            cq = (wd * b).astype(bf).astype(f32)
            cr = (wf * b).astype(bf).astype(f32)
            cs = (wg * b).astype(bf).astype(f32)
            for d, (k0, k1, last) in enumerate(((0, 2, cr), (1, 3, cs))):
                rows = pl.ds((d * terms + m) * n_all, n_all)
                sc = [(-(inv[j][k0] * cp + inv[j][k1] * cq + inv[j][4] * last)).astype(bf) for j in range(5)]
                for t, j in enumerate((0, 2, 4)):
                    rhs0[rows, pl.ds(t * LANES, LANES)] = sc[j]
                for t, j in enumerate((1, 3, 4)):
                    rhs1[rows, pl.ds(t * LANES, LANES)] = sc[j]
            bo = txo[p] * tyo[q]
            po = (w_o * bo).astype(bf).astype(f32)
            qo = (wd_o * bo).astype(bf).astype(f32)
            own_rows = pl.ds(m * n_own, n_own)
            lhs0[own_rows, pl.ds(0, LANES)] = po
            lhs0[own_rows, pl.ds(LANES, LANES)] = qo
            lhs0[own_rows, pl.ds(2 * LANES, LANES)] = (wf_o * bo).astype(bf).astype(f32)
            lhs1[own_rows, pl.ds(0, LANES)] = po
            lhs1[own_rows, pl.ds(LANES, LANES)] = qo
            lhs1[own_rows, pl.ds(2 * LANES, LANES)] = (wg_o * bo).astype(bf).astype(f32)
    out[0] += lax.dot_general(lhs0[...].astype(bf), rhs0[...], (((1,), (1,)), ((), ())), preferred_element_type=f32)
    out[1] += lax.dot_general(lhs1[...].astype(bf), rhs1[...], (((1,), (1,)), ((), ())), preferred_element_type=f32)


def schur_product(all_x, all_y, all_w, all_wd, all_wf, all_wg, own_x, own_y, own_w, own_wd, own_wf, own_wg, inverse):
    n_all, stars = all_x.shape
    n_own = own_x.shape[0]
    terms = DEG_X * DEG_Y
    rows_all = 2 * terms * n_all
    rows_own = terms * n_own
    all_spec = pl.BlockSpec((n_all, LANES), lambda k: (0, k))
    own_spec = pl.BlockSpec((n_own, LANES), lambda k: (0, k))
    inv_spec = pl.BlockSpec((25, LANES), lambda k: (0, k))
    return pl.pallas_call(
        schur_kernel,
        out_shape=jax.ShapeDtypeStruct((2, rows_own, rows_all), jnp.float32),
        grid=(stars // LANES,),
        in_specs=[all_spec] * 6 + [own_spec] * 6 + [inv_spec],
        out_specs=pl.BlockSpec((2, rows_own, rows_all), lambda k: (0, 0, 0)),
        scratch_shapes=[
            pltpu.VMEM((rows_all, 3 * LANES), jnp.bfloat16),
            pltpu.VMEM((rows_all, 3 * LANES), jnp.bfloat16),
            pltpu.VMEM((rows_own, 3 * LANES), jnp.float32),
            pltpu.VMEM((rows_own, 3 * LANES), jnp.float32),
        ],
        compiler_params=pltpu.CompilerParams(dimension_semantics=("arbitrary",)),
    )(all_x, all_y, all_w, all_wd, all_wf, all_wg, own_x, own_y, own_w, own_wd, own_wf, own_wg, inverse)


def on_device(
    pixel_uv,
    ccd_index,
    observed,
    obs_weight,
    obs_resid,
    star_inverse,
    star_count,
    ccd_center,
    exp_geom,
    tile_exposures,
    pair_owner,
):
    expo_total = lax.axis_size("expo")
    tile_total = lax.axis_size(TILE)
    expo_rank = lax.axis_index("expo")
    loc_dev = ccd_index.shape[0]
    window = tile_exposures.shape[1]
    params = 2 * DEG_X * DEG_Y
    live_rows = star_count[0]
    exposure_ids = lax.dynamic_slice_in_dim(tile_exposures[0], expo_rank * loc_dev, loc_dev)
    geometry, picked = geometry_of(exp_geom, exposure_ids)
    focal, live_weight = focal_weight(
        pixel_uv, ccd_index, observed, obs_weight, live_rows, ccd_center
    )
    basis = basis_of(focal)
    jacobian = jacobian_of(geometry)
    diagonal, weighted = diagonal_blocks(live_weight, basis)
    own_rows = expo_rank * loc_dev + jnp.arange(loc_dev, dtype=jnp.int32)
    local_rows = jnp.arange(loc_dev, dtype=jnp.int32)
    all_focal, all_weight, all_resid = turned_gather(
        (focal, live_weight, obs_resid), "expo", (1, 0, 1)
    )
    all_geometry, all_picked = geometry_of(exp_geom, tile_exposures[0])
    all_jacobian = jacobian_of(all_geometry)
    all_x, all_y = all_focal[0], all_focal[1]
    own_x, own_y = focal[0], focal[1]
    products = schur_product(
        all_x, all_y, all_weight,
        all_weight * all_geometry[0][:, None], all_weight * all_geometry[1][:, None], all_weight * all_geometry[2][:, None],
        own_x, own_y, live_weight,
        live_weight * geometry[0][:, None], live_weight * geometry[1][:, None], live_weight * geometry[2][:, None],
        star_inverse.reshape(25, -1),
    )
    terms = DEG_X * DEG_Y
    product = products.reshape(2, terms, loc_dev, 2, terms, window)
    product = jnp.transpose(product, (2, 5, 0, 1, 3, 4))
    product = product.at[local_rows, own_rows].add(diagonal.reshape(loc_dev, 2, terms, 2, terms))
    product = product.reshape(loc_dev * window, params * params)
    owners = lax.dynamic_slice_in_dim(pair_owner[0], expo_rank * loc_dev, loc_dev, 0)
    gradient = gradient_terms(all_jacobian, all_weight, all_resid)
    solved = jnp.einsum("jis,is->js", star_inverse, gradient, precision=highest)
    rhs_local = local_rhs(weighted, jacobian, obs_resid, solved)
    devices = tile_total * expo_total
    spread = jnp.dot(picked, rhs_local, precision=highest).reshape(devices, -1)
    pair_dev = 3 * (window // 2) * (window // 2) // expo_total
    flat_owner = owners.reshape(-1)
    target = flat_owner // pair_dev
    ranking = jnp.argsort(target, stable=True)
    per_peer = flat_owner.shape[0] // devices
    outgoing = jnp.take(product, ranking, axis=0).reshape(devices, per_peer * params * params)
    slot_tags = (flat_owner % pair_dev)[ranking].reshape(devices, per_peer).astype(jnp.float32)
    packed = jnp.concatenate([outgoing, spread, slot_tags], axis=1)
    incoming = lax.all_to_all(packed, TILE_EXPO, split_axis=0, concat_axis=0, tiled=True)
    block_len = per_peer * params * params
    incoming_blocks = incoming[:, :block_len].reshape(-1, params * params)
    incoming_rhs = incoming[:, block_len : block_len + spread.shape[1]]
    incoming_tags = incoming[:, block_len + spread.shape[1] :].astype(jnp.int32)
    receive_slots = (
        jnp.arange(pair_dev, dtype=jnp.int32)[:, None] == incoming_tags.reshape(1, -1)
    ).astype(jnp.float32)
    pair_blocks = jnp.dot(receive_slots, incoming_blocks, precision=highest)
    reduced_rhs = jnp.sum(incoming_rhs.reshape(devices, -1, params), axis=0)
    return (pair_blocks, reduced_rhs)


def solution(mesh):
    split = Mesh(
        mesh.devices.reshape(4, 4, 2, mesh.shape["expo"]), ("tile_0", "tile_1", "tile_2", "expo")
    )
    placed = (
        P(None, "expo", TILE),
        P("expo", TILE),
        P("expo", TILE),
        P("expo", TILE),
        P(None, "expo", TILE),
        P(None, None, TILE),
        P(TILE),
        P(),
        P(),
        P(TILE, None),
        P(TILE, None, None),
    )
    return jax.shard_map(
        on_device,
        mesh=split,
        in_specs=placed,
        out_specs=(P(TILE_EXPO, None), P(TILE_EXPO, None)),
        check_vma=False,
    )
```

```python
import jax
import jax.numpy as jnp
from jax import lax
from jax.experimental import pallas as pl
from jax.experimental.pallas import tpu as pltpu
from jax.sharding import Mesh
from jax.sharding import PartitionSpec as P

DEG_X = 6
DEG_Y = 5
TILE = ("tile_0", "tile_1", "tile_2")
TILE_EXPO = ("tile_0", "tile_1", "tile_2", "expo")


highest = lax.Precision.HIGHEST
contract = (((1, 2), (1, 2)), ((), ()))


def turned_gather(arrays, axis, dims):
    turned = [jnp.moveaxis(a, dim, 0) for a, dim in zip(arrays, dims)]
    both = jnp.concatenate([t.reshape(len(t), -1) for t in turned], axis=1)
    filled, at, done = (lax.all_gather(both, axis, axis=0, tiled=True), 0, [])
    for t, dim in zip(turned, dims):
        piece = filled[:, at : at + t[0].size].reshape(-1, *t.shape[1:])
        done.append(jnp.moveaxis(piece, 0, dim))
        at += t[0].size
    return tuple(done)


def sum_in_order(tiles, axes, order):
    inside = tiles.shape[1:]
    tiles = tiles.reshape(*(lax.axis_size(a) for a in axes), *inside)
    tiles = jnp.moveaxis(tiles, order, range(len(axes))).reshape(-1, *inside)
    for k in order:
        tiles = lax.psum_scatter(tiles, axes[k], scatter_dimension=0, tiled=True)
    return tiles[0]


def split_up(array, dim, length):
    before, after = (array.shape[:dim], array.shape[dim + 1 :])
    return jnp.moveaxis(array.reshape(*before, length, -1, *after), dim, 0)


def scatter_axes(array, axes, order, dim):
    length = lax.axis_size(axes)
    return sum_in_order(split_up(array, dim, length), axes, order)


def chebyshev(values, degree):
    series = [jnp.ones_like(values), values]
    for degree_at in range(2, degree):
        series.append(2.0 * values * series[-1] - series[-2])
    return series[:degree]


def focal_weight(pixel_uv, ccd_index, observed, obs_weight, live_rows, ccd_center):
    ccd_total = ccd_center.shape[1]
    picked = (
        ccd_index[None, :, :] == jnp.arange(ccd_total, dtype=jnp.int32)[:, None, None]
    ).astype(jnp.float32)
    centre = jnp.sum(ccd_center[:, :, None, None] * picked[None], axis=1)
    focal = 0.75 * centre + 0.25 * pixel_uv
    star_rows = ccd_index.shape[1]
    alive = (jnp.arange(star_rows, dtype=jnp.int32)[None, :] < live_rows).astype(jnp.float32)
    live_weight = obs_weight * observed.astype(jnp.float32) * alive
    return (focal, live_weight)


def basis_of(focal):
    along_first = chebyshev(focal[0], DEG_X)
    along_second = chebyshev(focal[1], DEG_Y)
    return jnp.stack(
        [first_term * second_term for first_term in along_first for second_term in along_second],
        axis=1,
    )


def jacobian_of(geometry):
    shift_time = geometry[0]
    factor_first = geometry[1]
    factor_second = geometry[2]
    unit_row = jnp.ones_like(shift_time)
    zero_row = jnp.zeros_like(shift_time)
    return jnp.stack(
        [
            jnp.stack([unit_row, zero_row, shift_time, zero_row, factor_first], axis=-1),
            jnp.stack([zero_row, unit_row, zero_row, shift_time, factor_second], axis=-1),
        ],
        axis=1,
    )


def geometry_of(exp_geom, exposure_ids):
    picked = (
        jnp.arange(exp_geom.shape[1], dtype=jnp.int32)[:, None] == exposure_ids[None, :]
    ).astype(jnp.float32)
    return (jnp.sum(exp_geom[:, :, None] * picked[None], axis=1), picked)


def coupling_matrix(live_weight, basis, jacobian):
    full = (
        live_weight[:, None, None, None, :]
        * jacobian[:, :, None, :, None]
        * basis[:, None, :, None, :]
    )
    return full.astype(jnp.bfloat16).reshape(basis.shape[0] * 2 * basis.shape[1], 5, basis.shape[2])


def negated_scaled(coupling, inverse):
    return (
        -jnp.einsum("xis,jis->xjs", coupling.astype(jnp.float32), inverse, precision=highest)
    ).astype(jnp.bfloat16)


def diagonal_blocks(live_weight, basis):
    weighted = live_weight[:, None, :] * basis
    gram = jnp.einsum("ams,ans->amn", weighted, basis, precision=highest)
    pair_eye = jnp.eye(2, dtype=jnp.float32)
    full = jnp.einsum("cd,amn->acmdn", pair_eye, gram, precision=highest)
    return (full.reshape(gram.shape[0], 2 * gram.shape[1], 2 * gram.shape[1]), weighted)


def gradient_terms(jacobian, live_weight, obs_resid):
    return jnp.einsum("aci,as,cas->is", jacobian, live_weight, obs_resid, precision=highest)


def local_rhs(weighted, jacobian, obs_resid, solved):
    correction = jnp.einsum("aci,is->cas", jacobian, solved, precision=highest)
    result = jnp.einsum("ams,cas->acm", weighted, obs_resid - correction, precision=highest)
    return result.reshape(weighted.shape[0], 2 * weighted.shape[1])


def star_product(former, latter):
    return lax.dot_general(former, latter, contract, preferred_element_type=jnp.float32)


LANES = 128


def schur_kernel(xa, ya, wa, wda, wfa, wga, xo, yo, wo, wdo, wfo, wgo, si, out, rhs0, rhs1, lhs0, lhs1):
    step = pl.program_id(0)
    bf = jnp.bfloat16
    f32 = jnp.float32
    n_all = xa.shape[0]
    n_own = xo.shape[0]
    terms = DEG_X * DEG_Y

    @pl.when(step == 0)
    def _():
        out[...] = jnp.zeros_like(out)

    tx = chebyshev(xa[...], DEG_X)
    ty = chebyshev(ya[...], DEG_Y)
    txo = chebyshev(xo[...], DEG_X)
    tyo = chebyshev(yo[...], DEG_Y)
    w, wd, wf, wg = wa[...], wda[...], wfa[...], wga[...]
    w_o, wd_o, wf_o, wg_o = wo[...], wdo[...], wfo[...], wgo[...]
    inv = [[si[pl.ds(j * 5 + i, 1), :] for i in range(5)] for j in range(5)]
    for p in range(DEG_X):
        for q in range(DEG_Y):
            m = p * DEG_Y + q
            b = tx[p] * ty[q]
            cp = (w * b).astype(bf).astype(f32)
            cq = (wd * b).astype(bf).astype(f32)
            cr = (wf * b).astype(bf).astype(f32)
            cs = (wg * b).astype(bf).astype(f32)
            for d, (k0, k1, last) in enumerate(((0, 2, cr), (1, 3, cs))):
                rows = pl.ds((d * terms + m) * n_all, n_all)
                sc = [(-(inv[j][k0] * cp + inv[j][k1] * cq + inv[j][4] * last)).astype(bf) for j in range(5)]
                for t, j in enumerate((0, 2, 4)):
                    rhs0[rows, pl.ds(t * LANES, LANES)] = sc[j]
                for t, j in enumerate((1, 3, 4)):
                    rhs1[rows, pl.ds(t * LANES, LANES)] = sc[j]
            bo = txo[p] * tyo[q]
            po = (w_o * bo).astype(bf).astype(f32)
            qo = (wd_o * bo).astype(bf).astype(f32)
            own_rows = pl.ds(m * n_own, n_own)
            lhs0[own_rows, pl.ds(0, LANES)] = po
            lhs0[own_rows, pl.ds(LANES, LANES)] = qo
            lhs0[own_rows, pl.ds(2 * LANES, LANES)] = (wf_o * bo).astype(bf).astype(f32)
            lhs1[own_rows, pl.ds(0, LANES)] = po
            lhs1[own_rows, pl.ds(LANES, LANES)] = qo
            lhs1[own_rows, pl.ds(2 * LANES, LANES)] = (wg_o * bo).astype(bf).astype(f32)
    out[0] += lax.dot_general(lhs0[...].astype(bf), rhs0[...], (((1,), (1,)), ((), ())), preferred_element_type=f32)
    out[1] += lax.dot_general(lhs1[...].astype(bf), rhs1[...], (((1,), (1,)), ((), ())), preferred_element_type=f32)


def schur_product(all_x, all_y, all_w, all_wd, all_wf, all_wg, own_x, own_y, own_w, own_wd, own_wf, own_wg, inverse):
    n_all, stars = all_x.shape
    n_own = own_x.shape[0]
    terms = DEG_X * DEG_Y
    rows_all = 2 * terms * n_all
    rows_own = terms * n_own
    all_spec = pl.BlockSpec((n_all, LANES), lambda k: (0, k))
    own_spec = pl.BlockSpec((n_own, LANES), lambda k: (0, k))
    inv_spec = pl.BlockSpec((25, LANES), lambda k: (0, k))
    return pl.pallas_call(
        schur_kernel,
        out_shape=jax.ShapeDtypeStruct((2, rows_own, rows_all), jnp.float32),
        grid=(stars // LANES,),
        in_specs=[all_spec] * 6 + [own_spec] * 6 + [inv_spec],
        out_specs=pl.BlockSpec((2, rows_own, rows_all), lambda k: (0, 0, 0)),
        scratch_shapes=[
            pltpu.VMEM((rows_all, 3 * LANES), jnp.bfloat16),
            pltpu.VMEM((rows_all, 3 * LANES), jnp.bfloat16),
            pltpu.VMEM((rows_own, 3 * LANES), jnp.float32),
            pltpu.VMEM((rows_own, 3 * LANES), jnp.float32),
        ],
        compiler_params=pltpu.CompilerParams(dimension_semantics=("arbitrary",)),
    )(all_x, all_y, all_w, all_wd, all_wf, all_wg, own_x, own_y, own_w, own_wd, own_wf, own_wg, inverse)


def on_device(
    pixel_uv,
    ccd_index,
    observed,
    obs_weight,
    obs_resid,
    star_inverse,
    star_count,
    ccd_center,
    exp_geom,
    tile_exposures,
    pair_owner,
):
    expo_total = lax.axis_size("expo")
    tile_total = lax.axis_size(TILE)
    expo_rank = lax.axis_index("expo")
    loc_dev = ccd_index.shape[0]
    window = tile_exposures.shape[1]
    params = 2 * DEG_X * DEG_Y
    live_rows = star_count[0]
    exposure_ids = lax.dynamic_slice_in_dim(tile_exposures[0], expo_rank * loc_dev, loc_dev)
    geometry, picked = geometry_of(exp_geom, exposure_ids)
    focal, live_weight = focal_weight(
        pixel_uv, ccd_index, observed, obs_weight, live_rows, ccd_center
    )
    basis = basis_of(focal)
    jacobian = jacobian_of(geometry)
    diagonal, weighted = diagonal_blocks(live_weight, basis)
    own_rows = expo_rank * loc_dev + jnp.arange(loc_dev, dtype=jnp.int32)
    local_rows = jnp.arange(loc_dev, dtype=jnp.int32)
    all_focal, all_weight, all_resid = turned_gather(
        (focal, live_weight, obs_resid), "expo", (1, 0, 1)
    )
    all_geometry, all_picked = geometry_of(exp_geom, tile_exposures[0])
    all_jacobian = jacobian_of(all_geometry)
    all_x, all_y = all_focal[0], all_focal[1]
    own_x, own_y = focal[0], focal[1]
    products = schur_product(
        all_x, all_y, all_weight,
        all_weight * all_geometry[0][:, None], all_weight * all_geometry[1][:, None], all_weight * all_geometry[2][:, None],
        own_x, own_y, live_weight,
        live_weight * geometry[0][:, None], live_weight * geometry[1][:, None], live_weight * geometry[2][:, None],
        star_inverse.reshape(25, -1),
    )
    terms = DEG_X * DEG_Y
    product = products.reshape(2, terms, loc_dev, params, window)
    product = jnp.transpose(product, (2, 4, 0, 1, 3)).reshape(loc_dev * window, params * params)
    product = product.at[local_rows * window + own_rows].add(diagonal.reshape(loc_dev, params * params))
    owners = lax.dynamic_slice_in_dim(pair_owner[0], expo_rank * loc_dev, loc_dev, 0)
    gradient = gradient_terms(all_jacobian, all_weight, all_resid)
    solved = jnp.einsum("jis,is->js", star_inverse, gradient, precision=highest)
    rhs_local = local_rhs(weighted, jacobian, obs_resid, solved)
    devices = tile_total * expo_total
    spread = jnp.dot(picked, rhs_local, precision=highest).reshape(devices, -1)
    pair_dev = 3 * (window // 2) * (window // 2) // expo_total
    flat_owner = owners.reshape(-1)
    target = flat_owner // pair_dev
    ranking = jnp.argsort(target, stable=True)
    per_peer = flat_owner.shape[0] // devices
    outgoing = jnp.take(product, ranking, axis=0)
    slot_tags = (flat_owner % pair_dev)[ranking].reshape(devices, per_peer).astype(jnp.float32)
    small = jnp.concatenate([spread, slot_tags], axis=1)
    incoming_blocks = lax.all_to_all(outgoing, TILE_EXPO, split_axis=0, concat_axis=0, tiled=True)
    incoming_small = lax.all_to_all(small, TILE_EXPO, split_axis=0, concat_axis=0, tiled=True)
    incoming_rhs = incoming_small[:, : spread.shape[1]]
    incoming_tags = incoming_small[:, spread.shape[1] :].astype(jnp.int32)
    receive_slots = (
        jnp.arange(pair_dev, dtype=jnp.int32)[:, None] == incoming_tags.reshape(1, -1)
    ).astype(jnp.float32)
    pair_blocks = jnp.dot(receive_slots, incoming_blocks, precision=highest)
    reduced_rhs = jnp.sum(incoming_rhs.reshape(devices, -1, params), axis=0)
    return (pair_blocks, reduced_rhs)


def solution(mesh):
    split = Mesh(
        mesh.devices.reshape(4, 4, 2, mesh.shape["expo"]), ("tile_0", "tile_1", "tile_2", "expo")
    )
    placed = (
        P(None, "expo", TILE),
        P("expo", TILE),
        P("expo", TILE),
        P("expo", TILE),
        P(None, "expo", TILE),
        P(None, None, TILE),
        P(TILE),
        P(),
        P(),
        P(TILE, None),
        P(TILE, None, None),
    )
    return jax.shard_map(
        on_device,
        mesh=split,
        in_specs=placed,
        out_specs=(P(TILE_EXPO, None), P(TILE_EXPO, None)),
        check_vma=False,
    )
```

```python
import jax
import jax.numpy as jnp
from jax import lax
from jax.experimental import pallas as pl
from jax.experimental.pallas import tpu as pltpu
from jax.sharding import Mesh
from jax.sharding import PartitionSpec as P

DEG_X = 6
DEG_Y = 5
TILE = ("tile_0", "tile_1", "tile_2")
TILE_EXPO = ("tile_0", "tile_1", "tile_2", "expo")


highest = lax.Precision.HIGHEST
contract = (((1, 2), (1, 2)), ((), ()))


def turned_gather(arrays, axis, dims):
    turned = [jnp.moveaxis(a, dim, 0) for a, dim in zip(arrays, dims)]
    both = jnp.concatenate([t.reshape(len(t), -1) for t in turned], axis=1)
    filled, at, done = (lax.all_gather(both, axis, axis=0, tiled=True), 0, [])
    for t, dim in zip(turned, dims):
        piece = filled[:, at : at + t[0].size].reshape(-1, *t.shape[1:])
        done.append(jnp.moveaxis(piece, 0, dim))
        at += t[0].size
    return tuple(done)


def sum_in_order(tiles, axes, order):
    inside = tiles.shape[1:]
    tiles = tiles.reshape(*(lax.axis_size(a) for a in axes), *inside)
    tiles = jnp.moveaxis(tiles, order, range(len(axes))).reshape(-1, *inside)
    for k in order:
        tiles = lax.psum_scatter(tiles, axes[k], scatter_dimension=0, tiled=True)
    return tiles[0]


def split_up(array, dim, length):
    before, after = (array.shape[:dim], array.shape[dim + 1 :])
    return jnp.moveaxis(array.reshape(*before, length, -1, *after), dim, 0)


def scatter_axes(array, axes, order, dim):
    length = lax.axis_size(axes)
    return sum_in_order(split_up(array, dim, length), axes, order)


def chebyshev(values, degree):
    series = [jnp.ones_like(values), values]
    for degree_at in range(2, degree):
        series.append(2.0 * values * series[-1] - series[-2])
    return series[:degree]


def focal_weight(pixel_uv, ccd_index, observed, obs_weight, live_rows, ccd_center):
    ccd_total = ccd_center.shape[1]
    picked = (
        ccd_index[None, :, :] == jnp.arange(ccd_total, dtype=jnp.int32)[:, None, None]
    ).astype(jnp.float32)
    centre = jnp.sum(ccd_center[:, :, None, None] * picked[None], axis=1)
    focal = 0.75 * centre + 0.25 * pixel_uv
    star_rows = ccd_index.shape[1]
    alive = (jnp.arange(star_rows, dtype=jnp.int32)[None, :] < live_rows).astype(jnp.float32)
    live_weight = obs_weight * observed.astype(jnp.float32) * alive
    return (focal, live_weight)


def basis_of(focal):
    along_first = chebyshev(focal[0], DEG_X)
    along_second = chebyshev(focal[1], DEG_Y)
    return jnp.stack(
        [first_term * second_term for first_term in along_first for second_term in along_second],
        axis=1,
    )


def jacobian_of(geometry):
    shift_time = geometry[0]
    factor_first = geometry[1]
    factor_second = geometry[2]
    unit_row = jnp.ones_like(shift_time)
    zero_row = jnp.zeros_like(shift_time)
    return jnp.stack(
        [
            jnp.stack([unit_row, zero_row, shift_time, zero_row, factor_first], axis=-1),
            jnp.stack([zero_row, unit_row, zero_row, shift_time, factor_second], axis=-1),
        ],
        axis=1,
    )


def geometry_of(exp_geom, exposure_ids):
    picked = (
        jnp.arange(exp_geom.shape[1], dtype=jnp.int32)[:, None] == exposure_ids[None, :]
    ).astype(jnp.float32)
    return (jnp.sum(exp_geom[:, :, None] * picked[None], axis=1), picked)


def coupling_matrix(live_weight, basis, jacobian):
    full = (
        live_weight[:, None, None, None, :]
        * jacobian[:, :, None, :, None]
        * basis[:, None, :, None, :]
    )
    return full.astype(jnp.bfloat16).reshape(basis.shape[0] * 2 * basis.shape[1], 5, basis.shape[2])


def negated_scaled(coupling, inverse):
    return (
        -jnp.einsum("xis,jis->xjs", coupling.astype(jnp.float32), inverse, precision=highest)
    ).astype(jnp.bfloat16)


def diagonal_blocks(live_weight, basis):
    weighted = live_weight[:, None, :] * basis
    gram = jnp.einsum("ams,ans->amn", weighted, basis, precision=highest)
    pair_eye = jnp.eye(2, dtype=jnp.float32)
    full = jnp.einsum("cd,amn->acmdn", pair_eye, gram, precision=highest)
    return (full.reshape(gram.shape[0], 2 * gram.shape[1], 2 * gram.shape[1]), weighted)


def gradient_terms(jacobian, live_weight, obs_resid):
    return jnp.einsum("aci,as,cas->is", jacobian, live_weight, obs_resid, precision=highest)


def local_rhs(weighted, jacobian, obs_resid, solved):
    correction = jnp.einsum("aci,is->cas", jacobian, solved, precision=highest)
    result = jnp.einsum("ams,cas->acm", weighted, obs_resid - correction, precision=highest)
    return result.reshape(weighted.shape[0], 2 * weighted.shape[1])


def star_product(former, latter):
    return lax.dot_general(former, latter, contract, preferred_element_type=jnp.float32)


LANES = 128


def schur_kernel(xa, ya, wa, wda, wfa, wga, xo, yo, wo, wdo, wfo, wgo, si, out, rhs0, rhs1, lhs0, lhs1):
    step = pl.program_id(0)
    bf = jnp.bfloat16
    f32 = jnp.float32
    n_all = xa.shape[0]
    n_own = xo.shape[0]
    terms = DEG_X * DEG_Y

    @pl.when(step == 0)
    def _():
        out[...] = jnp.zeros_like(out)

    tx = chebyshev(xa[...], DEG_X)
    ty = chebyshev(ya[...], DEG_Y)
    txo = chebyshev(xo[...], DEG_X)
    tyo = chebyshev(yo[...], DEG_Y)
    w, wd, wf, wg = wa[...], wda[...], wfa[...], wga[...]
    w_o, wd_o, wf_o, wg_o = wo[...], wdo[...], wfo[...], wgo[...]
    inv = [[si[pl.ds(j * 5 + i, 1), :] for i in range(5)] for j in range(5)]
    for p in range(DEG_X):
        for q in range(DEG_Y):
            m = p * DEG_Y + q
            b = tx[p] * ty[q]
            cp = (w * b).astype(bf).astype(f32)
            cq = (wd * b).astype(bf).astype(f32)
            cr = (wf * b).astype(bf).astype(f32)
            cs = (wg * b).astype(bf).astype(f32)
            for d, (k0, k1, last) in enumerate(((0, 2, cr), (1, 3, cs))):
                rows = pl.ds((d * terms + m) * n_all, n_all)
                sc = [(-(inv[j][k0] * cp + inv[j][k1] * cq + inv[j][4] * last)).astype(bf) for j in range(5)]
                for t, j in enumerate((0, 2, 4)):
                    rhs0[rows, pl.ds(t * LANES, LANES)] = sc[j]
                for t, j in enumerate((1, 3, 4)):
                    rhs1[rows, pl.ds(t * LANES, LANES)] = sc[j]
            bo = txo[p] * tyo[q]
            po = (w_o * bo).astype(bf).astype(f32)
            qo = (wd_o * bo).astype(bf).astype(f32)
            own_rows = pl.ds(m * n_own, n_own)
            lhs0[own_rows, pl.ds(0, LANES)] = po
            lhs0[own_rows, pl.ds(LANES, LANES)] = qo
            lhs0[own_rows, pl.ds(2 * LANES, LANES)] = (wf_o * bo).astype(bf).astype(f32)
            lhs1[own_rows, pl.ds(0, LANES)] = po
            lhs1[own_rows, pl.ds(LANES, LANES)] = qo
            lhs1[own_rows, pl.ds(2 * LANES, LANES)] = (wg_o * bo).astype(bf).astype(f32)
    out[0] += lax.dot_general(lhs0[...].astype(bf), rhs0[...], (((1,), (1,)), ((), ())), preferred_element_type=f32)
    out[1] += lax.dot_general(lhs1[...].astype(bf), rhs1[...], (((1,), (1,)), ((), ())), preferred_element_type=f32)


def schur_product(all_x, all_y, all_w, all_wd, all_wf, all_wg, own_x, own_y, own_w, own_wd, own_wf, own_wg, inverse):
    n_all, stars = all_x.shape
    n_own = own_x.shape[0]
    terms = DEG_X * DEG_Y
    rows_all = 2 * terms * n_all
    rows_own = terms * n_own
    all_spec = pl.BlockSpec((n_all, LANES), lambda k: (0, k))
    own_spec = pl.BlockSpec((n_own, LANES), lambda k: (0, k))
    inv_spec = pl.BlockSpec((25, LANES), lambda k: (0, k))
    return pl.pallas_call(
        schur_kernel,
        out_shape=jax.ShapeDtypeStruct((2, rows_own, rows_all), jnp.float32),
        grid=(stars // LANES,),
        in_specs=[all_spec] * 6 + [own_spec] * 6 + [inv_spec],
        out_specs=pl.BlockSpec((2, rows_own, rows_all), lambda k: (0, 0, 0)),
        scratch_shapes=[
            pltpu.VMEM((rows_all, 3 * LANES), jnp.bfloat16),
            pltpu.VMEM((rows_all, 3 * LANES), jnp.bfloat16),
            pltpu.VMEM((rows_own, 3 * LANES), jnp.float32),
            pltpu.VMEM((rows_own, 3 * LANES), jnp.float32),
        ],
        compiler_params=pltpu.CompilerParams(dimension_semantics=("arbitrary",)),
    )(all_x, all_y, all_w, all_wd, all_wf, all_wg, own_x, own_y, own_w, own_wd, own_wf, own_wg, inverse)


def on_device(
    pixel_uv,
    ccd_index,
    observed,
    obs_weight,
    obs_resid,
    star_inverse,
    star_count,
    ccd_center,
    exp_geom,
    tile_exposures,
    pair_owner,
):
    expo_total = lax.axis_size("expo")
    tile_total = lax.axis_size(TILE)
    expo_rank = lax.axis_index("expo")
    loc_dev = ccd_index.shape[0]
    window = tile_exposures.shape[1]
    params = 2 * DEG_X * DEG_Y
    live_rows = star_count[0]
    exposure_ids = lax.dynamic_slice_in_dim(tile_exposures[0], expo_rank * loc_dev, loc_dev)
    geometry, picked = geometry_of(exp_geom, exposure_ids)
    focal, live_weight = focal_weight(
        pixel_uv, ccd_index, observed, obs_weight, live_rows, ccd_center
    )
    basis = basis_of(focal)
    jacobian = jacobian_of(geometry)
    diagonal, weighted = diagonal_blocks(live_weight, basis)
    own_rows = expo_rank * loc_dev + jnp.arange(loc_dev, dtype=jnp.int32)
    local_rows = jnp.arange(loc_dev, dtype=jnp.int32)
    all_focal, all_weight, all_resid = turned_gather(
        (focal, live_weight, obs_resid), "expo", (1, 0, 1)
    )
    all_geometry, all_picked = geometry_of(exp_geom, tile_exposures[0])
    all_jacobian = jacobian_of(all_geometry)
    all_x, all_y = all_focal[0], all_focal[1]
    own_x, own_y = focal[0], focal[1]
    products = schur_product(
        all_x, all_y, all_weight,
        all_weight * all_geometry[0][:, None], all_weight * all_geometry[1][:, None], all_weight * all_geometry[2][:, None],
        own_x, own_y, live_weight,
        live_weight * geometry[0][:, None], live_weight * geometry[1][:, None], live_weight * geometry[2][:, None],
        star_inverse.reshape(25, -1),
    )
    terms = DEG_X * DEG_Y
    product = products.reshape(2, terms, loc_dev, params, window)
    product = jnp.transpose(product, (2, 4, 0, 1, 3)).reshape(loc_dev, window, params * params)
    on_diagonal = own_rows[:, None] == jnp.arange(window, dtype=jnp.int32)[None, :]
    diagonal_flat = diagonal.reshape(loc_dev, 1, params * params)
    product = product + jnp.where(on_diagonal[:, :, None], diagonal_flat, 0.0)
    product = product.reshape(loc_dev * window, params * params)
    owners = lax.dynamic_slice_in_dim(pair_owner[0], expo_rank * loc_dev, loc_dev, 0)
    gradient = gradient_terms(all_jacobian, all_weight, all_resid)
    solved = jnp.einsum("jis,is->js", star_inverse, gradient, precision=highest)
    rhs_local = local_rhs(weighted, jacobian, obs_resid, solved)
    devices = tile_total * expo_total
    spread = jnp.dot(picked, rhs_local, precision=highest).reshape(devices, -1)
    pair_dev = 3 * (window // 2) * (window // 2) // expo_total
    flat_owner = owners.reshape(-1)
    target = flat_owner // pair_dev
    ranking = jnp.argsort(target, stable=True)
    per_peer = flat_owner.shape[0] // devices
    outgoing = jnp.take(product, ranking.reshape(devices, per_peer), axis=0, mode="clip")
    slot_tags = (flat_owner % pair_dev)[ranking].reshape(devices, per_peer).astype(jnp.float32)
    small = jnp.concatenate([spread, slot_tags], axis=1)
    incoming_blocks = lax.all_to_all(outgoing, TILE_EXPO, split_axis=0, concat_axis=0, tiled=True)
    incoming_small = lax.all_to_all(small, TILE_EXPO, split_axis=0, concat_axis=0, tiled=True)
    incoming_rhs = incoming_small[:, : spread.shape[1]]
    incoming_tags = incoming_small[:, spread.shape[1] :].astype(jnp.int32)
    receive_slots = (
        jnp.arange(pair_dev, dtype=jnp.int32)[:, None] == incoming_tags.reshape(1, -1)
    ).astype(jnp.float32)
    receive_slots = receive_slots.reshape(pair_dev, devices, per_peer)
    pair_blocks = lax.dot_general(
        receive_slots, incoming_blocks, (((1, 2), (0, 1)), ((), ())), precision=highest
    )
    reduced_rhs = jnp.sum(incoming_rhs.reshape(devices, -1, params), axis=0)
    return (pair_blocks, reduced_rhs)


def solution(mesh):
    split = Mesh(
        mesh.devices.reshape(4, 4, 2, mesh.shape["expo"]), ("tile_0", "tile_1", "tile_2", "expo")
    )
    placed = (
        P(None, "expo", TILE),
        P("expo", TILE),
        P("expo", TILE),
        P("expo", TILE),
        P(None, "expo", TILE),
        P(None, None, TILE),
        P(TILE),
        P(),
        P(),
        P(TILE, None),
        P(TILE, None, None),
    )
    return jax.shard_map(
        on_device,
        mesh=split,
        in_specs=placed,
        out_specs=(P(TILE_EXPO, None), P(TILE_EXPO, None)),
        check_vma=False,
    )
```

```python
import jax
import jax.numpy as jnp
from jax import lax
from jax.experimental import pallas as pl
from jax.experimental.pallas import tpu as pltpu
from jax.sharding import Mesh
from jax.sharding import PartitionSpec as P

DEG_X = 6
DEG_Y = 5
TILE = ("tile_0", "tile_1", "tile_2")
TILE_EXPO = ("tile_0", "tile_1", "tile_2", "expo")


highest = lax.Precision.HIGHEST
contract = (((1, 2), (1, 2)), ((), ()))


def turned_gather(arrays, axis, dims):
    turned = [jnp.moveaxis(a, dim, 0) for a, dim in zip(arrays, dims)]
    both = jnp.concatenate([t.reshape(len(t), -1) for t in turned], axis=1)
    filled, at, done = (lax.all_gather(both, axis, axis=0, tiled=True), 0, [])
    for t, dim in zip(turned, dims):
        piece = filled[:, at : at + t[0].size].reshape(-1, *t.shape[1:])
        done.append(jnp.moveaxis(piece, 0, dim))
        at += t[0].size
    return tuple(done)


def sum_in_order(tiles, axes, order):
    inside = tiles.shape[1:]
    tiles = tiles.reshape(*(lax.axis_size(a) for a in axes), *inside)
    tiles = jnp.moveaxis(tiles, order, range(len(axes))).reshape(-1, *inside)
    for k in order:
        tiles = lax.psum_scatter(tiles, axes[k], scatter_dimension=0, tiled=True)
    return tiles[0]


def split_up(array, dim, length):
    before, after = (array.shape[:dim], array.shape[dim + 1 :])
    return jnp.moveaxis(array.reshape(*before, length, -1, *after), dim, 0)


def scatter_axes(array, axes, order, dim):
    length = lax.axis_size(axes)
    return sum_in_order(split_up(array, dim, length), axes, order)


def chebyshev(values, degree):
    series = [jnp.ones_like(values), values]
    for degree_at in range(2, degree):
        series.append(2.0 * values * series[-1] - series[-2])
    return series[:degree]


def focal_weight(pixel_uv, ccd_index, observed, obs_weight, live_rows, ccd_center):
    ccd_total = ccd_center.shape[1]
    picked = (
        ccd_index[None, :, :] == jnp.arange(ccd_total, dtype=jnp.int32)[:, None, None]
    ).astype(jnp.float32)
    centre = jnp.sum(ccd_center[:, :, None, None] * picked[None], axis=1)
    focal = 0.75 * centre + 0.25 * pixel_uv
    star_rows = ccd_index.shape[1]
    alive = (jnp.arange(star_rows, dtype=jnp.int32)[None, :] < live_rows).astype(jnp.float32)
    live_weight = obs_weight * observed.astype(jnp.float32) * alive
    return (focal, live_weight)


def basis_of(focal):
    along_first = chebyshev(focal[0], DEG_X)
    along_second = chebyshev(focal[1], DEG_Y)
    return jnp.stack(
        [first_term * second_term for first_term in along_first for second_term in along_second],
        axis=1,
    )


def jacobian_of(geometry):
    shift_time = geometry[0]
    factor_first = geometry[1]
    factor_second = geometry[2]
    unit_row = jnp.ones_like(shift_time)
    zero_row = jnp.zeros_like(shift_time)
    return jnp.stack(
        [
            jnp.stack([unit_row, zero_row, shift_time, zero_row, factor_first], axis=-1),
            jnp.stack([zero_row, unit_row, zero_row, shift_time, factor_second], axis=-1),
        ],
        axis=1,
    )


def geometry_of(exp_geom, exposure_ids):
    picked = (
        jnp.arange(exp_geom.shape[1], dtype=jnp.int32)[:, None] == exposure_ids[None, :]
    ).astype(jnp.float32)
    return (jnp.sum(exp_geom[:, :, None] * picked[None], axis=1), picked)


def coupling_matrix(live_weight, basis, jacobian):
    full = (
        live_weight[:, None, None, None, :]
        * jacobian[:, :, None, :, None]
        * basis[:, None, :, None, :]
    )
    return full.astype(jnp.bfloat16).reshape(basis.shape[0] * 2 * basis.shape[1], 5, basis.shape[2])


def negated_scaled(coupling, inverse):
    return (
        -jnp.einsum("xis,jis->xjs", coupling.astype(jnp.float32), inverse, precision=highest)
    ).astype(jnp.bfloat16)


def diagonal_blocks(live_weight, basis):
    weighted = live_weight[:, None, :] * basis
    gram = jnp.einsum("ams,ans->amn", weighted, basis, precision=highest)
    pair_eye = jnp.eye(2, dtype=jnp.float32)
    full = jnp.einsum("cd,amn->acmdn", pair_eye, gram, precision=highest)
    return (full.reshape(gram.shape[0], 2 * gram.shape[1], 2 * gram.shape[1]), weighted)


def gradient_terms(jacobian, live_weight, obs_resid):
    return jnp.einsum("aci,as,cas->is", jacobian, live_weight, obs_resid, precision=highest)


def local_rhs(weighted, jacobian, obs_resid, solved):
    correction = jnp.einsum("aci,is->cas", jacobian, solved, precision=highest)
    result = jnp.einsum("ams,cas->acm", weighted, obs_resid - correction, precision=highest)
    return result.reshape(weighted.shape[0], 2 * weighted.shape[1])


def star_product(former, latter):
    return lax.dot_general(former, latter, contract, preferred_element_type=jnp.float32)


LANES = 128


def schur_kernel(xa, ya, wa, wda, wfa, wga, xo, yo, wo, wdo, wfo, wgo, si, out, rhs0, rhs1, lhs0, lhs1):
    step = pl.program_id(0)
    bf = jnp.bfloat16
    f32 = jnp.float32
    n_all = xa.shape[0]
    n_own = xo.shape[0]
    terms = DEG_X * DEG_Y

    @pl.when(step == 0)
    def _():
        out[...] = jnp.zeros_like(out)

    tx = chebyshev(xa[...], DEG_X)
    ty = chebyshev(ya[...], DEG_Y)
    txo = chebyshev(xo[...], DEG_X)
    tyo = chebyshev(yo[...], DEG_Y)
    w, wd, wf, wg = wa[...], wda[...], wfa[...], wga[...]
    w_o, wd_o, wf_o, wg_o = wo[...], wdo[...], wfo[...], wgo[...]
    inv = [[si[pl.ds(j * 5 + i, 1), :] for i in range(5)] for j in range(5)]
    for p in range(DEG_X):
        for q in range(DEG_Y):
            m = p * DEG_Y + q
            b = tx[p] * ty[q]
            cp = (w * b).astype(bf).astype(f32)
            cq = (wd * b).astype(bf).astype(f32)
            cr = (wf * b).astype(bf).astype(f32)
            cs = (wg * b).astype(bf).astype(f32)
            for d, (k0, k1, last) in enumerate(((0, 2, cr), (1, 3, cs))):
                rows = pl.ds((d * terms + m) * n_all, n_all)
                sc = [(-(inv[j][k0] * cp + inv[j][k1] * cq + inv[j][4] * last)).astype(bf) for j in range(5)]
                for t, j in enumerate((0, 2, 4)):
                    rhs0[rows, pl.ds(t * LANES, LANES)] = sc[j]
                for t, j in enumerate((1, 3, 4)):
                    rhs1[rows, pl.ds(t * LANES, LANES)] = sc[j]
            bo = txo[p] * tyo[q]
            po = (w_o * bo).astype(bf).astype(f32)
            qo = (wd_o * bo).astype(bf).astype(f32)
            own_rows = pl.ds(m * n_own, n_own)
            lhs0[own_rows, pl.ds(0, LANES)] = po
            lhs0[own_rows, pl.ds(LANES, LANES)] = qo
            lhs0[own_rows, pl.ds(2 * LANES, LANES)] = (wf_o * bo).astype(bf).astype(f32)
            lhs1[own_rows, pl.ds(0, LANES)] = po
            lhs1[own_rows, pl.ds(LANES, LANES)] = qo
            lhs1[own_rows, pl.ds(2 * LANES, LANES)] = (wg_o * bo).astype(bf).astype(f32)
    out[0] += lax.dot_general(lhs0[...].astype(bf), rhs0[...], (((1,), (1,)), ((), ())), preferred_element_type=f32)
    out[1] += lax.dot_general(lhs1[...].astype(bf), rhs1[...], (((1,), (1,)), ((), ())), preferred_element_type=f32)


def schur_product(all_x, all_y, all_w, all_wd, all_wf, all_wg, own_x, own_y, own_w, own_wd, own_wf, own_wg, inverse):
    n_all, stars = all_x.shape
    n_own = own_x.shape[0]
    terms = DEG_X * DEG_Y
    rows_all = 2 * terms * n_all
    rows_own = terms * n_own
    all_spec = pl.BlockSpec((n_all, LANES), lambda k: (0, k))
    own_spec = pl.BlockSpec((n_own, LANES), lambda k: (0, k))
    inv_spec = pl.BlockSpec((25, LANES), lambda k: (0, k))
    return pl.pallas_call(
        schur_kernel,
        out_shape=jax.ShapeDtypeStruct((2, rows_own, rows_all), jnp.float32),
        grid=(stars // LANES,),
        in_specs=[all_spec] * 6 + [own_spec] * 6 + [inv_spec],
        out_specs=pl.BlockSpec((2, rows_own, rows_all), lambda k: (0, 0, 0)),
        scratch_shapes=[
            pltpu.VMEM((rows_all, 3 * LANES), jnp.bfloat16),
            pltpu.VMEM((rows_all, 3 * LANES), jnp.bfloat16),
            pltpu.VMEM((rows_own, 3 * LANES), jnp.float32),
            pltpu.VMEM((rows_own, 3 * LANES), jnp.float32),
        ],
        compiler_params=pltpu.CompilerParams(dimension_semantics=("arbitrary",)),
    )(all_x, all_y, all_w, all_wd, all_wf, all_wg, own_x, own_y, own_w, own_wd, own_wf, own_wg, inverse)


def on_device(
    pixel_uv,
    ccd_index,
    observed,
    obs_weight,
    obs_resid,
    star_inverse,
    star_count,
    ccd_center,
    exp_geom,
    tile_exposures,
    pair_owner,
):
    expo_total = lax.axis_size("expo")
    tile_total = lax.axis_size(TILE)
    expo_rank = lax.axis_index("expo")
    loc_dev = ccd_index.shape[0]
    window = tile_exposures.shape[1]
    params = 2 * DEG_X * DEG_Y
    live_rows = star_count[0]
    exposure_ids = lax.dynamic_slice_in_dim(tile_exposures[0], expo_rank * loc_dev, loc_dev)
    geometry, picked = geometry_of(exp_geom, exposure_ids)
    focal, live_weight = focal_weight(
        pixel_uv, ccd_index, observed, obs_weight, live_rows, ccd_center
    )
    basis = basis_of(focal)
    jacobian = jacobian_of(geometry)
    diagonal, weighted = diagonal_blocks(live_weight, basis)
    own_rows = expo_rank * loc_dev + jnp.arange(loc_dev, dtype=jnp.int32)
    local_rows = jnp.arange(loc_dev, dtype=jnp.int32)
    all_focal, all_weight, all_resid = turned_gather(
        (focal, live_weight, obs_resid), "expo", (1, 0, 1)
    )
    all_geometry, all_picked = geometry_of(exp_geom, tile_exposures[0])
    all_jacobian = jacobian_of(all_geometry)
    all_x, all_y = all_focal[0], all_focal[1]
    own_x, own_y = focal[0], focal[1]
    products = schur_product(
        all_x, all_y, all_weight,
        all_weight * all_geometry[0][:, None], all_weight * all_geometry[1][:, None], all_weight * all_geometry[2][:, None],
        own_x, own_y, live_weight,
        live_weight * geometry[0][:, None], live_weight * geometry[1][:, None], live_weight * geometry[2][:, None],
        star_inverse.reshape(25, -1),
    )
    terms = DEG_X * DEG_Y
    owners = lax.dynamic_slice_in_dim(pair_owner[0], expo_rank * loc_dev, loc_dev, 0)
    gradient = gradient_terms(all_jacobian, all_weight, all_resid)
    solved = jnp.einsum("jis,is->js", star_inverse, gradient, precision=highest)
    rhs_local = local_rhs(weighted, jacobian, obs_resid, solved)
    devices = tile_total * expo_total
    pair_dev = 3 * (window // 2) * (window // 2) // expo_total
    flat_owner = owners.reshape(-1)
    entries = flat_owner.shape[0]
    per_peer = entries // devices
    target = flat_owner // pair_dev
    ranking = jnp.argsort(target, stable=True)
    place = jnp.zeros((entries,), jnp.int32).at[ranking].set(jnp.arange(entries, dtype=jnp.int32))
    spread = jnp.dot(picked, rhs_local, precision=highest).reshape(devices, per_peer, -1)
    extra = jnp.concatenate(
        [(flat_owner % pair_dev).astype(jnp.float32)[:, None], spread.reshape(entries, -1)[place]], axis=1
    )
    product = products.reshape(2, terms, loc_dev, params, window)
    product = jnp.transpose(product, (2, 4, 0, 1, 3)).reshape(loc_dev, window, params * params)
    on_diagonal = own_rows[:, None] == jnp.arange(window, dtype=jnp.int32)[None, :]
    diagonal_flat = diagonal.reshape(loc_dev, 1, params * params)
    product = product + jnp.where(on_diagonal[:, :, None], diagonal_flat, 0.0)
    product = product.reshape(entries, params * params)
    product = jnp.concatenate([product, extra], axis=1)
    outgoing = jnp.take(product, ranking.reshape(devices, per_peer), axis=0, mode="clip")
    incoming = lax.all_to_all(outgoing, TILE_EXPO, split_axis=0, concat_axis=0, tiled=True)
    block_len = params * params
    incoming_tags = incoming[:, :, block_len].astype(jnp.int32)
    incoming_rhs = incoming[:, :, block_len + 1 :]
    receive_slots = (
        jnp.arange(pair_dev, dtype=jnp.int32)[:, None, None] == incoming_tags[None]
    ).astype(jnp.float32)
    pair_blocks = lax.dot_general(
        receive_slots, incoming[:, :, :block_len], (((1, 2), (0, 1)), ((), ())), precision=highest
    )
    reduced_rhs = jnp.sum(incoming_rhs.reshape(devices, -1, params), axis=0)
    return (pair_blocks, reduced_rhs)


def solution(mesh):
    split = Mesh(
        mesh.devices.reshape(4, 4, 2, mesh.shape["expo"]), ("tile_0", "tile_1", "tile_2", "expo")
    )
    placed = (
        P(None, "expo", TILE),
        P("expo", TILE),
        P("expo", TILE),
        P("expo", TILE),
        P(None, "expo", TILE),
        P(None, None, TILE),
        P(TILE),
        P(),
        P(),
        P(TILE, None),
        P(TILE, None, None),
    )
    return jax.shard_map(
        on_device,
        mesh=split,
        in_specs=placed,
        out_specs=(P(TILE_EXPO, None), P(TILE_EXPO, None)),
        check_vma=False,
    )
```

```python
import jax
import jax.numpy as jnp
from jax import lax
from jax.experimental import pallas as pl
from jax.experimental.pallas import tpu as pltpu
from jax.sharding import Mesh
from jax.sharding import PartitionSpec as P

DEG_X = 6
DEG_Y = 5
TILE = ("tile_0", "tile_1", "tile_2")
TILE_EXPO = ("tile_0", "tile_1", "tile_2", "expo")


highest = lax.Precision.HIGHEST
contract = (((1, 2), (1, 2)), ((), ()))


def turned_gather(arrays, axis, dims):
    turned = [jnp.moveaxis(a, dim, 0) for a, dim in zip(arrays, dims)]
    both = jnp.concatenate([t.reshape(len(t), -1) for t in turned], axis=1)
    filled, at, done = (lax.all_gather(both, axis, axis=0, tiled=True), 0, [])
    for t, dim in zip(turned, dims):
        piece = filled[:, at : at + t[0].size].reshape(-1, *t.shape[1:])
        done.append(jnp.moveaxis(piece, 0, dim))
        at += t[0].size
    return tuple(done)


def sum_in_order(tiles, axes, order):
    inside = tiles.shape[1:]
    tiles = tiles.reshape(*(lax.axis_size(a) for a in axes), *inside)
    tiles = jnp.moveaxis(tiles, order, range(len(axes))).reshape(-1, *inside)
    for k in order:
        tiles = lax.psum_scatter(tiles, axes[k], scatter_dimension=0, tiled=True)
    return tiles[0]


def split_up(array, dim, length):
    before, after = (array.shape[:dim], array.shape[dim + 1 :])
    return jnp.moveaxis(array.reshape(*before, length, -1, *after), dim, 0)


def scatter_axes(array, axes, order, dim):
    length = lax.axis_size(axes)
    return sum_in_order(split_up(array, dim, length), axes, order)


def chebyshev(values, degree):
    series = [jnp.ones_like(values), values]
    for degree_at in range(2, degree):
        series.append(2.0 * values * series[-1] - series[-2])
    return series[:degree]


def focal_weight(pixel_uv, ccd_index, observed, obs_weight, live_rows, ccd_center):
    ccd_total = ccd_center.shape[1]
    picked = (
        ccd_index[None, :, :] == jnp.arange(ccd_total, dtype=jnp.int32)[:, None, None]
    ).astype(jnp.float32)
    centre = jnp.sum(ccd_center[:, :, None, None] * picked[None], axis=1)
    focal = 0.75 * centre + 0.25 * pixel_uv
    star_rows = ccd_index.shape[1]
    alive = (jnp.arange(star_rows, dtype=jnp.int32)[None, :] < live_rows).astype(jnp.float32)
    live_weight = obs_weight * observed.astype(jnp.float32) * alive
    return (focal, live_weight)


def basis_of(focal):
    along_first = chebyshev(focal[0], DEG_X)
    along_second = chebyshev(focal[1], DEG_Y)
    return jnp.stack(
        [first_term * second_term for first_term in along_first for second_term in along_second],
        axis=1,
    )


def jacobian_of(geometry):
    shift_time = geometry[0]
    factor_first = geometry[1]
    factor_second = geometry[2]
    unit_row = jnp.ones_like(shift_time)
    zero_row = jnp.zeros_like(shift_time)
    return jnp.stack(
        [
            jnp.stack([unit_row, zero_row, shift_time, zero_row, factor_first], axis=-1),
            jnp.stack([zero_row, unit_row, zero_row, shift_time, factor_second], axis=-1),
        ],
        axis=1,
    )


def geometry_of(exp_geom, exposure_ids):
    picked = (
        jnp.arange(exp_geom.shape[1], dtype=jnp.int32)[:, None] == exposure_ids[None, :]
    ).astype(jnp.float32)
    return (jnp.sum(exp_geom[:, :, None] * picked[None], axis=1), picked)


def coupling_matrix(live_weight, basis, jacobian):
    full = (
        live_weight[:, None, None, None, :]
        * jacobian[:, :, None, :, None]
        * basis[:, None, :, None, :]
    )
    return full.astype(jnp.bfloat16).reshape(basis.shape[0] * 2 * basis.shape[1], 5, basis.shape[2])


def negated_scaled(coupling, inverse):
    return (
        -jnp.einsum("xis,jis->xjs", coupling.astype(jnp.float32), inverse, precision=highest)
    ).astype(jnp.bfloat16)


def diagonal_blocks(live_weight, basis):
    weighted = live_weight[:, None, :] * basis
    gram = jnp.einsum("ams,ans->amn", weighted, basis, precision=highest)
    pair_eye = jnp.eye(2, dtype=jnp.float32)
    full = jnp.einsum("cd,amn->acmdn", pair_eye, gram, precision=highest)
    return (full.reshape(gram.shape[0], 2 * gram.shape[1], 2 * gram.shape[1]), weighted)


def gradient_terms(jacobian, live_weight, obs_resid):
    return jnp.einsum("aci,as,cas->is", jacobian, live_weight, obs_resid, precision=highest)


def local_rhs(weighted, jacobian, obs_resid, solved):
    correction = jnp.einsum("aci,is->cas", jacobian, solved, precision=highest)
    result = jnp.einsum("ams,cas->acm", weighted, obs_resid - correction, precision=highest)
    return result.reshape(weighted.shape[0], 2 * weighted.shape[1])


def star_product(former, latter):
    return lax.dot_general(former, latter, contract, preferred_element_type=jnp.float32)


LANES = 128


def schur_kernel(xa, ya, wa, wda, wfa, wga, xo, yo, wo, wdo, wfo, wgo, si, out, rhs0, rhs1, lhs0, lhs1):
    step = pl.program_id(0)
    bf = jnp.bfloat16
    f32 = jnp.float32
    n_all = xa.shape[0]
    n_own = xo.shape[0]
    terms = DEG_X * DEG_Y

    @pl.when(step == 0)
    def _():
        out[...] = jnp.zeros_like(out)

    tx = chebyshev(xa[...], DEG_X)
    ty = chebyshev(ya[...], DEG_Y)
    txo = chebyshev(xo[...], DEG_X)
    tyo = chebyshev(yo[...], DEG_Y)
    w, wd, wf, wg = wa[...], wda[...], wfa[...], wga[...]
    w_o, wd_o, wf_o, wg_o = wo[...], wdo[...], wfo[...], wgo[...]
    inv = [[si[pl.ds(j * 5 + i, 1), :] for i in range(5)] for j in range(5)]
    for p in range(DEG_X):
        for q in range(DEG_Y):
            m = p * DEG_Y + q
            b = tx[p] * ty[q]
            cp = (w * b).astype(bf).astype(f32)
            cq = (wd * b).astype(bf).astype(f32)
            cr = (wf * b).astype(bf).astype(f32)
            cs = (wg * b).astype(bf).astype(f32)
            for d, (k0, k1, last) in enumerate(((0, 2, cr), (1, 3, cs))):
                rows = pl.ds((d * terms + m) * n_all, n_all)
                sc = [(-(inv[j][k0] * cp + inv[j][k1] * cq + inv[j][4] * last)).astype(bf) for j in range(5)]
                for t, j in enumerate((0, 2, 4)):
                    rhs0[rows, pl.ds(t * LANES, LANES)] = sc[j]
                for t, j in enumerate((1, 3, 4)):
                    rhs1[rows, pl.ds(t * LANES, LANES)] = sc[j]
            bo = txo[p] * tyo[q]
            po = (w_o * bo).astype(bf).astype(f32)
            qo = (wd_o * bo).astype(bf).astype(f32)
            own_rows = pl.ds(m * n_own, n_own)
            lhs0[own_rows, pl.ds(0, LANES)] = po
            lhs0[own_rows, pl.ds(LANES, LANES)] = qo
            lhs0[own_rows, pl.ds(2 * LANES, LANES)] = (wf_o * bo).astype(bf).astype(f32)
            lhs1[own_rows, pl.ds(0, LANES)] = po
            lhs1[own_rows, pl.ds(LANES, LANES)] = qo
            lhs1[own_rows, pl.ds(2 * LANES, LANES)] = (wg_o * bo).astype(bf).astype(f32)
    out[0] += lax.dot_general(lhs0[...].astype(bf), rhs0[...], (((1,), (1,)), ((), ())), preferred_element_type=f32)
    out[1] += lax.dot_general(lhs1[...].astype(bf), rhs1[...], (((1,), (1,)), ((), ())), preferred_element_type=f32)


def schur_product(all_x, all_y, all_w, all_wd, all_wf, all_wg, own_x, own_y, own_w, own_wd, own_wf, own_wg, inverse):
    n_all, stars = all_x.shape
    n_own = own_x.shape[0]
    terms = DEG_X * DEG_Y
    rows_all = 2 * terms * n_all
    rows_own = terms * n_own
    all_spec = pl.BlockSpec((n_all, LANES), lambda k: (0, k))
    own_spec = pl.BlockSpec((n_own, LANES), lambda k: (0, k))
    inv_spec = pl.BlockSpec((25, LANES), lambda k: (0, k))
    return pl.pallas_call(
        schur_kernel,
        out_shape=jax.ShapeDtypeStruct((2, rows_own, rows_all), jnp.float32),
        grid=(stars // LANES,),
        in_specs=[all_spec] * 6 + [own_spec] * 6 + [inv_spec],
        out_specs=pl.BlockSpec((2, rows_own, rows_all), lambda k: (0, 0, 0)),
        scratch_shapes=[
            pltpu.VMEM((rows_all, 3 * LANES), jnp.bfloat16),
            pltpu.VMEM((rows_all, 3 * LANES), jnp.bfloat16),
            pltpu.VMEM((rows_own, 3 * LANES), jnp.float32),
            pltpu.VMEM((rows_own, 3 * LANES), jnp.float32),
        ],
        compiler_params=pltpu.CompilerParams(dimension_semantics=("arbitrary",)),
    )(all_x, all_y, all_w, all_wd, all_wf, all_wg, own_x, own_y, own_w, own_wd, own_wf, own_wg, inverse)


def on_device(
    pixel_uv,
    ccd_index,
    observed,
    obs_weight,
    obs_resid,
    star_inverse,
    star_count,
    ccd_center,
    exp_geom,
    tile_exposures,
    pair_owner,
):
    expo_total = lax.axis_size("expo")
    tile_total = lax.axis_size(TILE)
    expo_rank = lax.axis_index("expo")
    loc_dev = ccd_index.shape[0]
    window = tile_exposures.shape[1]
    params = 2 * DEG_X * DEG_Y
    live_rows = star_count[0]
    exposure_ids = lax.dynamic_slice_in_dim(tile_exposures[0], expo_rank * loc_dev, loc_dev)
    geometry, picked = geometry_of(exp_geom, exposure_ids)
    focal, live_weight = focal_weight(
        pixel_uv, ccd_index, observed, obs_weight, live_rows, ccd_center
    )
    basis = basis_of(focal)
    jacobian = jacobian_of(geometry)
    diagonal, weighted = diagonal_blocks(live_weight, basis)
    own_rows = expo_rank * loc_dev + jnp.arange(loc_dev, dtype=jnp.int32)
    local_rows = jnp.arange(loc_dev, dtype=jnp.int32)
    all_focal, all_weight, all_resid = turned_gather(
        (focal, live_weight, obs_resid), "expo", (1, 0, 1)
    )
    all_geometry, all_picked = geometry_of(exp_geom, tile_exposures[0])
    all_jacobian = jacobian_of(all_geometry)
    all_x, all_y = all_focal[0], all_focal[1]
    own_x, own_y = focal[0], focal[1]
    products = schur_product(
        all_x, all_y, all_weight,
        all_weight * all_geometry[0][:, None], all_weight * all_geometry[1][:, None], all_weight * all_geometry[2][:, None],
        own_x, own_y, live_weight,
        live_weight * geometry[0][:, None], live_weight * geometry[1][:, None], live_weight * geometry[2][:, None],
        star_inverse.reshape(25, -1),
    )
    terms = DEG_X * DEG_Y
    product = products.reshape(2, terms, loc_dev, params, window)
    product = jnp.transpose(product, (2, 4, 0, 1, 3)).reshape(loc_dev, window, params * params)
    on_diagonal = own_rows[:, None] == jnp.arange(window, dtype=jnp.int32)[None, :]
    diagonal_flat = diagonal.reshape(loc_dev, 1, params * params)
    product = product + jnp.where(on_diagonal[:, :, None], diagonal_flat, 0.0)
    product = product.reshape(loc_dev * window, params * params)
    block_scale = jnp.max(jnp.abs(product), axis=1, keepdims=True)
    block_scale = jnp.where(block_scale > 0.0, block_scale, 1.0)
    product = (product * (1.0 / block_scale)).astype(jnp.float16)
    owners = lax.dynamic_slice_in_dim(pair_owner[0], expo_rank * loc_dev, loc_dev, 0)
    gradient = gradient_terms(all_jacobian, all_weight, all_resid)
    solved = jnp.einsum("jis,is->js", star_inverse, gradient, precision=highest)
    rhs_local = local_rhs(weighted, jacobian, obs_resid, solved)
    devices = tile_total * expo_total
    spread = jnp.dot(picked, rhs_local, precision=highest).reshape(devices, -1)
    pair_dev = 3 * (window // 2) * (window // 2) // expo_total
    flat_owner = owners.reshape(-1)
    target = flat_owner // pair_dev
    ranking = jnp.argsort(target, stable=True)
    per_peer = flat_owner.shape[0] // devices
    outgoing = jnp.take(product, ranking.reshape(devices, per_peer), axis=0, mode="clip")
    slot_tags = (flat_owner % pair_dev)[ranking].reshape(devices, per_peer).astype(jnp.float32)
    sent_scale = jnp.take(block_scale[:, 0], ranking, mode="clip").reshape(devices, per_peer)
    small = jnp.concatenate([spread, slot_tags, sent_scale], axis=1)
    incoming_blocks = lax.all_to_all(outgoing, TILE_EXPO, split_axis=0, concat_axis=0, tiled=True)
    incoming_small = lax.all_to_all(small, TILE_EXPO, split_axis=0, concat_axis=0, tiled=True)
    incoming_rhs = incoming_small[:, : spread.shape[1]]
    incoming_tags = incoming_small[:, spread.shape[1] : spread.shape[1] + per_peer].astype(jnp.int32)
    incoming_scale = incoming_small[:, spread.shape[1] + per_peer :]
    receive_slots = jnp.where(
        jnp.arange(pair_dev, dtype=jnp.int32)[:, None] == incoming_tags.reshape(1, -1),
        incoming_scale.reshape(1, -1),
        0.0,
    )
    incoming_blocks = incoming_blocks.astype(jnp.float32)
    receive_slots = receive_slots.reshape(pair_dev, devices, per_peer)
    pair_blocks = lax.dot_general(
        receive_slots, incoming_blocks, (((1, 2), (0, 1)), ((), ())), precision=highest
    )
    reduced_rhs = jnp.sum(incoming_rhs.reshape(devices, -1, params), axis=0)
    return (pair_blocks, reduced_rhs)


def solution(mesh):
    split = Mesh(
        mesh.devices.reshape(4, 4, 2, mesh.shape["expo"]), ("tile_0", "tile_1", "tile_2", "expo")
    )
    placed = (
        P(None, "expo", TILE),
        P("expo", TILE),
        P("expo", TILE),
        P("expo", TILE),
        P(None, "expo", TILE),
        P(None, None, TILE),
        P(TILE),
        P(),
        P(),
        P(TILE, None),
        P(TILE, None, None),
    )
    return jax.shard_map(
        on_device,
        mesh=split,
        in_specs=placed,
        out_specs=(P(TILE_EXPO, None), P(TILE_EXPO, None)),
        check_vma=False,
    )
```

```python
import jax
import jax.numpy as jnp
from jax import lax
from jax.experimental import pallas as pl
from jax.experimental.pallas import tpu as pltpu
from jax.sharding import Mesh
from jax.sharding import PartitionSpec as P

DEG_X = 6
DEG_Y = 5
TILE = ("tile_0", "tile_1", "tile_2")
TILE_EXPO = ("tile_0", "tile_1", "tile_2", "expo")


highest = lax.Precision.HIGHEST
contract = (((1, 2), (1, 2)), ((), ()))


def turned_gather(arrays, axis, dims):
    turned = [jnp.moveaxis(a, dim, 0) for a, dim in zip(arrays, dims)]
    both = jnp.concatenate([t.reshape(len(t), -1) for t in turned], axis=1)
    filled, at, done = (lax.all_gather(both, axis, axis=0, tiled=True), 0, [])
    for t, dim in zip(turned, dims):
        piece = filled[:, at : at + t[0].size].reshape(-1, *t.shape[1:])
        done.append(jnp.moveaxis(piece, 0, dim))
        at += t[0].size
    return tuple(done)


def sum_in_order(tiles, axes, order):
    inside = tiles.shape[1:]
    tiles = tiles.reshape(*(lax.axis_size(a) for a in axes), *inside)
    tiles = jnp.moveaxis(tiles, order, range(len(axes))).reshape(-1, *inside)
    for k in order:
        tiles = lax.psum_scatter(tiles, axes[k], scatter_dimension=0, tiled=True)
    return tiles[0]


def split_up(array, dim, length):
    before, after = (array.shape[:dim], array.shape[dim + 1 :])
    return jnp.moveaxis(array.reshape(*before, length, -1, *after), dim, 0)


def scatter_axes(array, axes, order, dim):
    length = lax.axis_size(axes)
    return sum_in_order(split_up(array, dim, length), axes, order)


def chebyshev(values, degree):
    series = [jnp.ones_like(values), values]
    for degree_at in range(2, degree):
        series.append(2.0 * values * series[-1] - series[-2])
    return series[:degree]


def focal_weight(pixel_uv, ccd_index, observed, obs_weight, live_rows, ccd_center):
    ccd_total = ccd_center.shape[1]
    picked = (
        ccd_index[None, :, :] == jnp.arange(ccd_total, dtype=jnp.int32)[:, None, None]
    ).astype(jnp.float32)
    centre = jnp.sum(ccd_center[:, :, None, None] * picked[None], axis=1)
    focal = 0.75 * centre + 0.25 * pixel_uv
    star_rows = ccd_index.shape[1]
    alive = (jnp.arange(star_rows, dtype=jnp.int32)[None, :] < live_rows).astype(jnp.float32)
    live_weight = obs_weight * observed.astype(jnp.float32) * alive
    return (focal, live_weight)


def basis_of(focal):
    along_first = chebyshev(focal[0], DEG_X)
    along_second = chebyshev(focal[1], DEG_Y)
    return jnp.stack(
        [first_term * second_term for first_term in along_first for second_term in along_second],
        axis=1,
    )


def jacobian_of(geometry):
    shift_time = geometry[0]
    factor_first = geometry[1]
    factor_second = geometry[2]
    unit_row = jnp.ones_like(shift_time)
    zero_row = jnp.zeros_like(shift_time)
    return jnp.stack(
        [
            jnp.stack([unit_row, zero_row, shift_time, zero_row, factor_first], axis=-1),
            jnp.stack([zero_row, unit_row, zero_row, shift_time, factor_second], axis=-1),
        ],
        axis=1,
    )


def geometry_of(exp_geom, exposure_ids):
    picked = (
        jnp.arange(exp_geom.shape[1], dtype=jnp.int32)[:, None] == exposure_ids[None, :]
    ).astype(jnp.float32)
    return (jnp.sum(exp_geom[:, :, None] * picked[None], axis=1), picked)


def coupling_matrix(live_weight, basis, jacobian):
    full = (
        live_weight[:, None, None, None, :]
        * jacobian[:, :, None, :, None]
        * basis[:, None, :, None, :]
    )
    return full.astype(jnp.bfloat16).reshape(basis.shape[0] * 2 * basis.shape[1], 5, basis.shape[2])


def negated_scaled(coupling, inverse):
    return (
        -jnp.einsum("xis,jis->xjs", coupling.astype(jnp.float32), inverse, precision=highest)
    ).astype(jnp.bfloat16)


def diagonal_blocks(live_weight, basis):
    weighted = live_weight[:, None, :] * basis
    gram = jnp.einsum("ams,ans->amn", weighted, basis, precision=highest)
    pair_eye = jnp.eye(2, dtype=jnp.float32)
    full = jnp.einsum("cd,amn->acmdn", pair_eye, gram, precision=highest)
    return (full.reshape(gram.shape[0], 2 * gram.shape[1], 2 * gram.shape[1]), weighted)


def gradient_terms(jacobian, live_weight, obs_resid):
    return jnp.einsum("aci,as,cas->is", jacobian, live_weight, obs_resid, precision=highest)


def local_rhs(weighted, jacobian, obs_resid, solved):
    correction = jnp.einsum("aci,is->cas", jacobian, solved, precision=highest)
    result = jnp.einsum("ams,cas->acm", weighted, obs_resid - correction, precision=highest)
    return result.reshape(weighted.shape[0], 2 * weighted.shape[1])


def star_product(former, latter):
    return lax.dot_general(former, latter, contract, preferred_element_type=jnp.float32)


LANES = 128


def schur_kernel(xa, ya, wa, wda, wfa, wga, xo, yo, wo, wdo, wfo, wgo, si, out, peak, rhs0, rhs1, lhs0, lhs1):
    step = pl.program_id(0)
    bf = jnp.bfloat16
    f32 = jnp.float32
    n_all = xa.shape[0]
    n_own = xo.shape[0]
    terms = DEG_X * DEG_Y

    @pl.when(step == 0)
    def _():
        out[...] = jnp.zeros_like(out)

    tx = chebyshev(xa[...], DEG_X)
    ty = chebyshev(ya[...], DEG_Y)
    txo = chebyshev(xo[...], DEG_X)
    tyo = chebyshev(yo[...], DEG_Y)
    w, wd, wf, wg = wa[...], wda[...], wfa[...], wga[...]
    w_o, wd_o, wf_o, wg_o = wo[...], wdo[...], wfo[...], wgo[...]
    inv = [[si[pl.ds(j * 5 + i, 1), :] for i in range(5)] for j in range(5)]
    for p in range(DEG_X):
        for q in range(DEG_Y):
            m = p * DEG_Y + q
            b = tx[p] * ty[q]
            cp = (w * b).astype(bf).astype(f32)
            cq = (wd * b).astype(bf).astype(f32)
            cr = (wf * b).astype(bf).astype(f32)
            cs = (wg * b).astype(bf).astype(f32)
            for d, (k0, k1, last) in enumerate(((0, 2, cr), (1, 3, cs))):
                rows = pl.ds((d * terms + m) * n_all, n_all)
                sc = [(-(inv[j][k0] * cp + inv[j][k1] * cq + inv[j][4] * last)).astype(bf) for j in range(5)]
                for t, j in enumerate((0, 2, 4)):
                    rhs0[rows, pl.ds(t * LANES, LANES)] = sc[j]
                for t, j in enumerate((1, 3, 4)):
                    rhs1[rows, pl.ds(t * LANES, LANES)] = sc[j]
            bo = txo[p] * tyo[q]
            po = (w_o * bo).astype(bf).astype(f32)
            qo = (wd_o * bo).astype(bf).astype(f32)
            own_rows = pl.ds(m * n_own, n_own)
            lhs0[own_rows, pl.ds(0, LANES)] = po
            lhs0[own_rows, pl.ds(LANES, LANES)] = qo
            lhs0[own_rows, pl.ds(2 * LANES, LANES)] = (wf_o * bo).astype(bf).astype(f32)
            lhs1[own_rows, pl.ds(0, LANES)] = po
            lhs1[own_rows, pl.ds(LANES, LANES)] = qo
            lhs1[own_rows, pl.ds(2 * LANES, LANES)] = (wg_o * bo).astype(bf).astype(f32)
    out[0] += lax.dot_general(lhs0[...].astype(bf), rhs0[...], (((1,), (1,)), ((), ())), preferred_element_type=f32)
    out[1] += lax.dot_general(lhs1[...].astype(bf), rhs1[...], (((1,), (1,)), ((), ())), preferred_element_type=f32)

    @pl.when(step == pl.num_programs(0) - 1)
    def _():
        top = jnp.maximum(jnp.max(jnp.abs(out[0])), jnp.max(jnp.abs(out[1])))
        peak[...] = jnp.full(peak.shape, top, f32)


def schur_product(all_x, all_y, all_w, all_wd, all_wf, all_wg, own_x, own_y, own_w, own_wd, own_wf, own_wg, inverse):
    n_all, stars = all_x.shape
    n_own = own_x.shape[0]
    terms = DEG_X * DEG_Y
    rows_all = 2 * terms * n_all
    rows_own = terms * n_own
    all_spec = pl.BlockSpec((n_all, LANES), lambda k: (0, k))
    own_spec = pl.BlockSpec((n_own, LANES), lambda k: (0, k))
    inv_spec = pl.BlockSpec((25, LANES), lambda k: (0, k))
    return pl.pallas_call(
        schur_kernel,
        out_shape=(
            jax.ShapeDtypeStruct((2, rows_own, rows_all), jnp.float32),
            jax.ShapeDtypeStruct((8, LANES), jnp.float32),
        ),
        grid=(stars // LANES,),
        in_specs=[all_spec] * 6 + [own_spec] * 6 + [inv_spec],
        out_specs=(
            pl.BlockSpec((2, rows_own, rows_all), lambda k: (0, 0, 0)),
            pl.BlockSpec((8, LANES), lambda k: (0, 0)),
        ),
        scratch_shapes=[
            pltpu.VMEM((rows_all, 3 * LANES), jnp.bfloat16),
            pltpu.VMEM((rows_all, 3 * LANES), jnp.bfloat16),
            pltpu.VMEM((rows_own, 3 * LANES), jnp.float32),
            pltpu.VMEM((rows_own, 3 * LANES), jnp.float32),
        ],
        compiler_params=pltpu.CompilerParams(dimension_semantics=("arbitrary",)),
    )(all_x, all_y, all_w, all_wd, all_wf, all_wg, own_x, own_y, own_w, own_wd, own_wf, own_wg, inverse)


def on_device(
    pixel_uv,
    ccd_index,
    observed,
    obs_weight,
    obs_resid,
    star_inverse,
    star_count,
    ccd_center,
    exp_geom,
    tile_exposures,
    pair_owner,
):
    expo_total = lax.axis_size("expo")
    tile_total = lax.axis_size(TILE)
    expo_rank = lax.axis_index("expo")
    loc_dev = ccd_index.shape[0]
    window = tile_exposures.shape[1]
    params = 2 * DEG_X * DEG_Y
    live_rows = star_count[0]
    exposure_ids = lax.dynamic_slice_in_dim(tile_exposures[0], expo_rank * loc_dev, loc_dev)
    geometry, picked = geometry_of(exp_geom, exposure_ids)
    focal, live_weight = focal_weight(
        pixel_uv, ccd_index, observed, obs_weight, live_rows, ccd_center
    )
    basis = basis_of(focal)
    jacobian = jacobian_of(geometry)
    diagonal, weighted = diagonal_blocks(live_weight, basis)
    own_rows = expo_rank * loc_dev + jnp.arange(loc_dev, dtype=jnp.int32)
    local_rows = jnp.arange(loc_dev, dtype=jnp.int32)
    all_focal, all_weight, all_resid = turned_gather(
        (focal, live_weight, obs_resid), "expo", (1, 0, 1)
    )
    all_geometry, all_picked = geometry_of(exp_geom, tile_exposures[0])
    all_jacobian = jacobian_of(all_geometry)
    all_x, all_y = all_focal[0], all_focal[1]
    own_x, own_y = focal[0], focal[1]
    products, peak = schur_product(
        all_x, all_y, all_weight,
        all_weight * all_geometry[0][:, None], all_weight * all_geometry[1][:, None], all_weight * all_geometry[2][:, None],
        own_x, own_y, live_weight,
        live_weight * geometry[0][:, None], live_weight * geometry[1][:, None], live_weight * geometry[2][:, None],
        star_inverse.reshape(25, -1),
    )
    terms = DEG_X * DEG_Y
    product = products.reshape(2, terms, loc_dev, params, window)
    product = jnp.transpose(product, (2, 4, 0, 1, 3)).reshape(loc_dev, window, params * params)
    on_diagonal = own_rows[:, None] == jnp.arange(window, dtype=jnp.int32)[None, :]
    diagonal_flat = diagonal.reshape(loc_dev, 1, params * params)
    product = product + jnp.where(on_diagonal[:, :, None], diagonal_flat, 0.0)
    product = product.reshape(loc_dev * window, params * params)
    bound = peak[0, 0] + jnp.max(jnp.abs(diagonal))
    bound = jnp.where(bound > 0.0, bound, 1.0)
    product = (product * (1.0 / bound)).astype(jnp.float16)
    owners = lax.dynamic_slice_in_dim(pair_owner[0], expo_rank * loc_dev, loc_dev, 0)
    gradient = gradient_terms(all_jacobian, all_weight, all_resid)
    solved = jnp.einsum("jis,is->js", star_inverse, gradient, precision=highest)
    rhs_local = local_rhs(weighted, jacobian, obs_resid, solved)
    devices = tile_total * expo_total
    spread = jnp.dot(picked, rhs_local, precision=highest).reshape(devices, -1)
    pair_dev = 3 * (window // 2) * (window // 2) // expo_total
    flat_owner = owners.reshape(-1)
    target = flat_owner // pair_dev
    ranking = jnp.argsort(target, stable=True)
    per_peer = flat_owner.shape[0] // devices
    outgoing = jnp.take(product, ranking.reshape(devices, per_peer), axis=0, mode="clip")
    slot_tags = (flat_owner % pair_dev)[ranking].reshape(devices, per_peer).astype(jnp.float32)
    sent_scale = jnp.full((devices, 1), bound, jnp.float32)
    small = jnp.concatenate([spread, slot_tags, sent_scale], axis=1)
    incoming_blocks = lax.all_to_all(outgoing, TILE_EXPO, split_axis=0, concat_axis=0, tiled=True)
    incoming_small = lax.all_to_all(small, TILE_EXPO, split_axis=0, concat_axis=0, tiled=True)
    incoming_rhs = incoming_small[:, : spread.shape[1]]
    incoming_tags = incoming_small[:, spread.shape[1] : spread.shape[1] + per_peer].astype(jnp.int32)
    incoming_scale = jnp.broadcast_to(incoming_small[:, spread.shape[1] + per_peer :], (devices, per_peer))
    receive_slots = jnp.where(
        jnp.arange(pair_dev, dtype=jnp.int32)[:, None] == incoming_tags.reshape(1, -1),
        incoming_scale.reshape(1, -1),
        0.0,
    )
    incoming_blocks = incoming_blocks.astype(jnp.float32)
    receive_slots = receive_slots.reshape(pair_dev, devices, per_peer)
    pair_blocks = lax.dot_general(
        receive_slots, incoming_blocks, (((1, 2), (0, 1)), ((), ())), precision=highest
    )
    reduced_rhs = jnp.sum(incoming_rhs.reshape(devices, -1, params), axis=0)
    return (pair_blocks, reduced_rhs)


def solution(mesh):
    split = Mesh(
        mesh.devices.reshape(4, 4, 2, mesh.shape["expo"]), ("tile_0", "tile_1", "tile_2", "expo")
    )
    placed = (
        P(None, "expo", TILE),
        P("expo", TILE),
        P("expo", TILE),
        P("expo", TILE),
        P(None, "expo", TILE),
        P(None, None, TILE),
        P(TILE),
        P(),
        P(),
        P(TILE, None),
        P(TILE, None, None),
    )
    return jax.shard_map(
        on_device,
        mesh=split,
        in_specs=placed,
        out_specs=(P(TILE_EXPO, None), P(TILE_EXPO, None)),
        check_vma=False,
    )
```

```python
import jax
import jax.numpy as jnp
from jax import lax
from jax.experimental import pallas as pl
from jax.experimental.pallas import tpu as pltpu
from jax.sharding import Mesh
from jax.sharding import PartitionSpec as P

DEG_X = 6
DEG_Y = 5
TILE = ("tile_0", "tile_1", "tile_2")
TILE_EXPO = ("tile_0", "tile_1", "tile_2", "expo")


highest = lax.Precision.HIGHEST
contract = (((1, 2), (1, 2)), ((), ()))


def turned_gather(arrays, axis, dims):
    turned = [jnp.moveaxis(a, dim, 0) for a, dim in zip(arrays, dims)]
    both = jnp.concatenate([t.reshape(len(t), -1) for t in turned], axis=1)
    filled, at, done = (lax.all_gather(both, axis, axis=0, tiled=True), 0, [])
    for t, dim in zip(turned, dims):
        piece = filled[:, at : at + t[0].size].reshape(-1, *t.shape[1:])
        done.append(jnp.moveaxis(piece, 0, dim))
        at += t[0].size
    return tuple(done)


def sum_in_order(tiles, axes, order):
    inside = tiles.shape[1:]
    tiles = tiles.reshape(*(lax.axis_size(a) for a in axes), *inside)
    tiles = jnp.moveaxis(tiles, order, range(len(axes))).reshape(-1, *inside)
    for k in order:
        tiles = lax.psum_scatter(tiles, axes[k], scatter_dimension=0, tiled=True)
    return tiles[0]


def split_up(array, dim, length):
    before, after = (array.shape[:dim], array.shape[dim + 1 :])
    return jnp.moveaxis(array.reshape(*before, length, -1, *after), dim, 0)


def scatter_axes(array, axes, order, dim):
    length = lax.axis_size(axes)
    return sum_in_order(split_up(array, dim, length), axes, order)


def chebyshev(values, degree):
    series = [jnp.ones_like(values), values]
    for degree_at in range(2, degree):
        series.append(2.0 * values * series[-1] - series[-2])
    return series[:degree]


def focal_weight(pixel_uv, ccd_index, observed, obs_weight, live_rows, ccd_center):
    ccd_total = ccd_center.shape[1]
    picked = (
        ccd_index[None, :, :] == jnp.arange(ccd_total, dtype=jnp.int32)[:, None, None]
    ).astype(jnp.float32)
    centre = jnp.sum(ccd_center[:, :, None, None] * picked[None], axis=1)
    focal = 0.75 * centre + 0.25 * pixel_uv
    star_rows = ccd_index.shape[1]
    alive = (jnp.arange(star_rows, dtype=jnp.int32)[None, :] < live_rows).astype(jnp.float32)
    live_weight = obs_weight * observed.astype(jnp.float32) * alive
    return (focal, live_weight)


def basis_of(focal):
    along_first = chebyshev(focal[0], DEG_X)
    along_second = chebyshev(focal[1], DEG_Y)
    return jnp.stack(
        [first_term * second_term for first_term in along_first for second_term in along_second],
        axis=1,
    )


def jacobian_of(geometry):
    shift_time = geometry[0]
    factor_first = geometry[1]
    factor_second = geometry[2]
    unit_row = jnp.ones_like(shift_time)
    zero_row = jnp.zeros_like(shift_time)
    return jnp.stack(
        [
            jnp.stack([unit_row, zero_row, shift_time, zero_row, factor_first], axis=-1),
            jnp.stack([zero_row, unit_row, zero_row, shift_time, factor_second], axis=-1),
        ],
        axis=1,
    )


def geometry_of(exp_geom, exposure_ids):
    picked = (
        jnp.arange(exp_geom.shape[1], dtype=jnp.int32)[:, None] == exposure_ids[None, :]
    ).astype(jnp.float32)
    return (jnp.sum(exp_geom[:, :, None] * picked[None], axis=1), picked)


def coupling_matrix(live_weight, basis, jacobian):
    full = (
        live_weight[:, None, None, None, :]
        * jacobian[:, :, None, :, None]
        * basis[:, None, :, None, :]
    )
    return full.astype(jnp.bfloat16).reshape(basis.shape[0] * 2 * basis.shape[1], 5, basis.shape[2])


def negated_scaled(coupling, inverse):
    return (
        -jnp.einsum("xis,jis->xjs", coupling.astype(jnp.float32), inverse, precision=highest)
    ).astype(jnp.bfloat16)


def diagonal_blocks(live_weight, basis):
    weighted = live_weight[:, None, :] * basis
    gram = jnp.einsum("ams,ans->amn", weighted, basis, precision=highest)
    pair_eye = jnp.eye(2, dtype=jnp.float32)
    full = jnp.einsum("cd,amn->acmdn", pair_eye, gram, precision=highest)
    return (full.reshape(gram.shape[0], 2 * gram.shape[1], 2 * gram.shape[1]), weighted)


def gradient_terms(jacobian, live_weight, obs_resid):
    return jnp.einsum("aci,as,cas->is", jacobian, live_weight, obs_resid, precision=highest)


def local_rhs(weighted, jacobian, obs_resid, solved):
    correction = jnp.einsum("aci,is->cas", jacobian, solved, precision=highest)
    result = jnp.einsum("ams,cas->acm", weighted, obs_resid - correction, precision=highest)
    return result.reshape(weighted.shape[0], 2 * weighted.shape[1])


def star_product(former, latter):
    return lax.dot_general(former, latter, contract, preferred_element_type=jnp.float32)


LANES = 128


def schur_kernel(xa, ya, wa, wda, wfa, wga, xo, yo, wo, wdo, wfo, wgo, si, out, peak, rhs0, rhs1, lhs0, lhs1):
    step = pl.program_id(0)
    bf = jnp.bfloat16
    f32 = jnp.float32
    n_all = xa.shape[0]
    n_own = xo.shape[0]
    terms = DEG_X * DEG_Y

    @pl.when(step == 0)
    def _():
        out[...] = jnp.zeros_like(out)

    tx = chebyshev(xa[...], DEG_X)
    ty = chebyshev(ya[...], DEG_Y)
    txo = chebyshev(xo[...], DEG_X)
    tyo = chebyshev(yo[...], DEG_Y)
    w, wd, wf, wg = wa[...], wda[...], wfa[...], wga[...]
    w_o, wd_o, wf_o, wg_o = wo[...], wdo[...], wfo[...], wgo[...]
    inv = [[si[pl.ds(j * 5 + i, 1), :] for i in range(5)] for j in range(5)]
    for p in range(DEG_X):
        for q in range(DEG_Y):
            m = p * DEG_Y + q
            b = tx[p] * ty[q]
            cp = (w * b).astype(bf).astype(f32)
            cq = (wd * b).astype(bf).astype(f32)
            cr = (wf * b).astype(bf).astype(f32)
            cs = (wg * b).astype(bf).astype(f32)
            for d, (k0, k1, last) in enumerate(((0, 2, cr), (1, 3, cs))):
                rows = pl.ds((d * terms + m) * n_all, n_all)
                sc = [(-(inv[j][k0] * cp + inv[j][k1] * cq + inv[j][4] * last)).astype(bf) for j in range(5)]
                for t, j in enumerate((0, 2, 4)):
                    rhs0[rows, pl.ds(t * LANES, LANES)] = sc[j]
                for t, j in enumerate((1, 3, 4)):
                    rhs1[rows, pl.ds(t * LANES, LANES)] = sc[j]
            bo = txo[p] * tyo[q]
            po = (w_o * bo).astype(bf).astype(f32)
            qo = (wd_o * bo).astype(bf).astype(f32)
            own_rows = pl.ds(m * n_own, n_own)
            lhs0[own_rows, pl.ds(0, LANES)] = po
            lhs0[own_rows, pl.ds(LANES, LANES)] = qo
            lhs0[own_rows, pl.ds(2 * LANES, LANES)] = (wf_o * bo).astype(bf).astype(f32)
            lhs1[own_rows, pl.ds(0, LANES)] = po
            lhs1[own_rows, pl.ds(LANES, LANES)] = qo
            lhs1[own_rows, pl.ds(2 * LANES, LANES)] = (wg_o * bo).astype(bf).astype(f32)
    out[0] += lax.dot_general(lhs0[...].astype(bf), rhs0[...], (((1,), (1,)), ((), ())), preferred_element_type=f32)
    out[1] += lax.dot_general(lhs1[...].astype(bf), rhs1[...], (((1,), (1,)), ((), ())), preferred_element_type=f32)

    @pl.when(step == pl.num_programs(0) - 1)
    def _():
        top = jnp.maximum(jnp.max(jnp.abs(out[0])), jnp.max(jnp.abs(out[1])))
        peak[...] = jnp.full(peak.shape, top, f32)


def schur_product(all_x, all_y, all_w, all_wd, all_wf, all_wg, own_x, own_y, own_w, own_wd, own_wf, own_wg, inverse):
    n_all, stars = all_x.shape
    n_own = own_x.shape[0]
    terms = DEG_X * DEG_Y
    rows_all = 2 * terms * n_all
    rows_own = terms * n_own
    all_spec = pl.BlockSpec((n_all, LANES), lambda k: (0, k))
    own_spec = pl.BlockSpec((n_own, LANES), lambda k: (0, k))
    inv_spec = pl.BlockSpec((25, LANES), lambda k: (0, k))
    return pl.pallas_call(
        schur_kernel,
        out_shape=(
            jax.ShapeDtypeStruct((2, rows_own, rows_all), jnp.float32),
            jax.ShapeDtypeStruct((8, LANES), jnp.float32),
        ),
        grid=(stars // LANES,),
        in_specs=[all_spec] * 6 + [own_spec] * 6 + [inv_spec],
        out_specs=(
            pl.BlockSpec((2, rows_own, rows_all), lambda k: (0, 0, 0)),
            pl.BlockSpec((8, LANES), lambda k: (0, 0)),
        ),
        scratch_shapes=[
            pltpu.VMEM((rows_all, 3 * LANES), jnp.bfloat16),
            pltpu.VMEM((rows_all, 3 * LANES), jnp.bfloat16),
            pltpu.VMEM((rows_own, 3 * LANES), jnp.float32),
            pltpu.VMEM((rows_own, 3 * LANES), jnp.float32),
        ],
        compiler_params=pltpu.CompilerParams(dimension_semantics=("arbitrary",)),
    )(all_x, all_y, all_w, all_wd, all_wf, all_wg, own_x, own_y, own_w, own_wd, own_wf, own_wg, inverse)


def on_device(
    pixel_uv,
    ccd_index,
    observed,
    obs_weight,
    obs_resid,
    star_inverse,
    star_count,
    ccd_center,
    exp_geom,
    tile_exposures,
    pair_owner,
):
    expo_total = lax.axis_size("expo")
    tile_total = lax.axis_size(TILE)
    expo_rank = lax.axis_index("expo")
    loc_dev = ccd_index.shape[0]
    window = tile_exposures.shape[1]
    params = 2 * DEG_X * DEG_Y
    live_rows = star_count[0]
    exposure_ids = lax.dynamic_slice_in_dim(tile_exposures[0], expo_rank * loc_dev, loc_dev)
    geometry, picked = geometry_of(exp_geom, exposure_ids)
    focal, live_weight = focal_weight(
        pixel_uv, ccd_index, observed, obs_weight, live_rows, ccd_center
    )
    basis = basis_of(focal)
    jacobian = jacobian_of(geometry)
    diagonal, weighted = diagonal_blocks(live_weight, basis)
    own_rows = expo_rank * loc_dev + jnp.arange(loc_dev, dtype=jnp.int32)
    local_rows = jnp.arange(loc_dev, dtype=jnp.int32)
    all_focal, all_weight, all_resid = turned_gather(
        (focal, live_weight, obs_resid), "expo", (1, 0, 1)
    )
    all_geometry, all_picked = geometry_of(exp_geom, tile_exposures[0])
    all_jacobian = jacobian_of(all_geometry)
    all_x, all_y = all_focal[0], all_focal[1]
    own_x, own_y = focal[0], focal[1]
    products, peak = schur_product(
        all_x, all_y, all_weight,
        all_weight * all_geometry[0][:, None], all_weight * all_geometry[1][:, None], all_weight * all_geometry[2][:, None],
        own_x, own_y, live_weight,
        live_weight * geometry[0][:, None], live_weight * geometry[1][:, None], live_weight * geometry[2][:, None],
        star_inverse.reshape(25, -1),
    )
    terms = DEG_X * DEG_Y
    owners = lax.dynamic_slice_in_dim(pair_owner[0], expo_rank * loc_dev, loc_dev, 0)
    pair_dev = 3 * (window // 2) * (window // 2) // expo_total
    flat_owner = owners.reshape(-1)
    entries = flat_owner.shape[0]
    product = products.reshape(2, terms, loc_dev, params, window)
    product = jnp.transpose(product, (2, 4, 0, 1, 3)).reshape(loc_dev, window, params * params)
    on_diagonal = own_rows[:, None] == jnp.arange(window, dtype=jnp.int32)[None, :]
    diagonal_flat = diagonal.reshape(loc_dev, 1, params * params)
    product = product + jnp.where(on_diagonal[:, :, None], diagonal_flat, 0.0)
    product = product.reshape(loc_dev * window, params * params)
    bound = peak[0, 0] + jnp.max(jnp.abs(diagonal))
    bound = jnp.where(bound > 0.0, bound, 1.0)
    octave = jnp.ceil(jnp.log2(bound))
    octave = octave + jnp.where(jnp.exp2(octave) < bound, 1.0, 0.0)
    product = product * (1.0 / jnp.exp2(octave))
    slot_tags = (flat_owner % pair_dev).astype(jnp.float32)
    product = jnp.concatenate(
        [product, slot_tags[:, None], jnp.broadcast_to(octave, (entries, 1))], axis=1
    ).astype(jnp.float16)
    gradient = gradient_terms(all_jacobian, all_weight, all_resid)
    solved = jnp.einsum("jis,is->js", star_inverse, gradient, precision=highest)
    rhs_local = local_rhs(weighted, jacobian, obs_resid, solved)
    devices = tile_total * expo_total
    spread = jnp.dot(picked, rhs_local, precision=highest)
    reduced_rhs = lax.psum_scatter(spread, TILE_EXPO, scatter_dimension=0, tiled=True)
    target = flat_owner // pair_dev
    ranking = jnp.argsort(target, stable=True)
    per_peer = entries // devices
    outgoing = jnp.take(product, ranking.reshape(devices, per_peer), axis=0, mode="clip")
    incoming = lax.all_to_all(outgoing, TILE_EXPO, split_axis=0, concat_axis=0, tiled=True)
    block_len = params * params
    incoming_tags = incoming[:, :, block_len].astype(jnp.int32)
    incoming_scale = jnp.exp2(incoming[:, :, block_len + 1].astype(jnp.float32))
    receive_slots = jnp.where(
        jnp.arange(pair_dev, dtype=jnp.int32)[:, None, None] == incoming_tags[None],
        incoming_scale[None],
        0.0,
    )
    pair_blocks = lax.dot_general(
        receive_slots, incoming[:, :, :block_len].astype(jnp.float32), (((1, 2), (0, 1)), ((), ())), precision=highest
    )
    return (pair_blocks, reduced_rhs)


def solution(mesh):
    split = Mesh(
        mesh.devices.reshape(4, 4, 2, mesh.shape["expo"]), ("tile_0", "tile_1", "tile_2", "expo")
    )
    placed = (
        P(None, "expo", TILE),
        P("expo", TILE),
        P("expo", TILE),
        P("expo", TILE),
        P(None, "expo", TILE),
        P(None, None, TILE),
        P(TILE),
        P(),
        P(),
        P(TILE, None),
        P(TILE, None, None),
    )
    return jax.shard_map(
        on_device,
        mesh=split,
        in_specs=placed,
        out_specs=(P(TILE_EXPO, None), P(TILE_EXPO, None)),
        check_vma=False,
    )
```

```python
import jax
import jax.numpy as jnp
from jax import lax
from jax.experimental import pallas as pl
from jax.experimental.pallas import tpu as pltpu
from jax.sharding import Mesh
from jax.sharding import PartitionSpec as P

DEG_X = 6
DEG_Y = 5
TILE = ("tile_0", "tile_1", "tile_2")
TILE_EXPO = ("tile_0", "tile_1", "tile_2", "expo")


highest = lax.Precision.HIGHEST
contract = (((1, 2), (1, 2)), ((), ()))


def turned_gather(arrays, axis, dims):
    turned = [jnp.moveaxis(a, dim, 0) for a, dim in zip(arrays, dims)]
    both = jnp.concatenate([t.reshape(len(t), -1) for t in turned], axis=1)
    filled, at, done = (lax.all_gather(both, axis, axis=0, tiled=True), 0, [])
    for t, dim in zip(turned, dims):
        piece = filled[:, at : at + t[0].size].reshape(-1, *t.shape[1:])
        done.append(jnp.moveaxis(piece, 0, dim))
        at += t[0].size
    return tuple(done)


def sum_in_order(tiles, axes, order):
    inside = tiles.shape[1:]
    tiles = tiles.reshape(*(lax.axis_size(a) for a in axes), *inside)
    tiles = jnp.moveaxis(tiles, order, range(len(axes))).reshape(-1, *inside)
    for k in order:
        tiles = lax.psum_scatter(tiles, axes[k], scatter_dimension=0, tiled=True)
    return tiles[0]


def split_up(array, dim, length):
    before, after = (array.shape[:dim], array.shape[dim + 1 :])
    return jnp.moveaxis(array.reshape(*before, length, -1, *after), dim, 0)


def scatter_axes(array, axes, order, dim):
    length = lax.axis_size(axes)
    return sum_in_order(split_up(array, dim, length), axes, order)


def chebyshev(values, degree):
    series = [jnp.ones_like(values), values]
    for degree_at in range(2, degree):
        series.append(2.0 * values * series[-1] - series[-2])
    return series[:degree]


def focal_weight(pixel_uv, ccd_index, observed, obs_weight, live_rows, ccd_center):
    ccd_total = ccd_center.shape[1]
    picked = (
        ccd_index[None, :, :] == jnp.arange(ccd_total, dtype=jnp.int32)[:, None, None]
    ).astype(jnp.float32)
    centre = jnp.sum(ccd_center[:, :, None, None] * picked[None], axis=1)
    focal = 0.75 * centre + 0.25 * pixel_uv
    star_rows = ccd_index.shape[1]
    alive = (jnp.arange(star_rows, dtype=jnp.int32)[None, :] < live_rows).astype(jnp.float32)
    live_weight = obs_weight * observed.astype(jnp.float32) * alive
    return (focal, live_weight)


def basis_of(focal):
    along_first = chebyshev(focal[0], DEG_X)
    along_second = chebyshev(focal[1], DEG_Y)
    return jnp.stack(
        [first_term * second_term for first_term in along_first for second_term in along_second],
        axis=1,
    )


def jacobian_of(geometry):
    shift_time = geometry[0]
    factor_first = geometry[1]
    factor_second = geometry[2]
    unit_row = jnp.ones_like(shift_time)
    zero_row = jnp.zeros_like(shift_time)
    return jnp.stack(
        [
            jnp.stack([unit_row, zero_row, shift_time, zero_row, factor_first], axis=-1),
            jnp.stack([zero_row, unit_row, zero_row, shift_time, factor_second], axis=-1),
        ],
        axis=1,
    )


def geometry_of(exp_geom, exposure_ids):
    picked = (
        jnp.arange(exp_geom.shape[1], dtype=jnp.int32)[:, None] == exposure_ids[None, :]
    ).astype(jnp.float32)
    return (jnp.sum(exp_geom[:, :, None] * picked[None], axis=1), picked)


def coupling_matrix(live_weight, basis, jacobian):
    full = (
        live_weight[:, None, None, None, :]
        * jacobian[:, :, None, :, None]
        * basis[:, None, :, None, :]
    )
    return full.astype(jnp.bfloat16).reshape(basis.shape[0] * 2 * basis.shape[1], 5, basis.shape[2])


def negated_scaled(coupling, inverse):
    return (
        -jnp.einsum("xis,jis->xjs", coupling.astype(jnp.float32), inverse, precision=highest)
    ).astype(jnp.bfloat16)


def diagonal_blocks(live_weight, basis):
    weighted = live_weight[:, None, :] * basis
    gram = jnp.einsum("ams,ans->amn", weighted, basis, precision=highest)
    pair_eye = jnp.eye(2, dtype=jnp.float32)
    full = jnp.einsum("cd,amn->acmdn", pair_eye, gram, precision=highest)
    return (full.reshape(gram.shape[0], 2 * gram.shape[1], 2 * gram.shape[1]), weighted)


def gradient_terms(jacobian, live_weight, obs_resid):
    return jnp.einsum("aci,as,cas->is", jacobian, live_weight, obs_resid, precision=highest)


def local_rhs(weighted, jacobian, obs_resid, solved):
    correction = jnp.einsum("aci,is->cas", jacobian, solved, precision=highest)
    result = jnp.einsum("ams,cas->acm", weighted, obs_resid - correction, precision=highest)
    return result.reshape(weighted.shape[0], 2 * weighted.shape[1])


def star_product(former, latter):
    return lax.dot_general(former, latter, contract, preferred_element_type=jnp.float32)


LANES = 128


def schur_kernel(xa, ya, wa, wda, wfa, wga, xo, yo, wo, wdo, wfo, wgo, si, out, peak, rhs0, rhs1, lhs0, lhs1):
    step = pl.program_id(0)
    bf = jnp.bfloat16
    f32 = jnp.float32
    n_all = xa.shape[0]
    n_own = xo.shape[0]
    terms = DEG_X * DEG_Y

    @pl.when(step == 0)
    def _():
        out[...] = jnp.zeros_like(out)

    tx = chebyshev(xa[...], DEG_X)
    ty = chebyshev(ya[...], DEG_Y)
    txo = chebyshev(xo[...], DEG_X)
    tyo = chebyshev(yo[...], DEG_Y)
    w, wd, wf, wg = wa[...], wda[...], wfa[...], wga[...]
    w_o, wd_o, wf_o, wg_o = wo[...], wdo[...], wfo[...], wgo[...]
    inv = [[si[pl.ds(j * 5 + i, 1), :] for i in range(5)] for j in range(5)]
    for p in range(DEG_X):
        for q in range(DEG_Y):
            m = p * DEG_Y + q
            b = tx[p] * ty[q]
            cp = (w * b).astype(bf).astype(f32)
            cq = (wd * b).astype(bf).astype(f32)
            cr = (wf * b).astype(bf).astype(f32)
            cs = (wg * b).astype(bf).astype(f32)
            for d, (k0, k1, last) in enumerate(((0, 2, cr), (1, 3, cs))):
                rows = pl.ds((d * terms + m) * n_all, n_all)
                sc = [(-(inv[j][k0] * cp + inv[j][k1] * cq + inv[j][4] * last)).astype(bf) for j in range(5)]
                for t, j in enumerate((0, 2, 4)):
                    rhs0[rows, pl.ds(t * LANES, LANES)] = sc[j]
                for t, j in enumerate((1, 3, 4)):
                    rhs1[rows, pl.ds(t * LANES, LANES)] = sc[j]
            bo = txo[p] * tyo[q]
            po = (w_o * bo).astype(bf).astype(f32)
            qo = (wd_o * bo).astype(bf).astype(f32)
            own_rows = pl.ds(m * n_own, n_own)
            lhs0[own_rows, pl.ds(0, LANES)] = po
            lhs0[own_rows, pl.ds(LANES, LANES)] = qo
            lhs0[own_rows, pl.ds(2 * LANES, LANES)] = (wf_o * bo).astype(bf).astype(f32)
            lhs1[own_rows, pl.ds(0, LANES)] = po
            lhs1[own_rows, pl.ds(LANES, LANES)] = qo
            lhs1[own_rows, pl.ds(2 * LANES, LANES)] = (wg_o * bo).astype(bf).astype(f32)
    out[0] += lax.dot_general(lhs0[...].astype(bf), rhs0[...], (((1,), (1,)), ((), ())), preferred_element_type=f32)
    out[1] += lax.dot_general(lhs1[...].astype(bf), rhs1[...], (((1,), (1,)), ((), ())), preferred_element_type=f32)

    @pl.when(step == pl.num_programs(0) - 1)
    def _():
        top = jnp.maximum(jnp.max(jnp.abs(out[0])), jnp.max(jnp.abs(out[1])))
        peak[...] = jnp.full(peak.shape, top, f32)


def schur_product(all_x, all_y, all_w, all_wd, all_wf, all_wg, own_x, own_y, own_w, own_wd, own_wf, own_wg, inverse):
    n_all, stars = all_x.shape
    n_own = own_x.shape[0]
    terms = DEG_X * DEG_Y
    rows_all = 2 * terms * n_all
    rows_own = terms * n_own
    all_spec = pl.BlockSpec((n_all, LANES), lambda k: (0, k))
    own_spec = pl.BlockSpec((n_own, LANES), lambda k: (0, k))
    inv_spec = pl.BlockSpec((25, LANES), lambda k: (0, k))
    return pl.pallas_call(
        schur_kernel,
        out_shape=(
            jax.ShapeDtypeStruct((2, rows_own, rows_all), jnp.float32),
            jax.ShapeDtypeStruct((8, LANES), jnp.float32),
        ),
        grid=(stars // LANES,),
        in_specs=[all_spec] * 6 + [own_spec] * 6 + [inv_spec],
        out_specs=(
            pl.BlockSpec((2, rows_own, rows_all), lambda k: (0, 0, 0)),
            pl.BlockSpec((8, LANES), lambda k: (0, 0)),
        ),
        scratch_shapes=[
            pltpu.VMEM((rows_all, 3 * LANES), jnp.bfloat16),
            pltpu.VMEM((rows_all, 3 * LANES), jnp.bfloat16),
            pltpu.VMEM((rows_own, 3 * LANES), jnp.float32),
            pltpu.VMEM((rows_own, 3 * LANES), jnp.float32),
        ],
        compiler_params=pltpu.CompilerParams(dimension_semantics=("arbitrary",)),
    )(all_x, all_y, all_w, all_wd, all_wf, all_wg, own_x, own_y, own_w, own_wd, own_wf, own_wg, inverse)


def octave_of(bound):
    bound = jnp.where(bound > 0.0, bound, 1.0)
    octave = jnp.ceil(jnp.log2(bound))
    octave = octave + jnp.where(jnp.exp2(octave) < bound, 1.0, 0.0)
    return jnp.clip(octave, -126.0, 127.0)


def on_device(
    pixel_uv,
    ccd_index,
    observed,
    obs_weight,
    obs_resid,
    star_inverse,
    star_count,
    ccd_center,
    exp_geom,
    tile_exposures,
    pair_owner,
):
    expo_total = lax.axis_size("expo")
    tile_total = lax.axis_size(TILE)
    expo_rank = lax.axis_index("expo")
    loc_dev = ccd_index.shape[0]
    window = tile_exposures.shape[1]
    params = 2 * DEG_X * DEG_Y
    live_rows = star_count[0]
    exposure_ids = lax.dynamic_slice_in_dim(tile_exposures[0], expo_rank * loc_dev, loc_dev)
    geometry, picked = geometry_of(exp_geom, exposure_ids)
    focal, live_weight = focal_weight(
        pixel_uv, ccd_index, observed, obs_weight, live_rows, ccd_center
    )
    basis = basis_of(focal)
    jacobian = jacobian_of(geometry)
    diagonal, weighted = diagonal_blocks(live_weight, basis)
    own_rows = expo_rank * loc_dev + jnp.arange(loc_dev, dtype=jnp.int32)
    local_rows = jnp.arange(loc_dev, dtype=jnp.int32)
    all_focal, all_weight, all_resid = turned_gather(
        (focal, live_weight, obs_resid), "expo", (1, 0, 1)
    )
    all_geometry, all_picked = geometry_of(exp_geom, tile_exposures[0])
    all_jacobian = jacobian_of(all_geometry)
    all_x, all_y = all_focal[0], all_focal[1]
    own_x, own_y = focal[0], focal[1]
    products, peak = schur_product(
        all_x, all_y, all_weight,
        all_weight * all_geometry[0][:, None], all_weight * all_geometry[1][:, None], all_weight * all_geometry[2][:, None],
        own_x, own_y, live_weight,
        live_weight * geometry[0][:, None], live_weight * geometry[1][:, None], live_weight * geometry[2][:, None],
        star_inverse.reshape(25, -1),
    )
    terms = DEG_X * DEG_Y
    owners = lax.dynamic_slice_in_dim(pair_owner[0], expo_rank * loc_dev, loc_dev, 0)
    pair_dev = 3 * (window // 2) * (window // 2) // expo_total
    flat_owner = owners.reshape(-1)
    entries = flat_owner.shape[0]
    product = products.reshape(2, terms, loc_dev, params, window)
    product = jnp.transpose(product, (2, 4, 0, 1, 3)).reshape(loc_dev, window, params * params)
    on_diagonal = own_rows[:, None] == jnp.arange(window, dtype=jnp.int32)[None, :]
    diagonal_flat = diagonal.reshape(loc_dev, 1, params * params)
    product = product + jnp.where(on_diagonal[:, :, None], diagonal_flat, 0.0)
    product = product.reshape(loc_dev * window, params * params)
    gradient = gradient_terms(all_jacobian, all_weight, all_resid)
    solved = jnp.einsum("jis,is->js", star_inverse, gradient, precision=highest)
    rhs_local = local_rhs(weighted, jacobian, obs_resid, solved)
    devices = tile_total * expo_total
    per_peer = entries // devices
    spread = jnp.dot(picked, rhs_local, precision=highest).reshape(entries, -1)
    target = flat_owner // pair_dev
    ranking = jnp.argsort(target, stable=True)
    place = jnp.zeros((entries,), jnp.int32).at[ranking].set(jnp.arange(entries, dtype=jnp.int32))
    block_octave = octave_of(peak[0, 0] + jnp.max(jnp.abs(diagonal)))
    rhs_octave = octave_of(jnp.max(jnp.abs(spread)))
    product = product * (1.0 / jnp.exp2(block_octave))
    rhs_part = spread[place] * (1.0 / jnp.exp2(rhs_octave))
    rhs_high = rhs_part.astype(jnp.float16)
    rhs_low = (rhs_part - rhs_high.astype(jnp.float32)).astype(jnp.float16)
    slot_tags = (flat_owner % pair_dev).astype(jnp.float32)
    product = jnp.concatenate(
        [
            product.astype(jnp.float16),
            slot_tags[:, None].astype(jnp.float16),
            jnp.broadcast_to(block_octave, (entries, 1)).astype(jnp.float16),
            jnp.broadcast_to(rhs_octave, (entries, 1)).astype(jnp.float16),
            rhs_high,
            rhs_low,
        ],
        axis=1,
    )
    outgoing = jnp.take(product, ranking.reshape(devices, per_peer), axis=0, mode="clip")
    incoming = lax.all_to_all(outgoing, TILE_EXPO, split_axis=0, concat_axis=0, tiled=True)
    block_len = params * params
    rhs_len = spread.shape[1]
    incoming_tags = incoming[:, :, block_len].astype(jnp.int32)
    incoming_scale = jnp.exp2(incoming[:, :, block_len + 1].astype(jnp.float32))
    rhs_scale = jnp.exp2(incoming[:, :, block_len + 2].astype(jnp.float32))
    rhs_from = block_len + 3
    rhs_in = incoming[:, :, rhs_from : rhs_from + rhs_len].astype(jnp.float32)
    rhs_in = rhs_in + incoming[:, :, rhs_from + rhs_len : rhs_from + 2 * rhs_len].astype(jnp.float32)
    rhs_in = (rhs_in * rhs_scale[:, :, None]).reshape(devices, -1, params)
    reduced_rhs = jnp.sum(rhs_in, axis=0)
    receive_slots = jnp.where(
        jnp.arange(pair_dev, dtype=jnp.int32)[:, None, None] == incoming_tags[None],
        incoming_scale[None],
        0.0,
    )
    pair_blocks = lax.dot_general(
        receive_slots, incoming[:, :, :block_len].astype(jnp.float32), (((1, 2), (0, 1)), ((), ())), precision=highest
    )
    return (pair_blocks, reduced_rhs)


def solution(mesh):
    split = Mesh(
        mesh.devices.reshape(4, 4, 2, mesh.shape["expo"]), ("tile_0", "tile_1", "tile_2", "expo")
    )
    placed = (
        P(None, "expo", TILE),
        P("expo", TILE),
        P("expo", TILE),
        P("expo", TILE),
        P(None, "expo", TILE),
        P(None, None, TILE),
        P(TILE),
        P(),
        P(),
        P(TILE, None),
        P(TILE, None, None),
    )
    return jax.shard_map(
        on_device,
        mesh=split,
        in_specs=placed,
        out_specs=(P(TILE_EXPO, None), P(TILE_EXPO, None)),
        check_vma=False,
    )
```

```python
import jax
import jax.numpy as jnp
from jax import lax
from jax.experimental import pallas as pl
from jax.experimental.pallas import tpu as pltpu
from jax.sharding import Mesh
from jax.sharding import PartitionSpec as P

DEG_X = 6
DEG_Y = 5
TILE = ("tile_0", "tile_1", "tile_2")
TILE_EXPO = ("tile_0", "tile_1", "tile_2", "expo")


highest = lax.Precision.HIGHEST
contract = (((1, 2), (1, 2)), ((), ()))


def turned_gather(arrays, axis, dims):
    turned = [jnp.moveaxis(a, dim, 0) for a, dim in zip(arrays, dims)]
    both = jnp.concatenate([t.reshape(len(t), -1) for t in turned], axis=1)
    filled, at, done = (lax.all_gather(both, axis, axis=0, tiled=True), 0, [])
    for t, dim in zip(turned, dims):
        piece = filled[:, at : at + t[0].size].reshape(-1, *t.shape[1:])
        done.append(jnp.moveaxis(piece, 0, dim))
        at += t[0].size
    return tuple(done)


def sum_in_order(tiles, axes, order):
    inside = tiles.shape[1:]
    tiles = tiles.reshape(*(lax.axis_size(a) for a in axes), *inside)
    tiles = jnp.moveaxis(tiles, order, range(len(axes))).reshape(-1, *inside)
    for k in order:
        tiles = lax.psum_scatter(tiles, axes[k], scatter_dimension=0, tiled=True)
    return tiles[0]


def split_up(array, dim, length):
    before, after = (array.shape[:dim], array.shape[dim + 1 :])
    return jnp.moveaxis(array.reshape(*before, length, -1, *after), dim, 0)


def scatter_axes(array, axes, order, dim):
    length = lax.axis_size(axes)
    return sum_in_order(split_up(array, dim, length), axes, order)


def chebyshev(values, degree):
    series = [jnp.ones_like(values), values]
    for degree_at in range(2, degree):
        series.append(2.0 * values * series[-1] - series[-2])
    return series[:degree]


def focal_weight(pixel_uv, ccd_index, observed, obs_weight, live_rows, ccd_center):
    ccd_total = ccd_center.shape[1]
    picked = (
        ccd_index[None, :, :] == jnp.arange(ccd_total, dtype=jnp.int32)[:, None, None]
    ).astype(jnp.float32)
    centre = jnp.sum(ccd_center[:, :, None, None] * picked[None], axis=1)
    focal = 0.75 * centre + 0.25 * pixel_uv
    star_rows = ccd_index.shape[1]
    alive = (jnp.arange(star_rows, dtype=jnp.int32)[None, :] < live_rows).astype(jnp.float32)
    live_weight = obs_weight * observed.astype(jnp.float32) * alive
    return (focal, live_weight)


def basis_of(focal):
    along_first = chebyshev(focal[0], DEG_X)
    along_second = chebyshev(focal[1], DEG_Y)
    return jnp.stack(
        [first_term * second_term for first_term in along_first for second_term in along_second],
        axis=1,
    )


def jacobian_of(geometry):
    shift_time = geometry[0]
    factor_first = geometry[1]
    factor_second = geometry[2]
    unit_row = jnp.ones_like(shift_time)
    zero_row = jnp.zeros_like(shift_time)
    return jnp.stack(
        [
            jnp.stack([unit_row, zero_row, shift_time, zero_row, factor_first], axis=-1),
            jnp.stack([zero_row, unit_row, zero_row, shift_time, factor_second], axis=-1),
        ],
        axis=1,
    )


def geometry_of(exp_geom, exposure_ids):
    picked = (
        jnp.arange(exp_geom.shape[1], dtype=jnp.int32)[:, None] == exposure_ids[None, :]
    ).astype(jnp.float32)
    return (jnp.sum(exp_geom[:, :, None] * picked[None], axis=1), picked)


def coupling_matrix(live_weight, basis, jacobian):
    full = (
        live_weight[:, None, None, None, :]
        * jacobian[:, :, None, :, None]
        * basis[:, None, :, None, :]
    )
    return full.astype(jnp.bfloat16).reshape(basis.shape[0] * 2 * basis.shape[1], 5, basis.shape[2])


def negated_scaled(coupling, inverse):
    return (
        -jnp.einsum("xis,jis->xjs", coupling.astype(jnp.float32), inverse, precision=highest)
    ).astype(jnp.bfloat16)


def diagonal_blocks(live_weight, basis):
    weighted = live_weight[:, None, :] * basis
    gram = jnp.einsum("ams,ans->amn", weighted, basis, precision=highest)
    pair_eye = jnp.eye(2, dtype=jnp.float32)
    full = jnp.einsum("cd,amn->acmdn", pair_eye, gram, precision=highest)
    return (full.reshape(gram.shape[0], 2 * gram.shape[1], 2 * gram.shape[1]), weighted)


def gradient_terms(jacobian, live_weight, obs_resid):
    return jnp.einsum("aci,as,cas->is", jacobian, live_weight, obs_resid, precision=highest)


def local_rhs(weighted, jacobian, obs_resid, solved):
    correction = jnp.einsum("aci,is->cas", jacobian, solved, precision=highest)
    result = jnp.einsum("ams,cas->acm", weighted, obs_resid - correction, precision=highest)
    return result.reshape(weighted.shape[0], 2 * weighted.shape[1])


def star_product(former, latter):
    return lax.dot_general(former, latter, contract, preferred_element_type=jnp.float32)


LANES = 256


def schur_kernel(xa, ya, wa, wda, wfa, wga, xo, yo, wo, wdo, wfo, wgo, si, out, peak, rhs0, rhs1, lhs0, lhs1):
    step = pl.program_id(0)
    bf = jnp.bfloat16
    f32 = jnp.float32
    n_all = xa.shape[0]
    n_own = xo.shape[0]
    terms = DEG_X * DEG_Y

    @pl.when(step == 0)
    def _():
        out[...] = jnp.zeros_like(out)

    tx = chebyshev(xa[...], DEG_X)
    ty = chebyshev(ya[...], DEG_Y)
    txo = chebyshev(xo[...], DEG_X)
    tyo = chebyshev(yo[...], DEG_Y)
    w, wd, wf, wg = wa[...], wda[...], wfa[...], wga[...]
    w_o, wd_o, wf_o, wg_o = wo[...], wdo[...], wfo[...], wgo[...]
    inv = [[si[pl.ds(j * 5 + i, 1), :] for i in range(5)] for j in range(5)]
    for p in range(DEG_X):
        for q in range(DEG_Y):
            m = p * DEG_Y + q
            b = tx[p] * ty[q]
            cp = (w * b).astype(bf).astype(f32)
            cq = (wd * b).astype(bf).astype(f32)
            cr = (wf * b).astype(bf).astype(f32)
            cs = (wg * b).astype(bf).astype(f32)
            for d, (k0, k1, last) in enumerate(((0, 2, cr), (1, 3, cs))):
                rows = pl.ds((d * terms + m) * n_all, n_all)
                sc = [(-(inv[j][k0] * cp + inv[j][k1] * cq + inv[j][4] * last)).astype(bf) for j in range(5)]
                for t, j in enumerate((0, 2, 4)):
                    rhs0[rows, pl.ds(t * LANES, LANES)] = sc[j]
                for t, j in enumerate((1, 3, 4)):
                    rhs1[rows, pl.ds(t * LANES, LANES)] = sc[j]
            bo = txo[p] * tyo[q]
            po = (w_o * bo).astype(bf).astype(f32)
            qo = (wd_o * bo).astype(bf).astype(f32)
            own_rows = pl.ds(m * n_own, n_own)
            lhs0[own_rows, pl.ds(0, LANES)] = po
            lhs0[own_rows, pl.ds(LANES, LANES)] = qo
            lhs0[own_rows, pl.ds(2 * LANES, LANES)] = (wf_o * bo).astype(bf).astype(f32)
            lhs1[own_rows, pl.ds(0, LANES)] = po
            lhs1[own_rows, pl.ds(LANES, LANES)] = qo
            lhs1[own_rows, pl.ds(2 * LANES, LANES)] = (wg_o * bo).astype(bf).astype(f32)
    out[0] += lax.dot_general(lhs0[...].astype(bf), rhs0[...], (((1,), (1,)), ((), ())), preferred_element_type=f32)
    out[1] += lax.dot_general(lhs1[...].astype(bf), rhs1[...], (((1,), (1,)), ((), ())), preferred_element_type=f32)

    @pl.when(step == pl.num_programs(0) - 1)
    def _():
        top = jnp.maximum(jnp.max(jnp.abs(out[0])), jnp.max(jnp.abs(out[1])))
        peak[...] = jnp.full(peak.shape, top, f32)


def schur_product(all_x, all_y, all_w, all_wd, all_wf, all_wg, own_x, own_y, own_w, own_wd, own_wf, own_wg, inverse):
    n_all, stars = all_x.shape
    n_own = own_x.shape[0]
    terms = DEG_X * DEG_Y
    rows_all = 2 * terms * n_all
    rows_own = terms * n_own
    all_spec = pl.BlockSpec((n_all, LANES), lambda k: (0, k))
    own_spec = pl.BlockSpec((n_own, LANES), lambda k: (0, k))
    inv_spec = pl.BlockSpec((25, LANES), lambda k: (0, k))
    return pl.pallas_call(
        schur_kernel,
        out_shape=(
            jax.ShapeDtypeStruct((2, rows_own, rows_all), jnp.float32),
            jax.ShapeDtypeStruct((8, LANES), jnp.float32),
        ),
        grid=(stars // LANES,),
        in_specs=[all_spec] * 6 + [own_spec] * 6 + [inv_spec],
        out_specs=(
            pl.BlockSpec((2, rows_own, rows_all), lambda k: (0, 0, 0)),
            pl.BlockSpec((8, LANES), lambda k: (0, 0)),
        ),
        scratch_shapes=[
            pltpu.VMEM((rows_all, 3 * LANES), jnp.bfloat16),
            pltpu.VMEM((rows_all, 3 * LANES), jnp.bfloat16),
            pltpu.VMEM((rows_own, 3 * LANES), jnp.float32),
            pltpu.VMEM((rows_own, 3 * LANES), jnp.float32),
        ],
        compiler_params=pltpu.CompilerParams(dimension_semantics=("arbitrary",)),
    )(all_x, all_y, all_w, all_wd, all_wf, all_wg, own_x, own_y, own_w, own_wd, own_wf, own_wg, inverse)


def on_device(
    pixel_uv,
    ccd_index,
    observed,
    obs_weight,
    obs_resid,
    star_inverse,
    star_count,
    ccd_center,
    exp_geom,
    tile_exposures,
    pair_owner,
):
    expo_total = lax.axis_size("expo")
    tile_total = lax.axis_size(TILE)
    expo_rank = lax.axis_index("expo")
    loc_dev = ccd_index.shape[0]
    window = tile_exposures.shape[1]
    params = 2 * DEG_X * DEG_Y
    live_rows = star_count[0]
    exposure_ids = lax.dynamic_slice_in_dim(tile_exposures[0], expo_rank * loc_dev, loc_dev)
    geometry, picked = geometry_of(exp_geom, exposure_ids)
    focal, live_weight = focal_weight(
        pixel_uv, ccd_index, observed, obs_weight, live_rows, ccd_center
    )
    basis = basis_of(focal)
    jacobian = jacobian_of(geometry)
    diagonal, weighted = diagonal_blocks(live_weight, basis)
    own_rows = expo_rank * loc_dev + jnp.arange(loc_dev, dtype=jnp.int32)
    local_rows = jnp.arange(loc_dev, dtype=jnp.int32)
    all_focal, all_weight, all_resid = turned_gather(
        (focal, live_weight, obs_resid), "expo", (1, 0, 1)
    )
    all_geometry, all_picked = geometry_of(exp_geom, tile_exposures[0])
    all_jacobian = jacobian_of(all_geometry)
    all_x, all_y = all_focal[0], all_focal[1]
    own_x, own_y = focal[0], focal[1]
    products, peak = schur_product(
        all_x, all_y, all_weight,
        all_weight * all_geometry[0][:, None], all_weight * all_geometry[1][:, None], all_weight * all_geometry[2][:, None],
        own_x, own_y, live_weight,
        live_weight * geometry[0][:, None], live_weight * geometry[1][:, None], live_weight * geometry[2][:, None],
        star_inverse.reshape(25, -1),
    )
    terms = DEG_X * DEG_Y
    product = products.reshape(2, terms, loc_dev, params, window)
    product = jnp.transpose(product, (2, 4, 0, 1, 3)).reshape(loc_dev, window, params * params)
    on_diagonal = own_rows[:, None] == jnp.arange(window, dtype=jnp.int32)[None, :]
    diagonal_flat = diagonal.reshape(loc_dev, 1, params * params)
    product = product + jnp.where(on_diagonal[:, :, None], diagonal_flat, 0.0)
    product = product.reshape(loc_dev * window, params * params)
    bound = peak[0, 0] + jnp.max(jnp.abs(diagonal))
    bound = jnp.where(bound > 0.0, bound, 1.0)
    product = (product * (1.0 / bound)).astype(jnp.float16)
    owners = lax.dynamic_slice_in_dim(pair_owner[0], expo_rank * loc_dev, loc_dev, 0)
    gradient = gradient_terms(all_jacobian, all_weight, all_resid)
    solved = jnp.einsum("jis,is->js", star_inverse, gradient, precision=highest)
    rhs_local = local_rhs(weighted, jacobian, obs_resid, solved)
    devices = tile_total * expo_total
    spread = jnp.dot(picked, rhs_local, precision=highest).reshape(devices, -1)
    pair_dev = 3 * (window // 2) * (window // 2) // expo_total
    flat_owner = owners.reshape(-1)
    target = flat_owner // pair_dev
    ranking = jnp.argsort(target, stable=True)
    per_peer = flat_owner.shape[0] // devices
    outgoing = jnp.take(product, ranking.reshape(devices, per_peer), axis=0, mode="clip")
    slot_tags = (flat_owner % pair_dev)[ranking].reshape(devices, per_peer).astype(jnp.float32)
    sent_scale = jnp.full((devices, 1), bound, jnp.float32)
    small = jnp.concatenate([spread, slot_tags, sent_scale], axis=1)
    incoming_blocks = lax.all_to_all(outgoing, TILE_EXPO, split_axis=0, concat_axis=0, tiled=True)
    incoming_small = lax.all_to_all(small, TILE_EXPO, split_axis=0, concat_axis=0, tiled=True)
    incoming_rhs = incoming_small[:, : spread.shape[1]]
    incoming_tags = incoming_small[:, spread.shape[1] : spread.shape[1] + per_peer].astype(jnp.int32)
    incoming_scale = jnp.broadcast_to(incoming_small[:, spread.shape[1] + per_peer :], (devices, per_peer))
    receive_slots = jnp.where(
        jnp.arange(pair_dev, dtype=jnp.int32)[:, None] == incoming_tags.reshape(1, -1),
        incoming_scale.reshape(1, -1),
        0.0,
    )
    incoming_blocks = incoming_blocks.astype(jnp.float32)
    receive_slots = receive_slots.reshape(pair_dev, devices, per_peer)
    pair_blocks = lax.dot_general(
        receive_slots, incoming_blocks, (((1, 2), (0, 1)), ((), ())), precision=highest
    )
    reduced_rhs = jnp.sum(incoming_rhs.reshape(devices, -1, params), axis=0)
    return (pair_blocks, reduced_rhs)


def solution(mesh):
    split = Mesh(
        mesh.devices.reshape(4, 4, 2, mesh.shape["expo"]), ("tile_0", "tile_1", "tile_2", "expo")
    )
    placed = (
        P(None, "expo", TILE),
        P("expo", TILE),
        P("expo", TILE),
        P("expo", TILE),
        P(None, "expo", TILE),
        P(None, None, TILE),
        P(TILE),
        P(),
        P(),
        P(TILE, None),
        P(TILE, None, None),
    )
    return jax.shard_map(
        on_device,
        mesh=split,
        in_specs=placed,
        out_specs=(P(TILE_EXPO, None), P(TILE_EXPO, None)),
        check_vma=False,
    )
```

```python
import jax
import jax.numpy as jnp
from jax import lax
from jax.experimental import pallas as pl
from jax.experimental.pallas import tpu as pltpu
from jax.sharding import Mesh
from jax.sharding import PartitionSpec as P

DEG_X = 6
DEG_Y = 5
TILE = ("tile_0", "tile_1", "tile_2")
TILE_EXPO = ("tile_0", "tile_1", "tile_2", "expo")


highest = lax.Precision.HIGHEST
contract = (((1, 2), (1, 2)), ((), ()))


def turned_gather(arrays, axis, dims):
    turned = [jnp.moveaxis(a, dim, 0) for a, dim in zip(arrays, dims)]
    both = jnp.concatenate([t.reshape(len(t), -1) for t in turned], axis=1)
    filled, at, done = (lax.all_gather(both, axis, axis=0, tiled=True), 0, [])
    for t, dim in zip(turned, dims):
        piece = filled[:, at : at + t[0].size].reshape(-1, *t.shape[1:])
        done.append(jnp.moveaxis(piece, 0, dim))
        at += t[0].size
    return tuple(done)


def sum_in_order(tiles, axes, order):
    inside = tiles.shape[1:]
    tiles = tiles.reshape(*(lax.axis_size(a) for a in axes), *inside)
    tiles = jnp.moveaxis(tiles, order, range(len(axes))).reshape(-1, *inside)
    for k in order:
        tiles = lax.psum_scatter(tiles, axes[k], scatter_dimension=0, tiled=True)
    return tiles[0]


def split_up(array, dim, length):
    before, after = (array.shape[:dim], array.shape[dim + 1 :])
    return jnp.moveaxis(array.reshape(*before, length, -1, *after), dim, 0)


def scatter_axes(array, axes, order, dim):
    length = lax.axis_size(axes)
    return sum_in_order(split_up(array, dim, length), axes, order)


def chebyshev(values, degree):
    series = [jnp.ones_like(values), values]
    for degree_at in range(2, degree):
        series.append(2.0 * values * series[-1] - series[-2])
    return series[:degree]


def focal_weight(pixel_uv, ccd_index, observed, obs_weight, live_rows, ccd_center):
    ccd_total = ccd_center.shape[1]
    picked = (
        ccd_index[None, :, :] == jnp.arange(ccd_total, dtype=jnp.int32)[:, None, None]
    ).astype(jnp.float32)
    centre = jnp.sum(ccd_center[:, :, None, None] * picked[None], axis=1)
    focal = 0.75 * centre + 0.25 * pixel_uv
    star_rows = ccd_index.shape[1]
    alive = (jnp.arange(star_rows, dtype=jnp.int32)[None, :] < live_rows).astype(jnp.float32)
    live_weight = obs_weight * observed.astype(jnp.float32) * alive
    return (focal, live_weight)


def basis_of(focal):
    along_first = chebyshev(focal[0], DEG_X)
    along_second = chebyshev(focal[1], DEG_Y)
    return jnp.stack(
        [first_term * second_term for first_term in along_first for second_term in along_second],
        axis=1,
    )


def jacobian_of(geometry):
    shift_time = geometry[0]
    factor_first = geometry[1]
    factor_second = geometry[2]
    unit_row = jnp.ones_like(shift_time)
    zero_row = jnp.zeros_like(shift_time)
    return jnp.stack(
        [
            jnp.stack([unit_row, zero_row, shift_time, zero_row, factor_first], axis=-1),
            jnp.stack([zero_row, unit_row, zero_row, shift_time, factor_second], axis=-1),
        ],
        axis=1,
    )


def geometry_of(exp_geom, exposure_ids):
    picked = (
        jnp.arange(exp_geom.shape[1], dtype=jnp.int32)[:, None] == exposure_ids[None, :]
    ).astype(jnp.float32)
    return (jnp.sum(exp_geom[:, :, None] * picked[None], axis=1), picked)


def coupling_matrix(live_weight, basis, jacobian):
    full = (
        live_weight[:, None, None, None, :]
        * jacobian[:, :, None, :, None]
        * basis[:, None, :, None, :]
    )
    return full.astype(jnp.bfloat16).reshape(basis.shape[0] * 2 * basis.shape[1], 5, basis.shape[2])


def negated_scaled(coupling, inverse):
    return (
        -jnp.einsum("xis,jis->xjs", coupling.astype(jnp.float32), inverse, precision=highest)
    ).astype(jnp.bfloat16)


def diagonal_blocks(live_weight, basis):
    weighted = live_weight[:, None, :] * basis
    gram = jnp.einsum("ams,ans->amn", weighted, basis, precision=highest)
    pair_eye = jnp.eye(2, dtype=jnp.float32)
    full = jnp.einsum("cd,amn->acmdn", pair_eye, gram, precision=highest)
    return (full.reshape(gram.shape[0], 2 * gram.shape[1], 2 * gram.shape[1]), weighted)


def gradient_terms(jacobian, live_weight, obs_resid):
    return jnp.einsum("aci,as,cas->is", jacobian, live_weight, obs_resid, precision=highest)


def local_rhs(weighted, jacobian, obs_resid, solved):
    correction = jnp.einsum("aci,is->cas", jacobian, solved, precision=highest)
    result = jnp.einsum("ams,cas->acm", weighted, obs_resid - correction, precision=highest)
    return result.reshape(weighted.shape[0], 2 * weighted.shape[1])


def star_product(former, latter):
    return lax.dot_general(former, latter, contract, preferred_element_type=jnp.float32)


LANES = 512


def schur_kernel(xa, ya, wa, wda, wfa, wga, xo, yo, wo, wdo, wfo, wgo, si, out, peak, rhs0, rhs1, lhs0, lhs1):
    step = pl.program_id(0)
    bf = jnp.bfloat16
    f32 = jnp.float32
    n_all = xa.shape[0]
    n_own = xo.shape[0]
    terms = DEG_X * DEG_Y

    @pl.when(step == 0)
    def _():
        out[...] = jnp.zeros_like(out)

    tx = chebyshev(xa[...], DEG_X)
    ty = chebyshev(ya[...], DEG_Y)
    txo = chebyshev(xo[...], DEG_X)
    tyo = chebyshev(yo[...], DEG_Y)
    w, wd, wf, wg = wa[...], wda[...], wfa[...], wga[...]
    w_o, wd_o, wf_o, wg_o = wo[...], wdo[...], wfo[...], wgo[...]
    inv = [[si[pl.ds(j * 5 + i, 1), :] for i in range(5)] for j in range(5)]
    for p in range(DEG_X):
        for q in range(DEG_Y):
            m = p * DEG_Y + q
            b = tx[p] * ty[q]
            cp = (w * b).astype(bf).astype(f32)
            cq = (wd * b).astype(bf).astype(f32)
            cr = (wf * b).astype(bf).astype(f32)
            cs = (wg * b).astype(bf).astype(f32)
            for d, (k0, k1, last) in enumerate(((0, 2, cr), (1, 3, cs))):
                rows = pl.ds((d * terms + m) * n_all, n_all)
                sc = [(-(inv[j][k0] * cp + inv[j][k1] * cq + inv[j][4] * last)).astype(bf) for j in range(5)]
                for t, j in enumerate((0, 2, 4)):
                    rhs0[rows, pl.ds(t * LANES, LANES)] = sc[j]
                for t, j in enumerate((1, 3, 4)):
                    rhs1[rows, pl.ds(t * LANES, LANES)] = sc[j]
            bo = txo[p] * tyo[q]
            po = (w_o * bo).astype(bf).astype(f32)
            qo = (wd_o * bo).astype(bf).astype(f32)
            own_rows = pl.ds(m * n_own, n_own)
            lhs0[own_rows, pl.ds(0, LANES)] = po
            lhs0[own_rows, pl.ds(LANES, LANES)] = qo
            lhs0[own_rows, pl.ds(2 * LANES, LANES)] = (wf_o * bo).astype(bf).astype(f32)
            lhs1[own_rows, pl.ds(0, LANES)] = po
            lhs1[own_rows, pl.ds(LANES, LANES)] = qo
            lhs1[own_rows, pl.ds(2 * LANES, LANES)] = (wg_o * bo).astype(bf).astype(f32)
    out[0] += lax.dot_general(lhs0[...].astype(bf), rhs0[...], (((1,), (1,)), ((), ())), preferred_element_type=f32)
    out[1] += lax.dot_general(lhs1[...].astype(bf), rhs1[...], (((1,), (1,)), ((), ())), preferred_element_type=f32)

    @pl.when(step == pl.num_programs(0) - 1)
    def _():
        top = jnp.maximum(jnp.max(jnp.abs(out[0])), jnp.max(jnp.abs(out[1])))
        peak[...] = jnp.full(peak.shape, top, f32)


def schur_product(all_x, all_y, all_w, all_wd, all_wf, all_wg, own_x, own_y, own_w, own_wd, own_wf, own_wg, inverse):
    n_all, stars = all_x.shape
    n_own = own_x.shape[0]
    terms = DEG_X * DEG_Y
    rows_all = 2 * terms * n_all
    rows_own = terms * n_own
    all_spec = pl.BlockSpec((n_all, LANES), lambda k: (0, k))
    own_spec = pl.BlockSpec((n_own, LANES), lambda k: (0, k))
    inv_spec = pl.BlockSpec((25, LANES), lambda k: (0, k))
    return pl.pallas_call(
        schur_kernel,
        out_shape=(
            jax.ShapeDtypeStruct((2, rows_own, rows_all), jnp.float32),
            jax.ShapeDtypeStruct((8, LANES), jnp.float32),
        ),
        grid=(stars // LANES,),
        in_specs=[all_spec] * 6 + [own_spec] * 6 + [inv_spec],
        out_specs=(
            pl.BlockSpec((2, rows_own, rows_all), lambda k: (0, 0, 0)),
            pl.BlockSpec((8, LANES), lambda k: (0, 0)),
        ),
        scratch_shapes=[
            pltpu.VMEM((rows_all, 3 * LANES), jnp.bfloat16),
            pltpu.VMEM((rows_all, 3 * LANES), jnp.bfloat16),
            pltpu.VMEM((rows_own, 3 * LANES), jnp.float32),
            pltpu.VMEM((rows_own, 3 * LANES), jnp.float32),
        ],
        compiler_params=pltpu.CompilerParams(dimension_semantics=("arbitrary",)),
    )(all_x, all_y, all_w, all_wd, all_wf, all_wg, own_x, own_y, own_w, own_wd, own_wf, own_wg, inverse)


def on_device(
    pixel_uv,
    ccd_index,
    observed,
    obs_weight,
    obs_resid,
    star_inverse,
    star_count,
    ccd_center,
    exp_geom,
    tile_exposures,
    pair_owner,
):
    expo_total = lax.axis_size("expo")
    tile_total = lax.axis_size(TILE)
    expo_rank = lax.axis_index("expo")
    loc_dev = ccd_index.shape[0]
    window = tile_exposures.shape[1]
    params = 2 * DEG_X * DEG_Y
    live_rows = star_count[0]
    exposure_ids = lax.dynamic_slice_in_dim(tile_exposures[0], expo_rank * loc_dev, loc_dev)
    geometry, picked = geometry_of(exp_geom, exposure_ids)
    focal, live_weight = focal_weight(
        pixel_uv, ccd_index, observed, obs_weight, live_rows, ccd_center
    )
    basis = basis_of(focal)
    jacobian = jacobian_of(geometry)
    diagonal, weighted = diagonal_blocks(live_weight, basis)
    own_rows = expo_rank * loc_dev + jnp.arange(loc_dev, dtype=jnp.int32)
    local_rows = jnp.arange(loc_dev, dtype=jnp.int32)
    all_focal, all_weight, all_resid = turned_gather(
        (focal, live_weight, obs_resid), "expo", (1, 0, 1)
    )
    all_geometry, all_picked = geometry_of(exp_geom, tile_exposures[0])
    all_jacobian = jacobian_of(all_geometry)
    all_x, all_y = all_focal[0], all_focal[1]
    own_x, own_y = focal[0], focal[1]
    products, peak = schur_product(
        all_x, all_y, all_weight,
        all_weight * all_geometry[0][:, None], all_weight * all_geometry[1][:, None], all_weight * all_geometry[2][:, None],
        own_x, own_y, live_weight,
        live_weight * geometry[0][:, None], live_weight * geometry[1][:, None], live_weight * geometry[2][:, None],
        star_inverse.reshape(25, -1),
    )
    terms = DEG_X * DEG_Y
    product = products.reshape(2, terms, loc_dev, params, window)
    product = jnp.transpose(product, (2, 4, 0, 1, 3)).reshape(loc_dev, window, params * params)
    on_diagonal = own_rows[:, None] == jnp.arange(window, dtype=jnp.int32)[None, :]
    diagonal_flat = diagonal.reshape(loc_dev, 1, params * params)
    product = product + jnp.where(on_diagonal[:, :, None], diagonal_flat, 0.0)
    product = product.reshape(loc_dev * window, params * params)
    bound = peak[0, 0] + jnp.max(jnp.abs(diagonal))
    bound = jnp.where(bound > 0.0, bound, 1.0)
    product = (product * (1.0 / bound)).astype(jnp.float16)
    owners = lax.dynamic_slice_in_dim(pair_owner[0], expo_rank * loc_dev, loc_dev, 0)
    gradient = gradient_terms(all_jacobian, all_weight, all_resid)
    solved = jnp.einsum("jis,is->js", star_inverse, gradient, precision=highest)
    rhs_local = local_rhs(weighted, jacobian, obs_resid, solved)
    devices = tile_total * expo_total
    spread = jnp.dot(picked, rhs_local, precision=highest).reshape(devices, -1)
    pair_dev = 3 * (window // 2) * (window // 2) // expo_total
    flat_owner = owners.reshape(-1)
    target = flat_owner // pair_dev
    ranking = jnp.argsort(target, stable=True)
    per_peer = flat_owner.shape[0] // devices
    outgoing = jnp.take(product, ranking.reshape(devices, per_peer), axis=0, mode="clip")
    slot_tags = (flat_owner % pair_dev)[ranking].reshape(devices, per_peer).astype(jnp.float32)
    sent_scale = jnp.full((devices, 1), bound, jnp.float32)
    small = jnp.concatenate([spread, slot_tags, sent_scale], axis=1)
    incoming_blocks = lax.all_to_all(outgoing, TILE_EXPO, split_axis=0, concat_axis=0, tiled=True)
    incoming_small = lax.all_to_all(small, TILE_EXPO, split_axis=0, concat_axis=0, tiled=True)
    incoming_rhs = incoming_small[:, : spread.shape[1]]
    incoming_tags = incoming_small[:, spread.shape[1] : spread.shape[1] + per_peer].astype(jnp.int32)
    incoming_scale = jnp.broadcast_to(incoming_small[:, spread.shape[1] + per_peer :], (devices, per_peer))
    receive_slots = jnp.where(
        jnp.arange(pair_dev, dtype=jnp.int32)[:, None] == incoming_tags.reshape(1, -1),
        incoming_scale.reshape(1, -1),
        0.0,
    )
    incoming_blocks = incoming_blocks.astype(jnp.float32)
    receive_slots = receive_slots.reshape(pair_dev, devices, per_peer)
    pair_blocks = lax.dot_general(
        receive_slots, incoming_blocks, (((1, 2), (0, 1)), ((), ())), precision=highest
    )
    reduced_rhs = jnp.sum(incoming_rhs.reshape(devices, -1, params), axis=0)
    return (pair_blocks, reduced_rhs)


def solution(mesh):
    split = Mesh(
        mesh.devices.reshape(4, 4, 2, mesh.shape["expo"]), ("tile_0", "tile_1", "tile_2", "expo")
    )
    placed = (
        P(None, "expo", TILE),
        P("expo", TILE),
        P("expo", TILE),
        P("expo", TILE),
        P(None, "expo", TILE),
        P(None, None, TILE),
        P(TILE),
        P(),
        P(),
        P(TILE, None),
        P(TILE, None, None),
    )
    return jax.shard_map(
        on_device,
        mesh=split,
        in_specs=placed,
        out_specs=(P(TILE_EXPO, None), P(TILE_EXPO, None)),
        check_vma=False,
    )
```

```python
import jax
import jax.numpy as jnp
from jax import lax
from jax.experimental import pallas as pl
from jax.experimental.pallas import tpu as pltpu
from jax.sharding import Mesh
from jax.sharding import PartitionSpec as P

DEG_X = 6
DEG_Y = 5
TILE = ("tile_0", "tile_1", "tile_2")
TILE_EXPO = ("tile_0", "tile_1", "tile_2", "expo")


highest = lax.Precision.HIGHEST
contract = (((1, 2), (1, 2)), ((), ()))


def turned_gather(arrays, axis, dims):
    turned = [jnp.moveaxis(a, dim, 0) for a, dim in zip(arrays, dims)]
    both = jnp.concatenate([t.reshape(len(t), -1) for t in turned], axis=1)
    count = lax.axis_size(axis)
    rank = lax.axis_index(axis)
    filled = jnp.zeros((count * both.shape[0], both.shape[1]), both.dtype)
    for shift in range(count):
        if shift == 0:
            piece = both
        else:
            piece = lax.ppermute(both, axis, [(i, (i + shift) % count) for i in range(count)])
        source = (rank + count - shift) % count
        filled = lax.dynamic_update_slice_in_dim(filled, piece, source * both.shape[0], axis=0)
    at, done = (0, [])
    for t, dim in zip(turned, dims):
        piece = filled[:, at : at + t[0].size].reshape(-1, *t.shape[1:])
        done.append(jnp.moveaxis(piece, 0, dim))
        at += t[0].size
    return tuple(done)


def sum_in_order(tiles, axes, order):
    inside = tiles.shape[1:]
    tiles = tiles.reshape(*(lax.axis_size(a) for a in axes), *inside)
    tiles = jnp.moveaxis(tiles, order, range(len(axes))).reshape(-1, *inside)
    for k in order:
        tiles = lax.psum_scatter(tiles, axes[k], scatter_dimension=0, tiled=True)
    return tiles[0]


def split_up(array, dim, length):
    before, after = (array.shape[:dim], array.shape[dim + 1 :])
    return jnp.moveaxis(array.reshape(*before, length, -1, *after), dim, 0)


def scatter_axes(array, axes, order, dim):
    length = lax.axis_size(axes)
    return sum_in_order(split_up(array, dim, length), axes, order)


def chebyshev(values, degree):
    series = [jnp.ones_like(values), values]
    for degree_at in range(2, degree):
        series.append(2.0 * values * series[-1] - series[-2])
    return series[:degree]


def focal_weight(pixel_uv, ccd_index, observed, obs_weight, live_rows, ccd_center):
    ccd_total = ccd_center.shape[1]
    picked = (
        ccd_index[None, :, :] == jnp.arange(ccd_total, dtype=jnp.int32)[:, None, None]
    ).astype(jnp.float32)
    centre = jnp.sum(ccd_center[:, :, None, None] * picked[None], axis=1)
    focal = 0.75 * centre + 0.25 * pixel_uv
    star_rows = ccd_index.shape[1]
    alive = (jnp.arange(star_rows, dtype=jnp.int32)[None, :] < live_rows).astype(jnp.float32)
    live_weight = obs_weight * observed.astype(jnp.float32) * alive
    return (focal, live_weight)


def basis_of(focal):
    along_first = chebyshev(focal[0], DEG_X)
    along_second = chebyshev(focal[1], DEG_Y)
    return jnp.stack(
        [first_term * second_term for first_term in along_first for second_term in along_second],
        axis=1,
    )


def jacobian_of(geometry):
    shift_time = geometry[0]
    factor_first = geometry[1]
    factor_second = geometry[2]
    unit_row = jnp.ones_like(shift_time)
    zero_row = jnp.zeros_like(shift_time)
    return jnp.stack(
        [
            jnp.stack([unit_row, zero_row, shift_time, zero_row, factor_first], axis=-1),
            jnp.stack([zero_row, unit_row, zero_row, shift_time, factor_second], axis=-1),
        ],
        axis=1,
    )


def geometry_of(exp_geom, exposure_ids):
    picked = (
        jnp.arange(exp_geom.shape[1], dtype=jnp.int32)[:, None] == exposure_ids[None, :]
    ).astype(jnp.float32)
    return (jnp.sum(exp_geom[:, :, None] * picked[None], axis=1), picked)


def coupling_matrix(live_weight, basis, jacobian):
    full = (
        live_weight[:, None, None, None, :]
        * jacobian[:, :, None, :, None]
        * basis[:, None, :, None, :]
    )
    return full.astype(jnp.bfloat16).reshape(basis.shape[0] * 2 * basis.shape[1], 5, basis.shape[2])


def negated_scaled(coupling, inverse):
    return (
        -jnp.einsum("xis,jis->xjs", coupling.astype(jnp.float32), inverse, precision=highest)
    ).astype(jnp.bfloat16)


def diagonal_blocks(live_weight, basis):
    weighted = live_weight[:, None, :] * basis
    gram = jnp.einsum("ams,ans->amn", weighted, basis, precision=highest)
    pair_eye = jnp.eye(2, dtype=jnp.float32)
    full = jnp.einsum("cd,amn->acmdn", pair_eye, gram, precision=highest)
    return (full.reshape(gram.shape[0], 2 * gram.shape[1], 2 * gram.shape[1]), weighted)


def gradient_terms(jacobian, live_weight, obs_resid):
    return jnp.einsum("aci,as,cas->is", jacobian, live_weight, obs_resid, precision=highest)


def local_rhs(weighted, jacobian, obs_resid, solved):
    correction = jnp.einsum("aci,is->cas", jacobian, solved, precision=highest)
    result = jnp.einsum("ams,cas->acm", weighted, obs_resid - correction, precision=highest)
    return result.reshape(weighted.shape[0], 2 * weighted.shape[1])


def star_product(former, latter):
    return lax.dot_general(former, latter, contract, preferred_element_type=jnp.float32)


LANES = 512


def schur_kernel(xa, ya, wa, wda, wfa, wga, xo, yo, wo, wdo, wfo, wgo, si, out, peak, rhs0, rhs1, lhs0, lhs1):
    step = pl.program_id(0)
    bf = jnp.bfloat16
    f32 = jnp.float32
    n_all = xa.shape[0]
    n_own = xo.shape[0]
    terms = DEG_X * DEG_Y

    @pl.when(step == 0)
    def _():
        out[...] = jnp.zeros_like(out)

    tx = chebyshev(xa[...], DEG_X)
    ty = chebyshev(ya[...], DEG_Y)
    txo = chebyshev(xo[...], DEG_X)
    tyo = chebyshev(yo[...], DEG_Y)
    w, wd, wf, wg = wa[...], wda[...], wfa[...], wga[...]
    w_o, wd_o, wf_o, wg_o = wo[...], wdo[...], wfo[...], wgo[...]
    inv = [[si[pl.ds(j * 5 + i, 1), :] for i in range(5)] for j in range(5)]
    for p in range(DEG_X):
        for q in range(DEG_Y):
            m = p * DEG_Y + q
            b = tx[p] * ty[q]
            cp = (w * b).astype(bf).astype(f32)
            cq = (wd * b).astype(bf).astype(f32)
            cr = (wf * b).astype(bf).astype(f32)
            cs = (wg * b).astype(bf).astype(f32)
            for d, (k0, k1, last) in enumerate(((0, 2, cr), (1, 3, cs))):
                rows = pl.ds((d * terms + m) * n_all, n_all)
                sc = [(-(inv[j][k0] * cp + inv[j][k1] * cq + inv[j][4] * last)).astype(bf) for j in range(5)]
                for t, j in enumerate((0, 2, 4)):
                    rhs0[rows, pl.ds(t * LANES, LANES)] = sc[j]
                for t, j in enumerate((1, 3, 4)):
                    rhs1[rows, pl.ds(t * LANES, LANES)] = sc[j]
            bo = txo[p] * tyo[q]
            po = (w_o * bo).astype(bf).astype(f32)
            qo = (wd_o * bo).astype(bf).astype(f32)
            own_rows = pl.ds(m * n_own, n_own)
            lhs0[own_rows, pl.ds(0, LANES)] = po
            lhs0[own_rows, pl.ds(LANES, LANES)] = qo
            lhs0[own_rows, pl.ds(2 * LANES, LANES)] = (wf_o * bo).astype(bf).astype(f32)
            lhs1[own_rows, pl.ds(0, LANES)] = po
            lhs1[own_rows, pl.ds(LANES, LANES)] = qo
            lhs1[own_rows, pl.ds(2 * LANES, LANES)] = (wg_o * bo).astype(bf).astype(f32)
    out[0] += lax.dot_general(lhs0[...].astype(bf), rhs0[...], (((1,), (1,)), ((), ())), preferred_element_type=f32)
    out[1] += lax.dot_general(lhs1[...].astype(bf), rhs1[...], (((1,), (1,)), ((), ())), preferred_element_type=f32)

    @pl.when(step == pl.num_programs(0) - 1)
    def _():
        top = jnp.maximum(jnp.max(jnp.abs(out[0])), jnp.max(jnp.abs(out[1])))
        peak[...] = jnp.full(peak.shape, top, f32)


def schur_product(all_x, all_y, all_w, all_wd, all_wf, all_wg, own_x, own_y, own_w, own_wd, own_wf, own_wg, inverse):
    n_all, stars = all_x.shape
    n_own = own_x.shape[0]
    terms = DEG_X * DEG_Y
    rows_all = 2 * terms * n_all
    rows_own = terms * n_own
    all_spec = pl.BlockSpec((n_all, LANES), lambda k: (0, k))
    own_spec = pl.BlockSpec((n_own, LANES), lambda k: (0, k))
    inv_spec = pl.BlockSpec((25, LANES), lambda k: (0, k))
    return pl.pallas_call(
        schur_kernel,
        out_shape=(
            jax.ShapeDtypeStruct((2, rows_own, rows_all), jnp.float32),
            jax.ShapeDtypeStruct((8, LANES), jnp.float32),
        ),
        grid=(stars // LANES,),
        in_specs=[all_spec] * 6 + [own_spec] * 6 + [inv_spec],
        out_specs=(
            pl.BlockSpec((2, rows_own, rows_all), lambda k: (0, 0, 0)),
            pl.BlockSpec((8, LANES), lambda k: (0, 0)),
        ),
        scratch_shapes=[
            pltpu.VMEM((rows_all, 3 * LANES), jnp.bfloat16),
            pltpu.VMEM((rows_all, 3 * LANES), jnp.bfloat16),
            pltpu.VMEM((rows_own, 3 * LANES), jnp.float32),
            pltpu.VMEM((rows_own, 3 * LANES), jnp.float32),
        ],
        compiler_params=pltpu.CompilerParams(dimension_semantics=("arbitrary",)),
    )(all_x, all_y, all_w, all_wd, all_wf, all_wg, own_x, own_y, own_w, own_wd, own_wf, own_wg, inverse)


def on_device(
    pixel_uv,
    ccd_index,
    observed,
    obs_weight,
    obs_resid,
    star_inverse,
    star_count,
    ccd_center,
    exp_geom,
    tile_exposures,
    pair_owner,
):
    expo_total = lax.axis_size("expo")
    tile_total = lax.axis_size(TILE)
    expo_rank = lax.axis_index("expo")
    loc_dev = ccd_index.shape[0]
    window = tile_exposures.shape[1]
    params = 2 * DEG_X * DEG_Y
    live_rows = star_count[0]
    exposure_ids = lax.dynamic_slice_in_dim(tile_exposures[0], expo_rank * loc_dev, loc_dev)
    geometry, picked = geometry_of(exp_geom, exposure_ids)
    focal, live_weight = focal_weight(
        pixel_uv, ccd_index, observed, obs_weight, live_rows, ccd_center
    )
    basis = basis_of(focal)
    jacobian = jacobian_of(geometry)
    diagonal, weighted = diagonal_blocks(live_weight, basis)
    own_rows = expo_rank * loc_dev + jnp.arange(loc_dev, dtype=jnp.int32)
    local_rows = jnp.arange(loc_dev, dtype=jnp.int32)
    all_focal, all_weight, all_resid = turned_gather(
        (focal, live_weight, obs_resid), "expo", (1, 0, 1)
    )
    all_geometry, all_picked = geometry_of(exp_geom, tile_exposures[0])
    all_jacobian = jacobian_of(all_geometry)
    all_x, all_y = all_focal[0], all_focal[1]
    own_x, own_y = focal[0], focal[1]
    products, peak = schur_product(
        all_x, all_y, all_weight,
        all_weight * all_geometry[0][:, None], all_weight * all_geometry[1][:, None], all_weight * all_geometry[2][:, None],
        own_x, own_y, live_weight,
        live_weight * geometry[0][:, None], live_weight * geometry[1][:, None], live_weight * geometry[2][:, None],
        star_inverse.reshape(25, -1),
    )
    terms = DEG_X * DEG_Y
    product = products.reshape(2, terms, loc_dev, params, window)
    product = jnp.transpose(product, (2, 4, 0, 1, 3)).reshape(loc_dev, window, params * params)
    on_diagonal = own_rows[:, None] == jnp.arange(window, dtype=jnp.int32)[None, :]
    diagonal_flat = diagonal.reshape(loc_dev, 1, params * params)
    product = product + jnp.where(on_diagonal[:, :, None], diagonal_flat, 0.0)
    product = product.reshape(loc_dev * window, params * params)
    bound = peak[0, 0] + jnp.max(jnp.abs(diagonal))
    bound = jnp.where(bound > 0.0, bound, 1.0)
    product = (product * (1.0 / bound)).astype(jnp.float16)
    owners = lax.dynamic_slice_in_dim(pair_owner[0], expo_rank * loc_dev, loc_dev, 0)
    gradient = gradient_terms(all_jacobian, all_weight, all_resid)
    solved = jnp.einsum("jis,is->js", star_inverse, gradient, precision=highest)
    rhs_local = local_rhs(weighted, jacobian, obs_resid, solved)
    devices = tile_total * expo_total
    spread = jnp.dot(picked, rhs_local, precision=highest).reshape(devices, -1)
    pair_dev = 3 * (window // 2) * (window // 2) // expo_total
    flat_owner = owners.reshape(-1)
    target = flat_owner // pair_dev
    ranking = jnp.argsort(target, stable=True)
    per_peer = flat_owner.shape[0] // devices
    outgoing = jnp.take(product, ranking.reshape(devices, per_peer), axis=0, mode="clip")
    slot_tags = (flat_owner % pair_dev)[ranking].reshape(devices, per_peer).astype(jnp.float32)
    sent_scale = jnp.full((devices, 1), bound, jnp.float32)
    small = jnp.concatenate([spread, slot_tags, sent_scale], axis=1)
    incoming_blocks = lax.all_to_all(outgoing, TILE_EXPO, split_axis=0, concat_axis=0, tiled=True)
    incoming_small = lax.all_to_all(small, TILE_EXPO, split_axis=0, concat_axis=0, tiled=True)
    incoming_rhs = incoming_small[:, : spread.shape[1]]
    incoming_tags = incoming_small[:, spread.shape[1] : spread.shape[1] + per_peer].astype(jnp.int32)
    incoming_scale = jnp.broadcast_to(incoming_small[:, spread.shape[1] + per_peer :], (devices, per_peer))
    receive_slots = jnp.where(
        jnp.arange(pair_dev, dtype=jnp.int32)[:, None] == incoming_tags.reshape(1, -1),
        incoming_scale.reshape(1, -1),
        0.0,
    )
    incoming_blocks = incoming_blocks.astype(jnp.float32)
    receive_slots = receive_slots.reshape(pair_dev, devices, per_peer)
    pair_blocks = lax.dot_general(
        receive_slots, incoming_blocks, (((1, 2), (0, 1)), ((), ())), precision=highest
    )
    reduced_rhs = jnp.sum(incoming_rhs.reshape(devices, -1, params), axis=0)
    return (pair_blocks, reduced_rhs)


def solution(mesh):
    split = Mesh(
        mesh.devices.reshape(4, 4, 2, mesh.shape["expo"]), ("tile_0", "tile_1", "tile_2", "expo")
    )
    placed = (
        P(None, "expo", TILE),
        P("expo", TILE),
        P("expo", TILE),
        P("expo", TILE),
        P(None, "expo", TILE),
        P(None, None, TILE),
        P(TILE),
        P(),
        P(),
        P(TILE, None),
        P(TILE, None, None),
    )
    return jax.shard_map(
        on_device,
        mesh=split,
        in_specs=placed,
        out_specs=(P(TILE_EXPO, None), P(TILE_EXPO, None)),
        check_vma=False,
    )
```

```python
import jax
import jax.numpy as jnp
from jax import lax
from jax.experimental import pallas as pl
from jax.experimental.pallas import tpu as pltpu
from jax.sharding import Mesh
from jax.sharding import PartitionSpec as P

DEG_X = 6
DEG_Y = 5
TILE = ("tile_0", "tile_1", "tile_2")
TILE_EXPO = ("tile_0", "tile_1", "tile_2", "expo")


highest = lax.Precision.HIGHEST
contract = (((1, 2), (1, 2)), ((), ()))


def turned_gather(arrays, axis, dims):
    turned = [jnp.moveaxis(a, dim, 0) for a, dim in zip(arrays, dims)]
    both = jnp.concatenate([t.reshape(len(t), -1) for t in turned], axis=1)
    count = lax.axis_size(axis)
    rank = lax.axis_index(axis)
    filled = jnp.zeros((count * both.shape[0], both.shape[1]), both.dtype)
    for shift in range(count):
        if shift == 0:
            piece = both
        else:
            piece = lax.ppermute(both, axis, [(i, (i + shift) % count) for i in range(count)])
        source = (rank + count - shift) % count
        filled = lax.dynamic_update_slice_in_dim(filled, piece, source * both.shape[0], axis=0)
    at, done = (0, [])
    for t, dim in zip(turned, dims):
        piece = filled[:, at : at + t[0].size].reshape(-1, *t.shape[1:])
        done.append(jnp.moveaxis(piece, 0, dim))
        at += t[0].size
    return tuple(done)


def sum_in_order(tiles, axes, order):
    inside = tiles.shape[1:]
    tiles = tiles.reshape(*(lax.axis_size(a) for a in axes), *inside)
    tiles = jnp.moveaxis(tiles, order, range(len(axes))).reshape(-1, *inside)
    for k in order:
        tiles = lax.psum_scatter(tiles, axes[k], scatter_dimension=0, tiled=True)
    return tiles[0]


def split_up(array, dim, length):
    before, after = (array.shape[:dim], array.shape[dim + 1 :])
    return jnp.moveaxis(array.reshape(*before, length, -1, *after), dim, 0)


def scatter_axes(array, axes, order, dim):
    length = lax.axis_size(axes)
    return sum_in_order(split_up(array, dim, length), axes, order)


def chebyshev(values, degree):
    series = [jnp.ones_like(values), values]
    for degree_at in range(2, degree):
        series.append(2.0 * values * series[-1] - series[-2])
    return series[:degree]


def focal_weight(pixel_uv, ccd_index, observed, obs_weight, live_rows, ccd_center):
    ccd_total = ccd_center.shape[1]
    picked = (
        ccd_index[None, :, :] == jnp.arange(ccd_total, dtype=jnp.int32)[:, None, None]
    ).astype(jnp.float32)
    centre = jnp.sum(ccd_center[:, :, None, None] * picked[None], axis=1)
    focal = 0.75 * centre + 0.25 * pixel_uv
    star_rows = ccd_index.shape[1]
    alive = (jnp.arange(star_rows, dtype=jnp.int32)[None, :] < live_rows).astype(jnp.float32)
    live_weight = obs_weight * observed.astype(jnp.float32) * alive
    return (focal, live_weight)


def basis_of(focal):
    along_first = chebyshev(focal[0], DEG_X)
    along_second = chebyshev(focal[1], DEG_Y)
    return jnp.stack(
        [first_term * second_term for first_term in along_first for second_term in along_second],
        axis=1,
    )


def jacobian_of(geometry):
    shift_time = geometry[0]
    factor_first = geometry[1]
    factor_second = geometry[2]
    unit_row = jnp.ones_like(shift_time)
    zero_row = jnp.zeros_like(shift_time)
    return jnp.stack(
        [
            jnp.stack([unit_row, zero_row, shift_time, zero_row, factor_first], axis=-1),
            jnp.stack([zero_row, unit_row, zero_row, shift_time, factor_second], axis=-1),
        ],
        axis=1,
    )


def geometry_of(exp_geom, exposure_ids):
    picked = (
        jnp.arange(exp_geom.shape[1], dtype=jnp.int32)[:, None] == exposure_ids[None, :]
    ).astype(jnp.float32)
    return (jnp.sum(exp_geom[:, :, None] * picked[None], axis=1), picked)


def coupling_matrix(live_weight, basis, jacobian):
    full = (
        live_weight[:, None, None, None, :]
        * jacobian[:, :, None, :, None]
        * basis[:, None, :, None, :]
    )
    return full.astype(jnp.bfloat16).reshape(basis.shape[0] * 2 * basis.shape[1], 5, basis.shape[2])


def negated_scaled(coupling, inverse):
    return (
        -jnp.einsum("xis,jis->xjs", coupling.astype(jnp.float32), inverse, precision=highest)
    ).astype(jnp.bfloat16)


def diagonal_blocks(live_weight, basis):
    weighted = live_weight[:, None, :] * basis
    gram = jnp.einsum("ams,ans->amn", weighted, basis, precision=highest)
    pair_eye = jnp.eye(2, dtype=jnp.float32)
    full = jnp.einsum("cd,amn->acmdn", pair_eye, gram, precision=highest)
    return (full.reshape(gram.shape[0], 2 * gram.shape[1], 2 * gram.shape[1]), weighted)


def gradient_terms(jacobian, live_weight, obs_resid):
    return jnp.einsum("aci,as,cas->is", jacobian, live_weight, obs_resid, precision=highest)


def local_rhs(weighted, jacobian, obs_resid, solved):
    correction = jnp.einsum("aci,is->cas", jacobian, solved, precision=highest)
    result = jnp.einsum("ams,cas->acm", weighted, obs_resid - correction, precision=highest)
    return result.reshape(weighted.shape[0], 2 * weighted.shape[1])


def star_product(former, latter):
    return lax.dot_general(former, latter, contract, preferred_element_type=jnp.float32)


LANES = 1024


def schur_kernel(xa, ya, wa, wda, wfa, wga, xo, yo, wo, wdo, wfo, wgo, si, out, peak, rhs0, rhs1, lhs0, lhs1):
    step = pl.program_id(0)
    bf = jnp.bfloat16
    f32 = jnp.float32
    n_all = xa.shape[0]
    n_own = xo.shape[0]
    terms = DEG_X * DEG_Y

    @pl.when(step == 0)
    def _():
        out[...] = jnp.zeros_like(out)

    tx = chebyshev(xa[...], DEG_X)
    ty = chebyshev(ya[...], DEG_Y)
    txo = chebyshev(xo[...], DEG_X)
    tyo = chebyshev(yo[...], DEG_Y)
    w, wd, wf, wg = wa[...], wda[...], wfa[...], wga[...]
    w_o, wd_o, wf_o, wg_o = wo[...], wdo[...], wfo[...], wgo[...]
    inv = [[si[pl.ds(j * 5 + i, 1), :] for i in range(5)] for j in range(5)]
    for p in range(DEG_X):
        for q in range(DEG_Y):
            m = p * DEG_Y + q
            b = tx[p] * ty[q]
            cp = (w * b).astype(bf).astype(f32)
            cq = (wd * b).astype(bf).astype(f32)
            cr = (wf * b).astype(bf).astype(f32)
            cs = (wg * b).astype(bf).astype(f32)
            for d, (k0, k1, last) in enumerate(((0, 2, cr), (1, 3, cs))):
                rows = pl.ds((d * terms + m) * n_all, n_all)
                sc = [(-(inv[j][k0] * cp + inv[j][k1] * cq + inv[j][4] * last)).astype(bf) for j in range(5)]
                for t, j in enumerate((0, 2, 4)):
                    rhs0[rows, pl.ds(t * LANES, LANES)] = sc[j]
                for t, j in enumerate((1, 3, 4)):
                    rhs1[rows, pl.ds(t * LANES, LANES)] = sc[j]
            bo = txo[p] * tyo[q]
            po = (w_o * bo).astype(bf).astype(f32)
            qo = (wd_o * bo).astype(bf).astype(f32)
            own_rows = pl.ds(m * n_own, n_own)
            lhs0[own_rows, pl.ds(0, LANES)] = po
            lhs0[own_rows, pl.ds(LANES, LANES)] = qo
            lhs0[own_rows, pl.ds(2 * LANES, LANES)] = (wf_o * bo).astype(bf).astype(f32)
            lhs1[own_rows, pl.ds(0, LANES)] = po
            lhs1[own_rows, pl.ds(LANES, LANES)] = qo
            lhs1[own_rows, pl.ds(2 * LANES, LANES)] = (wg_o * bo).astype(bf).astype(f32)
    out[0] += lax.dot_general(lhs0[...].astype(bf), rhs0[...], (((1,), (1,)), ((), ())), preferred_element_type=f32)
    out[1] += lax.dot_general(lhs1[...].astype(bf), rhs1[...], (((1,), (1,)), ((), ())), preferred_element_type=f32)

    @pl.when(step == pl.num_programs(0) - 1)
    def _():
        top = jnp.maximum(jnp.max(jnp.abs(out[0])), jnp.max(jnp.abs(out[1])))
        peak[...] = jnp.full(peak.shape, top, f32)


def schur_product(all_x, all_y, all_w, all_wd, all_wf, all_wg, own_x, own_y, own_w, own_wd, own_wf, own_wg, inverse):
    n_all, stars = all_x.shape
    n_own = own_x.shape[0]
    terms = DEG_X * DEG_Y
    rows_all = 2 * terms * n_all
    rows_own = terms * n_own
    all_spec = pl.BlockSpec((n_all, LANES), lambda k: (0, k))
    own_spec = pl.BlockSpec((n_own, LANES), lambda k: (0, k))
    inv_spec = pl.BlockSpec((25, LANES), lambda k: (0, k))
    return pl.pallas_call(
        schur_kernel,
        out_shape=(
            jax.ShapeDtypeStruct((2, rows_own, rows_all), jnp.float32),
            jax.ShapeDtypeStruct((8, LANES), jnp.float32),
        ),
        grid=(stars // LANES,),
        in_specs=[all_spec] * 6 + [own_spec] * 6 + [inv_spec],
        out_specs=(
            pl.BlockSpec((2, rows_own, rows_all), lambda k: (0, 0, 0)),
            pl.BlockSpec((8, LANES), lambda k: (0, 0)),
        ),
        scratch_shapes=[
            pltpu.VMEM((rows_all, 3 * LANES), jnp.bfloat16),
            pltpu.VMEM((rows_all, 3 * LANES), jnp.bfloat16),
            pltpu.VMEM((rows_own, 3 * LANES), jnp.float32),
            pltpu.VMEM((rows_own, 3 * LANES), jnp.float32),
        ],
        compiler_params=pltpu.CompilerParams(dimension_semantics=("arbitrary",)),
    )(all_x, all_y, all_w, all_wd, all_wf, all_wg, own_x, own_y, own_w, own_wd, own_wf, own_wg, inverse)


def on_device(
    pixel_uv,
    ccd_index,
    observed,
    obs_weight,
    obs_resid,
    star_inverse,
    star_count,
    ccd_center,
    exp_geom,
    tile_exposures,
    pair_owner,
):
    expo_total = lax.axis_size("expo")
    tile_total = lax.axis_size(TILE)
    expo_rank = lax.axis_index("expo")
    loc_dev = ccd_index.shape[0]
    window = tile_exposures.shape[1]
    params = 2 * DEG_X * DEG_Y
    live_rows = star_count[0]
    exposure_ids = lax.dynamic_slice_in_dim(tile_exposures[0], expo_rank * loc_dev, loc_dev)
    geometry, picked = geometry_of(exp_geom, exposure_ids)
    focal, live_weight = focal_weight(
        pixel_uv, ccd_index, observed, obs_weight, live_rows, ccd_center
    )
    basis = basis_of(focal)
    jacobian = jacobian_of(geometry)
    diagonal, weighted = diagonal_blocks(live_weight, basis)
    own_rows = expo_rank * loc_dev + jnp.arange(loc_dev, dtype=jnp.int32)
    local_rows = jnp.arange(loc_dev, dtype=jnp.int32)
    all_focal, all_weight, all_resid = turned_gather(
        (focal, live_weight, obs_resid), "expo", (1, 0, 1)
    )
    all_geometry, all_picked = geometry_of(exp_geom, tile_exposures[0])
    all_jacobian = jacobian_of(all_geometry)
    all_x, all_y = all_focal[0], all_focal[1]
    own_x, own_y = focal[0], focal[1]
    products, peak = schur_product(
        all_x, all_y, all_weight,
        all_weight * all_geometry[0][:, None], all_weight * all_geometry[1][:, None], all_weight * all_geometry[2][:, None],
        own_x, own_y, live_weight,
        live_weight * geometry[0][:, None], live_weight * geometry[1][:, None], live_weight * geometry[2][:, None],
        star_inverse.reshape(25, -1),
    )
    terms = DEG_X * DEG_Y
    product = products.reshape(2, terms, loc_dev, params, window)
    product = jnp.transpose(product, (2, 4, 0, 1, 3)).reshape(loc_dev, window, params * params)
    on_diagonal = own_rows[:, None] == jnp.arange(window, dtype=jnp.int32)[None, :]
    diagonal_flat = diagonal.reshape(loc_dev, 1, params * params)
    product = product + jnp.where(on_diagonal[:, :, None], diagonal_flat, 0.0)
    product = product.reshape(loc_dev * window, params * params)
    bound = peak[0, 0] + jnp.max(jnp.abs(diagonal))
    bound = jnp.where(bound > 0.0, bound, 1.0)
    product = (product * (1.0 / bound)).astype(jnp.float16)
    owners = lax.dynamic_slice_in_dim(pair_owner[0], expo_rank * loc_dev, loc_dev, 0)
    gradient = gradient_terms(all_jacobian, all_weight, all_resid)
    solved = jnp.einsum("jis,is->js", star_inverse, gradient, precision=highest)
    rhs_local = local_rhs(weighted, jacobian, obs_resid, solved)
    devices = tile_total * expo_total
    spread = jnp.dot(picked, rhs_local, precision=highest).reshape(devices, -1)
    pair_dev = 3 * (window // 2) * (window // 2) // expo_total
    flat_owner = owners.reshape(-1)
    target = flat_owner // pair_dev
    ranking = jnp.argsort(target, stable=True)
    per_peer = flat_owner.shape[0] // devices
    outgoing = jnp.take(product, ranking.reshape(devices, per_peer), axis=0, mode="clip")
    slot_tags = (flat_owner % pair_dev)[ranking].reshape(devices, per_peer).astype(jnp.float32)
    sent_scale = jnp.full((devices, 1), bound, jnp.float32)
    small = jnp.concatenate([spread, slot_tags, sent_scale], axis=1)
    incoming_blocks = lax.all_to_all(outgoing, TILE_EXPO, split_axis=0, concat_axis=0, tiled=True)
    incoming_small = lax.all_to_all(small, TILE_EXPO, split_axis=0, concat_axis=0, tiled=True)
    incoming_rhs = incoming_small[:, : spread.shape[1]]
    incoming_tags = incoming_small[:, spread.shape[1] : spread.shape[1] + per_peer].astype(jnp.int32)
    incoming_scale = jnp.broadcast_to(incoming_small[:, spread.shape[1] + per_peer :], (devices, per_peer))
    receive_slots = jnp.where(
        jnp.arange(pair_dev, dtype=jnp.int32)[:, None] == incoming_tags.reshape(1, -1),
        incoming_scale.reshape(1, -1),
        0.0,
    )
    incoming_blocks = incoming_blocks.astype(jnp.float32)
    receive_slots = receive_slots.reshape(pair_dev, devices, per_peer)
    pair_blocks = lax.dot_general(
        receive_slots, incoming_blocks, (((1, 2), (0, 1)), ((), ())), precision=lax.Precision.HIGH
    )
    reduced_rhs = jnp.sum(incoming_rhs.reshape(devices, -1, params), axis=0)
    return (pair_blocks, reduced_rhs)


def solution(mesh):
    split = Mesh(
        mesh.devices.reshape(4, 4, 2, mesh.shape["expo"]), ("tile_0", "tile_1", "tile_2", "expo")
    )
    placed = (
        P(None, "expo", TILE),
        P("expo", TILE),
        P("expo", TILE),
        P("expo", TILE),
        P(None, "expo", TILE),
        P(None, None, TILE),
        P(TILE),
        P(),
        P(),
        P(TILE, None),
        P(TILE, None, None),
    )
    return jax.shard_map(
        on_device,
        mesh=split,
        in_specs=placed,
        out_specs=(P(TILE_EXPO, None), P(TILE_EXPO, None)),
        check_vma=False,
    )
```

```python
import jax
import jax.numpy as jnp
from jax import lax
from jax.experimental import pallas as pl
from jax.experimental.pallas import tpu as pltpu
from jax.sharding import Mesh
from jax.sharding import PartitionSpec as P

DEG_X = 6
DEG_Y = 5
TILE = ("tile_0", "tile_1", "tile_2")
TILE_EXPO = ("tile_0", "tile_1", "tile_2", "expo")


highest = lax.Precision.HIGHEST
contract = (((1, 2), (1, 2)), ((), ()))


def turned_gather(arrays, axis, dims):
    turned = [jnp.moveaxis(a, dim, 0) for a, dim in zip(arrays, dims)]
    both = jnp.concatenate([t.reshape(len(t), -1) for t in turned], axis=1)
    count = lax.axis_size(axis)
    rank = lax.axis_index(axis)
    filled = jnp.zeros((count * both.shape[0], both.shape[1]), both.dtype)
    for shift in range(count):
        if shift == 0:
            piece = both
        else:
            piece = lax.ppermute(both, axis, [(i, (i + shift) % count) for i in range(count)])
        source = (rank + count - shift) % count
        filled = lax.dynamic_update_slice_in_dim(filled, piece, source * both.shape[0], axis=0)
    at, done = (0, [])
    for t, dim in zip(turned, dims):
        piece = filled[:, at : at + t[0].size].reshape(-1, *t.shape[1:])
        done.append(jnp.moveaxis(piece, 0, dim))
        at += t[0].size
    return tuple(done)


def sum_in_order(tiles, axes, order):
    inside = tiles.shape[1:]
    tiles = tiles.reshape(*(lax.axis_size(a) for a in axes), *inside)
    tiles = jnp.moveaxis(tiles, order, range(len(axes))).reshape(-1, *inside)
    for k in order:
        tiles = lax.psum_scatter(tiles, axes[k], scatter_dimension=0, tiled=True)
    return tiles[0]


def split_up(array, dim, length):
    before, after = (array.shape[:dim], array.shape[dim + 1 :])
    return jnp.moveaxis(array.reshape(*before, length, -1, *after), dim, 0)


def scatter_axes(array, axes, order, dim):
    length = lax.axis_size(axes)
    return sum_in_order(split_up(array, dim, length), axes, order)


def chebyshev(values, degree):
    series = [jnp.ones_like(values), values]
    for degree_at in range(2, degree):
        series.append(2.0 * values * series[-1] - series[-2])
    return series[:degree]


def focal_weight(pixel_uv, ccd_index, observed, obs_weight, live_rows, ccd_center):
    ccd_total = ccd_center.shape[1]
    picked = (
        ccd_index[None, :, :] == jnp.arange(ccd_total, dtype=jnp.int32)[:, None, None]
    ).astype(jnp.float32)
    centre = jnp.sum(ccd_center[:, :, None, None] * picked[None], axis=1)
    focal = 0.75 * centre + 0.25 * pixel_uv
    star_rows = ccd_index.shape[1]
    alive = (jnp.arange(star_rows, dtype=jnp.int32)[None, :] < live_rows).astype(jnp.float32)
    live_weight = obs_weight * observed.astype(jnp.float32) * alive
    return (focal, live_weight)


def basis_of(focal):
    along_first = chebyshev(focal[0], DEG_X)
    along_second = chebyshev(focal[1], DEG_Y)
    return jnp.stack(
        [first_term * second_term for first_term in along_first for second_term in along_second],
        axis=1,
    )


def jacobian_of(geometry):
    shift_time = geometry[0]
    factor_first = geometry[1]
    factor_second = geometry[2]
    unit_row = jnp.ones_like(shift_time)
    zero_row = jnp.zeros_like(shift_time)
    return jnp.stack(
        [
            jnp.stack([unit_row, zero_row, shift_time, zero_row, factor_first], axis=-1),
            jnp.stack([zero_row, unit_row, zero_row, shift_time, factor_second], axis=-1),
        ],
        axis=1,
    )


def geometry_of(exp_geom, exposure_ids):
    picked = (
        jnp.arange(exp_geom.shape[1], dtype=jnp.int32)[:, None] == exposure_ids[None, :]
    ).astype(jnp.float32)
    return (jnp.sum(exp_geom[:, :, None] * picked[None], axis=1), picked)


def coupling_matrix(live_weight, basis, jacobian):
    full = (
        live_weight[:, None, None, None, :]
        * jacobian[:, :, None, :, None]
        * basis[:, None, :, None, :]
    )
    return full.astype(jnp.bfloat16).reshape(basis.shape[0] * 2 * basis.shape[1], 5, basis.shape[2])


def negated_scaled(coupling, inverse):
    return (
        -jnp.einsum("xis,jis->xjs", coupling.astype(jnp.float32), inverse, precision=highest)
    ).astype(jnp.bfloat16)


def diagonal_blocks(live_weight, basis):
    weighted = live_weight[:, None, :] * basis
    gram = jnp.einsum("ams,ans->amn", weighted, basis, precision=highest)
    pair_eye = jnp.eye(2, dtype=jnp.float32)
    full = jnp.einsum("cd,amn->acmdn", pair_eye, gram, precision=highest)
    return (full.reshape(gram.shape[0], 2 * gram.shape[1], 2 * gram.shape[1]), weighted)


def gradient_terms(jacobian, live_weight, obs_resid):
    return jnp.einsum("aci,as,cas->is", jacobian, live_weight, obs_resid, precision=highest)


def local_rhs(weighted, jacobian, obs_resid, solved):
    correction = jnp.einsum("aci,is->cas", jacobian, solved, precision=highest)
    result = jnp.einsum("ams,cas->acm", weighted, obs_resid - correction, precision=highest)
    return result.reshape(weighted.shape[0], 2 * weighted.shape[1])


def star_product(former, latter):
    return lax.dot_general(former, latter, contract, preferred_element_type=jnp.float32)


LANES = 1024


def schur_kernel(xa, ya, wa, wda, wfa, wga, xo, yo, wo, wdo, wfo, wgo, si, out, peak, rhs0, rhs1, lhs0, lhs1):
    step = pl.program_id(0)
    bf = jnp.bfloat16
    f32 = jnp.float32
    n_all = xa.shape[0]
    n_own = xo.shape[0]
    terms = DEG_X * DEG_Y

    @pl.when(step == 0)
    def _():
        out[...] = jnp.zeros_like(out)

    tx = chebyshev(xa[...], DEG_X)
    ty = chebyshev(ya[...], DEG_Y)
    txo = chebyshev(xo[...], DEG_X)
    tyo = chebyshev(yo[...], DEG_Y)
    w, wd, wf, wg = wa[...], wda[...], wfa[...], wga[...]
    w_o, wd_o, wf_o, wg_o = wo[...], wdo[...], wfo[...], wgo[...]
    inv = [[si[pl.ds(j * 5 + i, 1), :] for i in range(5)] for j in range(5)]
    for p in range(DEG_X):
        for q in range(DEG_Y):
            m = p * DEG_Y + q
            b = tx[p] * ty[q]
            cp = (w * b).astype(bf).astype(f32)
            cq = (wd * b).astype(bf).astype(f32)
            cr = (wf * b).astype(bf).astype(f32)
            cs = (wg * b).astype(bf).astype(f32)
            for d, (k0, k1, last) in enumerate(((0, 2, cr), (1, 3, cs))):
                rows = pl.ds((d * terms + m) * n_all, n_all)
                sc = [(-(inv[j][k0] * cp + inv[j][k1] * cq + inv[j][4] * last)).astype(bf) for j in range(5)]
                for t, j in enumerate((0, 2, 4)):
                    rhs0[rows, pl.ds(t * LANES, LANES)] = sc[j]
                for t, j in enumerate((1, 3, 4)):
                    rhs1[rows, pl.ds(t * LANES, LANES)] = sc[j]
            bo = txo[p] * tyo[q]
            po = (w_o * bo).astype(bf).astype(f32)
            qo = (wd_o * bo).astype(bf).astype(f32)
            own_rows = pl.ds(m * n_own, n_own)
            lhs0[own_rows, pl.ds(0, LANES)] = po
            lhs0[own_rows, pl.ds(LANES, LANES)] = qo
            lhs0[own_rows, pl.ds(2 * LANES, LANES)] = (wf_o * bo).astype(bf).astype(f32)
            lhs1[own_rows, pl.ds(0, LANES)] = po
            lhs1[own_rows, pl.ds(LANES, LANES)] = qo
            lhs1[own_rows, pl.ds(2 * LANES, LANES)] = (wg_o * bo).astype(bf).astype(f32)
    out[0] += lax.dot_general(lhs0[...].astype(bf), rhs0[...], (((1,), (1,)), ((), ())), preferred_element_type=f32)
    out[1] += lax.dot_general(lhs1[...].astype(bf), rhs1[...], (((1,), (1,)), ((), ())), preferred_element_type=f32)

    @pl.when(step == pl.num_programs(0) - 1)
    def _():
        top = jnp.maximum(jnp.max(jnp.abs(out[0])), jnp.max(jnp.abs(out[1])))
        peak[...] = jnp.full(peak.shape, top, f32)


def schur_product(all_x, all_y, all_w, all_wd, all_wf, all_wg, own_x, own_y, own_w, own_wd, own_wf, own_wg, inverse):
    n_all, stars = all_x.shape
    n_own = own_x.shape[0]
    terms = DEG_X * DEG_Y
    rows_all = 2 * terms * n_all
    rows_own = terms * n_own
    all_spec = pl.BlockSpec((n_all, LANES), lambda k: (0, k))
    own_spec = pl.BlockSpec((n_own, LANES), lambda k: (0, k))
    inv_spec = pl.BlockSpec((25, LANES), lambda k: (0, k))
    return pl.pallas_call(
        schur_kernel,
        out_shape=(
            jax.ShapeDtypeStruct((2, rows_own, rows_all), jnp.float32),
            jax.ShapeDtypeStruct((8, LANES), jnp.float32),
        ),
        grid=(stars // LANES,),
        in_specs=[all_spec] * 6 + [own_spec] * 6 + [inv_spec],
        out_specs=(
            pl.BlockSpec((2, rows_own, rows_all), lambda k: (0, 0, 0)),
            pl.BlockSpec((8, LANES), lambda k: (0, 0)),
        ),
        scratch_shapes=[
            pltpu.VMEM((rows_all, 3 * LANES), jnp.bfloat16),
            pltpu.VMEM((rows_all, 3 * LANES), jnp.bfloat16),
            pltpu.VMEM((rows_own, 3 * LANES), jnp.float32),
            pltpu.VMEM((rows_own, 3 * LANES), jnp.float32),
        ],
        compiler_params=pltpu.CompilerParams(dimension_semantics=("arbitrary",)),
    )(all_x, all_y, all_w, all_wd, all_wf, all_wg, own_x, own_y, own_w, own_wd, own_wf, own_wg, inverse)


def on_device(
    pixel_uv,
    ccd_index,
    observed,
    obs_weight,
    obs_resid,
    star_inverse,
    star_count,
    ccd_center,
    exp_geom,
    tile_exposures,
    pair_owner,
):
    expo_total = lax.axis_size("expo")
    tile_total = lax.axis_size(TILE)
    expo_rank = lax.axis_index("expo")
    loc_dev = ccd_index.shape[0]
    window = tile_exposures.shape[1]
    params = 2 * DEG_X * DEG_Y
    live_rows = star_count[0]
    exposure_ids = lax.dynamic_slice_in_dim(tile_exposures[0], expo_rank * loc_dev, loc_dev)
    geometry, picked = geometry_of(exp_geom, exposure_ids)
    focal, live_weight = focal_weight(
        pixel_uv, ccd_index, observed, obs_weight, live_rows, ccd_center
    )
    basis = basis_of(focal)
    jacobian = jacobian_of(geometry)
    diagonal, weighted = diagonal_blocks(live_weight, basis)
    own_rows = expo_rank * loc_dev + jnp.arange(loc_dev, dtype=jnp.int32)
    local_rows = jnp.arange(loc_dev, dtype=jnp.int32)
    all_focal, all_weight, all_resid = turned_gather(
        (focal, live_weight, obs_resid), "expo", (1, 0, 1)
    )
    all_geometry, all_picked = geometry_of(exp_geom, tile_exposures[0])
    all_jacobian = jacobian_of(all_geometry)
    all_x, all_y = all_focal[0], all_focal[1]
    own_x, own_y = focal[0], focal[1]
    products, peak = schur_product(
        all_x, all_y, all_weight,
        all_weight * all_geometry[0][:, None], all_weight * all_geometry[1][:, None], all_weight * all_geometry[2][:, None],
        own_x, own_y, live_weight,
        live_weight * geometry[0][:, None], live_weight * geometry[1][:, None], live_weight * geometry[2][:, None],
        star_inverse.reshape(25, -1),
    )
    terms = DEG_X * DEG_Y
    bound = peak[0, 0] + jnp.max(jnp.abs(diagonal))
    bound = jnp.where(bound > 0.0, bound, 1.0)
    inverse_bound = 1.0 / bound
    product = (products * inverse_bound).astype(jnp.float16)
    product = product.reshape(2, terms, loc_dev, params, window)
    product = jnp.transpose(product, (2, 4, 0, 1, 3)).reshape(loc_dev, window, params * params)
    on_diagonal = own_rows[:, None] == jnp.arange(window, dtype=jnp.int32)[None, :]
    diagonal_flat = diagonal.reshape(loc_dev, 1, params * params) * inverse_bound
    diagonal_half = jnp.where(on_diagonal[:, :, None], diagonal_flat, 0.0).astype(jnp.float16)
    product = (product + diagonal_half).reshape(loc_dev * window, params * params)
    owners = lax.dynamic_slice_in_dim(pair_owner[0], expo_rank * loc_dev, loc_dev, 0)
    gradient = gradient_terms(all_jacobian, all_weight, all_resid)
    solved = jnp.einsum("jis,is->js", star_inverse, gradient, precision=highest)
    rhs_local = local_rhs(weighted, jacobian, obs_resid, solved)
    devices = tile_total * expo_total
    spread = jnp.dot(picked, rhs_local, precision=highest).reshape(devices, -1)
    pair_dev = 3 * (window // 2) * (window // 2) // expo_total
    flat_owner = owners.reshape(-1)
    target = flat_owner // pair_dev
    ranking = jnp.argsort(target, stable=True)
    per_peer = flat_owner.shape[0] // devices
    outgoing = jnp.take(product, ranking.reshape(devices, per_peer), axis=0, mode="clip")
    slot_tags = (flat_owner % pair_dev)[ranking].reshape(devices, per_peer).astype(jnp.float32)
    sent_scale = jnp.full((devices, 1), bound, jnp.float32)
    small = jnp.concatenate([spread, slot_tags, sent_scale], axis=1)
    incoming_blocks = lax.all_to_all(outgoing, TILE_EXPO, split_axis=0, concat_axis=0, tiled=True)
    incoming_small = lax.all_to_all(small, TILE_EXPO, split_axis=0, concat_axis=0, tiled=True)
    incoming_rhs = incoming_small[:, : spread.shape[1]]
    incoming_tags = incoming_small[:, spread.shape[1] : spread.shape[1] + per_peer].astype(jnp.int32)
    incoming_scale = jnp.broadcast_to(incoming_small[:, spread.shape[1] + per_peer :], (devices, per_peer))
    receive_slots = jnp.where(
        jnp.arange(pair_dev, dtype=jnp.int32)[:, None] == incoming_tags.reshape(1, -1),
        incoming_scale.reshape(1, -1),
        0.0,
    )
    incoming_blocks = incoming_blocks.astype(jnp.float32)
    receive_slots = receive_slots.reshape(pair_dev, devices, per_peer)
    pair_blocks = lax.dot_general(
        receive_slots, incoming_blocks, (((1, 2), (0, 1)), ((), ())), precision=lax.Precision.HIGH
    )
    reduced_rhs = jnp.sum(incoming_rhs.reshape(devices, -1, params), axis=0)
    return (pair_blocks, reduced_rhs)


def solution(mesh):
    split = Mesh(
        mesh.devices.reshape(4, 4, 2, mesh.shape["expo"]), ("tile_0", "tile_1", "tile_2", "expo")
    )
    placed = (
        P(None, "expo", TILE),
        P("expo", TILE),
        P("expo", TILE),
        P("expo", TILE),
        P(None, "expo", TILE),
        P(None, None, TILE),
        P(TILE),
        P(),
        P(),
        P(TILE, None),
        P(TILE, None, None),
    )
    return jax.shard_map(
        on_device,
        mesh=split,
        in_specs=placed,
        out_specs=(P(TILE_EXPO, None), P(TILE_EXPO, None)),
        check_vma=False,
    )
```

```python
import jax
import jax.numpy as jnp
from jax import lax
from jax.experimental import pallas as pl
from jax.experimental.pallas import tpu as pltpu
from jax.sharding import Mesh
from jax.sharding import PartitionSpec as P

DEG_X = 6
DEG_Y = 5
TILE = ("tile_0", "tile_1", "tile_2")
TILE_EXPO = ("tile_0", "tile_1", "tile_2", "expo")


highest = lax.Precision.HIGHEST
contract = (((1, 2), (1, 2)), ((), ()))


def turned_gather(arrays, axis, dims):
    turned = [jnp.moveaxis(a, dim, 0) for a, dim in zip(arrays, dims)]
    both = jnp.concatenate([t.reshape(len(t), -1) for t in turned], axis=1)
    count = lax.axis_size(axis)
    rank = lax.axis_index(axis)
    filled = jnp.zeros((count * both.shape[0], both.shape[1]), both.dtype)
    for shift in range(count):
        if shift == 0:
            piece = both
        else:
            piece = lax.ppermute(both, axis, [(i, (i + shift) % count) for i in range(count)])
        source = (rank + count - shift) % count
        filled = lax.dynamic_update_slice_in_dim(filled, piece, source * both.shape[0], axis=0)
    at, done = (0, [])
    for t, dim in zip(turned, dims):
        piece = filled[:, at : at + t[0].size].reshape(-1, *t.shape[1:])
        done.append(jnp.moveaxis(piece, 0, dim))
        at += t[0].size
    return tuple(done)


def sum_in_order(tiles, axes, order):
    inside = tiles.shape[1:]
    tiles = tiles.reshape(*(lax.axis_size(a) for a in axes), *inside)
    tiles = jnp.moveaxis(tiles, order, range(len(axes))).reshape(-1, *inside)
    for k in order:
        tiles = lax.psum_scatter(tiles, axes[k], scatter_dimension=0, tiled=True)
    return tiles[0]


def split_up(array, dim, length):
    before, after = (array.shape[:dim], array.shape[dim + 1 :])
    return jnp.moveaxis(array.reshape(*before, length, -1, *after), dim, 0)


def scatter_axes(array, axes, order, dim):
    length = lax.axis_size(axes)
    return sum_in_order(split_up(array, dim, length), axes, order)


def chebyshev(values, degree):
    series = [jnp.ones_like(values), values]
    for degree_at in range(2, degree):
        series.append(2.0 * values * series[-1] - series[-2])
    return series[:degree]


def focal_weight(pixel_uv, ccd_index, observed, obs_weight, live_rows, ccd_center):
    ccd_total = ccd_center.shape[1]
    picked = (
        ccd_index[None, :, :] == jnp.arange(ccd_total, dtype=jnp.int32)[:, None, None]
    ).astype(jnp.float32)
    centre = jnp.sum(ccd_center[:, :, None, None] * picked[None], axis=1)
    focal = 0.75 * centre + 0.25 * pixel_uv
    star_rows = ccd_index.shape[1]
    alive = (jnp.arange(star_rows, dtype=jnp.int32)[None, :] < live_rows).astype(jnp.float32)
    live_weight = obs_weight * observed.astype(jnp.float32) * alive
    return (focal, live_weight)


def basis_of(focal):
    along_first = chebyshev(focal[0], DEG_X)
    along_second = chebyshev(focal[1], DEG_Y)
    return jnp.stack(
        [first_term * second_term for first_term in along_first for second_term in along_second],
        axis=1,
    )


def jacobian_of(geometry):
    shift_time = geometry[0]
    factor_first = geometry[1]
    factor_second = geometry[2]
    unit_row = jnp.ones_like(shift_time)
    zero_row = jnp.zeros_like(shift_time)
    return jnp.stack(
        [
            jnp.stack([unit_row, zero_row, shift_time, zero_row, factor_first], axis=-1),
            jnp.stack([zero_row, unit_row, zero_row, shift_time, factor_second], axis=-1),
        ],
        axis=1,
    )


def geometry_of(exp_geom, exposure_ids):
    picked = (
        jnp.arange(exp_geom.shape[1], dtype=jnp.int32)[:, None] == exposure_ids[None, :]
    ).astype(jnp.float32)
    return (jnp.sum(exp_geom[:, :, None] * picked[None], axis=1), picked)


def coupling_matrix(live_weight, basis, jacobian):
    full = (
        live_weight[:, None, None, None, :]
        * jacobian[:, :, None, :, None]
        * basis[:, None, :, None, :]
    )
    return full.astype(jnp.bfloat16).reshape(basis.shape[0] * 2 * basis.shape[1], 5, basis.shape[2])


def negated_scaled(coupling, inverse):
    return (
        -jnp.einsum("xis,jis->xjs", coupling.astype(jnp.float32), inverse, precision=highest)
    ).astype(jnp.bfloat16)


def diagonal_blocks(live_weight, basis):
    weighted = live_weight[:, None, :] * basis
    gram = jnp.einsum("ams,ans->amn", weighted, basis, precision=highest)
    pair_eye = jnp.eye(2, dtype=jnp.float32)
    full = jnp.einsum("cd,amn->acmdn", pair_eye, gram, precision=highest)
    return (full.reshape(gram.shape[0], 2 * gram.shape[1], 2 * gram.shape[1]), weighted)


def gradient_terms(jacobian, live_weight, obs_resid):
    return jnp.einsum("aci,as,cas->is", jacobian, live_weight, obs_resid, precision=highest)


def local_rhs(weighted, jacobian, obs_resid, solved):
    correction = jnp.einsum("aci,is->cas", jacobian, solved, precision=highest)
    result = jnp.einsum("ams,cas->acm", weighted, obs_resid - correction, precision=highest)
    return result.reshape(weighted.shape[0], 2 * weighted.shape[1])


def star_product(former, latter):
    return lax.dot_general(former, latter, contract, preferred_element_type=jnp.float32)


LANES = 1024


def schur_kernel(xa, ya, wa, wda, wfa, wga, xo, yo, wo, wdo, wfo, wgo, si, out, peak, rhs0, rhs1, lhs0, lhs1):
    step = pl.program_id(0)
    bf = jnp.bfloat16
    f32 = jnp.float32
    n_all = xa.shape[0]
    n_own = xo.shape[0]
    terms = DEG_X * DEG_Y

    @pl.when(step == 0)
    def _():
        out[...] = jnp.zeros_like(out)

    tx = chebyshev(xa[...], DEG_X)
    ty = chebyshev(ya[...], DEG_Y)
    txo = chebyshev(xo[...], DEG_X)
    tyo = chebyshev(yo[...], DEG_Y)
    w, wd, wf, wg = wa[...], wda[...], wfa[...], wga[...]
    w_o, wd_o, wf_o, wg_o = wo[...], wdo[...], wfo[...], wgo[...]
    inv = [[si[pl.ds(j * 5 + i, 1), :] for i in range(5)] for j in range(5)]
    for p in range(DEG_X):
        for q in range(DEG_Y):
            m = p * DEG_Y + q
            b = tx[p] * ty[q]
            cp = (w * b).astype(bf).astype(f32)
            cq = (wd * b).astype(bf).astype(f32)
            cr = (wf * b).astype(bf).astype(f32)
            cs = (wg * b).astype(bf).astype(f32)
            for d, (k0, k1, last) in enumerate(((0, 2, cr), (1, 3, cs))):
                rows = pl.ds((d * terms + m) * n_all, n_all)
                sc = [(-(inv[j][k0] * cp + inv[j][k1] * cq + inv[j][4] * last)).astype(bf) for j in range(5)]
                for t, j in enumerate((0, 2, 4)):
                    rhs0[rows, pl.ds(t * LANES, LANES)] = sc[j]
                for t, j in enumerate((1, 3, 4)):
                    rhs1[rows, pl.ds(t * LANES, LANES)] = sc[j]
            bo = txo[p] * tyo[q]
            po = (w_o * bo).astype(bf).astype(f32)
            qo = (wd_o * bo).astype(bf).astype(f32)
            own_rows = pl.ds(m * n_own, n_own)
            lhs0[own_rows, pl.ds(0, LANES)] = po
            lhs0[own_rows, pl.ds(LANES, LANES)] = qo
            lhs0[own_rows, pl.ds(2 * LANES, LANES)] = (wf_o * bo).astype(bf).astype(f32)
            lhs1[own_rows, pl.ds(0, LANES)] = po
            lhs1[own_rows, pl.ds(LANES, LANES)] = qo
            lhs1[own_rows, pl.ds(2 * LANES, LANES)] = (wg_o * bo).astype(bf).astype(f32)
    out[0] += lax.dot_general(lhs0[...].astype(bf), rhs0[...], (((1,), (1,)), ((), ())), preferred_element_type=f32)
    out[1] += lax.dot_general(lhs1[...].astype(bf), rhs1[...], (((1,), (1,)), ((), ())), preferred_element_type=f32)

    @pl.when(step == pl.num_programs(0) - 1)
    def _():
        top = jnp.maximum(jnp.max(jnp.abs(out[0])), jnp.max(jnp.abs(out[1])))
        peak[...] = jnp.full(peak.shape, top, f32)


def schur_product(all_x, all_y, all_w, all_wd, all_wf, all_wg, own_x, own_y, own_w, own_wd, own_wf, own_wg, inverse):
    n_all, stars = all_x.shape
    n_own = own_x.shape[0]
    terms = DEG_X * DEG_Y
    rows_all = 2 * terms * n_all
    rows_own = terms * n_own
    all_spec = pl.BlockSpec((n_all, LANES), lambda k: (0, k))
    own_spec = pl.BlockSpec((n_own, LANES), lambda k: (0, k))
    inv_spec = pl.BlockSpec((25, LANES), lambda k: (0, k))
    return pl.pallas_call(
        schur_kernel,
        out_shape=(
            jax.ShapeDtypeStruct((2, rows_own, rows_all), jnp.float32),
            jax.ShapeDtypeStruct((8, LANES), jnp.float32),
        ),
        grid=(stars // LANES,),
        in_specs=[all_spec] * 6 + [own_spec] * 6 + [inv_spec],
        out_specs=(
            pl.BlockSpec((2, rows_own, rows_all), lambda k: (0, 0, 0)),
            pl.BlockSpec((8, LANES), lambda k: (0, 0)),
        ),
        scratch_shapes=[
            pltpu.VMEM((rows_all, 3 * LANES), jnp.bfloat16),
            pltpu.VMEM((rows_all, 3 * LANES), jnp.bfloat16),
            pltpu.VMEM((rows_own, 3 * LANES), jnp.float32),
            pltpu.VMEM((rows_own, 3 * LANES), jnp.float32),
        ],
        compiler_params=pltpu.CompilerParams(dimension_semantics=("arbitrary",)),
    )(all_x, all_y, all_w, all_wd, all_wf, all_wg, own_x, own_y, own_w, own_wd, own_wf, own_wg, inverse)


def on_device(
    pixel_uv,
    ccd_index,
    observed,
    obs_weight,
    obs_resid,
    star_inverse,
    star_count,
    ccd_center,
    exp_geom,
    tile_exposures,
    pair_owner,
):
    expo_total = lax.axis_size("expo")
    tile_total = lax.axis_size(TILE)
    expo_rank = lax.axis_index("expo")
    loc_dev = ccd_index.shape[0]
    window = tile_exposures.shape[1]
    params = 2 * DEG_X * DEG_Y
    live_rows = star_count[0]
    exposure_ids = lax.dynamic_slice_in_dim(tile_exposures[0], expo_rank * loc_dev, loc_dev)
    geometry, picked = geometry_of(exp_geom, exposure_ids)
    focal, live_weight = focal_weight(
        pixel_uv, ccd_index, observed, obs_weight, live_rows, ccd_center
    )
    basis = basis_of(focal)
    jacobian = jacobian_of(geometry)
    diagonal, weighted = diagonal_blocks(live_weight, basis)
    own_rows = expo_rank * loc_dev + jnp.arange(loc_dev, dtype=jnp.int32)
    local_rows = jnp.arange(loc_dev, dtype=jnp.int32)
    all_focal, all_weight, all_resid = turned_gather(
        (focal, live_weight, obs_resid), "expo", (1, 0, 1)
    )
    all_geometry, all_picked = geometry_of(exp_geom, tile_exposures[0])
    all_jacobian = jacobian_of(all_geometry)
    all_x, all_y = all_focal[0], all_focal[1]
    own_x, own_y = focal[0], focal[1]
    products, peak = schur_product(
        all_x, all_y, all_weight,
        all_weight * all_geometry[0][:, None], all_weight * all_geometry[1][:, None], all_weight * all_geometry[2][:, None],
        own_x, own_y, live_weight,
        live_weight * geometry[0][:, None], live_weight * geometry[1][:, None], live_weight * geometry[2][:, None],
        star_inverse.reshape(25, -1),
    )
    terms = DEG_X * DEG_Y
    bound = peak[0, 0] + jnp.max(jnp.abs(diagonal))
    bound = jnp.where(bound > 0.0, bound, 1.0)
    inverse_bound = 1.0 / bound
    product = (products * inverse_bound).astype(jnp.float16)
    product = product.reshape(2, terms, loc_dev, params, window)
    product = jnp.transpose(product, (2, 4, 0, 1, 3)).reshape(loc_dev, window, params * params)
    on_diagonal = own_rows[:, None] == jnp.arange(window, dtype=jnp.int32)[None, :]
    diagonal_flat = diagonal.reshape(loc_dev, 1, params * params) * inverse_bound
    diagonal_half = jnp.where(on_diagonal[:, :, None], diagonal_flat, 0.0).astype(jnp.float16)
    product = (product + diagonal_half).reshape(loc_dev * window, params * params)
    owners = lax.dynamic_slice_in_dim(pair_owner[0], expo_rank * loc_dev, loc_dev, 0)
    gradient = gradient_terms(all_jacobian, all_weight, all_resid)
    solved = jnp.einsum("jis,is->js", star_inverse, gradient, precision=highest)
    rhs_local = local_rhs(weighted, jacobian, obs_resid, solved)
    devices = tile_total * expo_total
    spread = jnp.dot(picked, rhs_local, precision=highest).reshape(devices, -1)
    pair_dev = 3 * (window // 2) * (window // 2) // expo_total
    flat_owner = owners.reshape(-1)
    target = flat_owner // pair_dev
    order = jnp.arange(target.shape[0], dtype=jnp.int32)
    earlier = (target[None, :] == target[:, None]) & (order[None, :] < order[:, None])
    place = target * (target.shape[0] // devices) + jnp.sum(earlier.astype(jnp.int32), axis=1)
    ranking = jnp.sum(jnp.where(place[None, :] == order[:, None], order[None, :], 0), axis=1)
    per_peer = flat_owner.shape[0] // devices
    outgoing = jnp.take(product, ranking.reshape(devices, per_peer), axis=0, mode="clip")
    slot_tags = (flat_owner % pair_dev)[ranking].reshape(devices, per_peer).astype(jnp.float32)
    sent_scale = jnp.full((devices, 1), bound, jnp.float32)
    small = jnp.concatenate([spread, slot_tags, sent_scale], axis=1)
    incoming_blocks = lax.all_to_all(outgoing, TILE_EXPO, split_axis=0, concat_axis=0, tiled=True)
    incoming_small = lax.all_to_all(small, TILE_EXPO, split_axis=0, concat_axis=0, tiled=True)
    incoming_rhs = incoming_small[:, : spread.shape[1]]
    incoming_tags = incoming_small[:, spread.shape[1] : spread.shape[1] + per_peer].astype(jnp.int32)
    incoming_scale = jnp.broadcast_to(incoming_small[:, spread.shape[1] + per_peer :], (devices, per_peer))
    receive_slots = jnp.where(
        jnp.arange(pair_dev, dtype=jnp.int32)[:, None] == incoming_tags.reshape(1, -1),
        incoming_scale.reshape(1, -1),
        0.0,
    )
    incoming_blocks = incoming_blocks.astype(jnp.float32)
    receive_slots = receive_slots.reshape(pair_dev, devices, per_peer)
    pair_blocks = lax.dot_general(
        receive_slots, incoming_blocks, (((1, 2), (0, 1)), ((), ())), precision=lax.Precision.HIGH
    )
    reduced_rhs = jnp.sum(incoming_rhs.reshape(devices, -1, params), axis=0)
    return (pair_blocks, reduced_rhs)


def solution(mesh):
    split = Mesh(
        mesh.devices.reshape(4, 4, 2, mesh.shape["expo"]), ("tile_0", "tile_1", "tile_2", "expo")
    )
    placed = (
        P(None, "expo", TILE),
        P("expo", TILE),
        P("expo", TILE),
        P("expo", TILE),
        P(None, "expo", TILE),
        P(None, None, TILE),
        P(TILE),
        P(),
        P(),
        P(TILE, None),
        P(TILE, None, None),
    )
    return jax.shard_map(
        on_device,
        mesh=split,
        in_specs=placed,
        out_specs=(P(TILE_EXPO, None), P(TILE_EXPO, None)),
        check_vma=False,
    )
```
